32 devices in a mesh: dp: 4 (over y, x), ctx: 8 (over z, core).
Axes of the slice: x: 2, y: 2, z: 4, core: 2. Of those that a mesh axis runs over, the one named last changes fastest.
Arguments:
- queries: bfloat16 [4, 1024, 4096], P('dp', 'ctx'), may hold values from -6 to 6
- keys: bfloat16 [4, 8192, 128], P('dp', 'ctx'), may hold values from -6 to 6
- head_weights: bfloat16 [4, 1024, 32], P('dp', 'ctx'), may hold values from -6 to 6
- block_ids: int32 [4, 16, 32], P('dp', 'ctx'), may hold values from -1 to 127, as said below
- target_mass: bfloat16 [4, 1024, 2048], P('dp', 'ctx'), may hold values from 0.0099487305 to 10
- key_gain: float32 [128], replicated, may hold values from 0.5 to 1.5
- key_bias: float32 [128], replicated, may hold values from -1.8 to 1.8
Outputs:
- seq_loss: float32 [4], P('dp')
- grad_queries: float32 [4, 1024, 4096], P('dp', 'ctx')
- grad_head_weights: float32 [4, 1024, 32], P('dp', 'ctx')
- grad_keys: float32 [4, 8192, 128], P('dp', 'ctx')
- grad_gain: float32 [128], replicated
- grad_bias: float32 [128], replicated
The draws below stay inside these ranges and needn't reach their ends.
Inputs may be any that keep to these rules, and one draw needn't show every extreme that they name: `block_ids`: query block b of a sequence lies in the last 2 key blocks of the positions of index b // 2 of ctx. Its slots list distinct block ids, none after its own block; the first two are its own block and the block before it; filled slots come first and -1 marks the empty rest. The 2 query blocks of one index of ctx list at most 4 blocks that lie in the positions of any one index of ctx, and exactly 3 of their own index.
All inputs are finite; a program needn't handle non-finite values.
Results may differ from the reference program's by a relative error of at most 0.00115.
The reference program's roundings to bfloat16 on the way (of `normed_keys`, `normed_queries` and `score_grad`) count: a program that leaves them out, or rounds other values in their place, can miss the bound.
Values may be sent and summed in bfloat16 or wider, within the bound.
No kernel may reach another device: no remote copies, remote signals or barrier semaphores. Data moves between devices by JAX's collectives and lax.ppermute only.
A program may use at most 64 MiB of HBM per device.

```python
import math
import jax
import jax.numpy as jnp
from jax import lax

H = 32
DH = 128
BS = 64
NSEL = 32
QD = 128
KD = 1024
SEQS = 4
QB_DEV = 2
KB_DEV = 16
NQ = 1024
SEQLEN = 8192
NQB = 16
NB = 128
SLOTS = 2048
N_CTX = 8


def draw_block_ids(key, part):

    def one_sequence(seq_key):
        hot_key, prio_key, first_key, second_key = jax.random.split(seq_key, 4)
        hot_owner = (jax.random.randint(hot_key, (N_CTX,), 0, 4) == 0).astype(jnp.int32)
        number = jnp.arange(NQB, dtype=jnp.int32)
        device = number // QB_DEV
        own_block = device * KB_DEV + KB_DEV - QB_DEV + number % QB_DEV
        owners = jnp.arange(N_CTX, dtype=jnp.int32)
        priority = jax.random.randint(prio_key, (NQB, N_CTX), 0, 1 << 20) + hot_owner[None, :] * (1 << 20)
        priority = priority * N_CTX + owners[None, :]
        priority = jnp.where(owners[None, :] < device[:, None], priority, -1 - owners[None, :])
        others = min(NSEL // 2 - 1, N_CTX - 1)
        ignored, chosen = lax.top_k(priority, others)
        live = jnp.arange(others, dtype=jnp.int32)[None, :] < device[:, None]
        first = jax.random.randint(first_key, (NQB, others), 0, KB_DEV)
        second = (first + jax.random.randint(second_key, (NQB, others), 1, KB_DEV)) % KB_DEV
        paired = jnp.stack([chosen * KB_DEV + first, chosen * KB_DEV + second], -1)
        paired = jnp.where(live[:, :, None], paired, -1).reshape(NQB, 2 * others)
        own_pair = jnp.stack([own_block, own_block - 1], -1)
        empty = jnp.full((NQB, NSEL - 2 - 2 * others), -1, jnp.int32)
        return jnp.concatenate([own_pair, paired.astype(jnp.int32), empty], 1).astype(jnp.int32)
    return jax.vmap(one_sequence)(jax.random.split(key, SEQS))


def level_of(stream_key, dims, pieces, least, largest):
    gain, own = 1.0, jax.random.fold_in(stream_key, 6)
    for position, blocks in pieces:
        steps = jnp.exp(jax.random.uniform(jax.random.fold_in(own, position), (blocks,), jnp.float32, least / len(pieces), largest / len(pieces)))
        gain = gain * jnp.repeat(steps, dims[position] // blocks).reshape([-1 if axis == position else 1 for axis in range(len(dims))])
    return gain


def centred(own_key, shape, scale, limit, shards=(), held_as=jnp.bfloat16):
    factor_of = level_of(own_key, shape, shards, -0.22, 0.18) if shards else 1.0
    values = jax.random.normal(own_key, shape, jnp.float32) * scale * factor_of
    return jnp.minimum(jnp.maximum(values, -limit), limit).astype(held_as)


def setup_inputs(seed: int = 0) -> dict:
    arg_keys = jax.random.split(jax.random.key(seed), 8)
    return {
        "queries": centred(arg_keys[0], (SEQS, NQ, H * DH), 1.0, 6.0, ((0, 4), (1, 8))),
        "keys": centred(arg_keys[1], (SEQS, SEQLEN, DH), 1.0, 6.0, ((0, 4), (1, 8))),
        "head_weights": centred(arg_keys[2], (SEQS, NQ, H), 1.0, 6.0, ((0, 4), (1, 8))),
        "block_ids": draw_block_ids(jax.random.fold_in(arg_keys[7], 71), 0),
        "target_mass": jnp.clip(jnp.exp(math.log(10.0) - 6.912895 * jax.random.uniform(arg_keys[4], (SEQS, NQ, SLOTS), jnp.float32) ** level_of(arg_keys[4], (SEQS, NQ, SLOTS), ((0, 4), (1, 8)), -0.2, 0.2)), 0.0099487305, 10.0).astype(jnp.bfloat16),
        "key_gain": jnp.clip(1.0 + 0.1 * jax.random.normal(arg_keys[5], (DH,), jnp.float32), 0.5, 1.5),
        "key_bias": centred(arg_keys[6], (DH,), 0.3, 1.8, (), jnp.float32),
    }


epsilon = 1e-06
soft_cap = 20.0

def key_norm(key_rows, key_gain, key_bias):
    key_float = key_rows.astype(jnp.float32)
    key_mean = lax.optimization_barrier(jnp.mean(key_float, -1, keepdims=True))
    centered = key_float - key_mean
    key_var = lax.optimization_barrier(jnp.mean(centered * centered, -1, keepdims=True))
    key_scale = lax.rsqrt(key_var + epsilon)
    key_hat = centered * key_scale
    normed_keys = (key_hat * key_gain + key_bias).astype(jnp.bfloat16)
    return (key_hat, key_scale, normed_keys)

def query_norm(query_rows):
    query_float = query_rows.astype(jnp.float32).reshape(query_rows.shape[0], H, DH)
    query_scale = lax.rsqrt(lax.optimization_barrier(jnp.mean(query_float * query_float, -1, keepdims=True)) + epsilon)
    query_hat = query_float * query_scale
    return (query_hat, query_scale, query_hat.astype(jnp.bfloat16))

def score_block(normed_queries, weight_rows, mass_rows, query_pos, slot_keys, slot_pos, slot_live):
    inv_root = DH ** (-0.5)
    scores = jnp.einsum('thd,jd->thj', normed_queries.astype(jnp.float32), slot_keys.astype(jnp.float32)) * inv_root
    activated = jax.nn.softplus(scores)
    mixture = lax.optimization_barrier(jnp.sum(weight_rows[:, :, None] * activated, 1))
    squashed = jnp.tanh(mixture / soft_cap)
    logits = soft_cap * squashed
    is_valid = slot_live[None, :] & (slot_pos[None, :] <= query_pos[:, None])
    exp_terms = jnp.where(is_valid, jnp.exp(logits - soft_cap), 0.0)
    denominator = lax.optimization_barrier(jnp.sum(exp_terms, 1, keepdims=True))
    log_prob = logits - soft_cap - jnp.log(denominator)
    kept_mass = jnp.where(is_valid, mass_rows, 0.0)
    target = kept_mass / lax.optimization_barrier(jnp.sum(kept_mass, 1, keepdims=True))
    divergence = jnp.sum(jnp.where(is_valid, target * (jnp.log(jnp.where(is_valid, target, 1.0)) - log_prob), 0.0))
    mix_grad = (exp_terms / denominator - target) * (1.0 - squashed * squashed)
    score_grad = (mix_grad[:, None, :] * weight_rows[:, :, None] * jax.nn.sigmoid(scores)).astype(jnp.bfloat16)
    weight_grad = lax.optimization_barrier(jnp.sum(mix_grad[:, None, :] * activated, 2))
    query_grad = jnp.einsum('thj,jd->thd', score_grad.astype(jnp.float32), slot_keys.astype(jnp.float32)) * inv_root
    slot_grad = jnp.einsum('thj,thd->jd', score_grad.astype(jnp.float32), normed_queries.astype(jnp.float32)) * inv_root
    return (divergence, query_grad, weight_grad, slot_grad)

def reference(queries, keys, head_weights, block_ids, target_mass, key_gain, key_bias):

    def one_sequence(per_seq):
        query_rows, key_rows, weight_rows, block_list, mass_rows = per_seq
        key_hat, key_scale, normed_keys = key_norm(key_rows, key_gain, key_bias)
        query_hat, query_scale, normed_queries = query_norm(query_rows)
        key_blocks = normed_keys.reshape(NB, BS, DH)
        offsets = jnp.arange(BS, dtype=jnp.int32)

        def block_step(grad_blocks, scanned):
            block_number, query_block, weight_block, mass_block, listed_ids = scanned
            is_listed = listed_ids >= 0
            block_safe = jnp.maximum(listed_ids, 0).astype(jnp.int32)
            slot_keys = key_blocks[block_safe].reshape(SLOTS, DH)
            slot_pos = (block_safe[:, None] * BS + offsets[None, :]).reshape(SLOTS)
            slot_live = jnp.repeat(is_listed, BS)
            query_pos = block_number // QB_DEV * KD + KD - QD + block_number % QB_DEV * BS + offsets
            divergence, query_grad, weight_grad, slot_grad = score_block(query_block, weight_block, mass_block, query_pos, slot_keys, slot_pos, slot_live)
            live_factor = is_listed.astype(jnp.float32)[:, None, None]
            grad_blocks = grad_blocks.at[block_safe].add(slot_grad.reshape(NSEL, BS, DH) * live_factor)
            return (grad_blocks, (divergence, query_grad, weight_grad))
        initial = jnp.zeros((NB, BS, DH), jnp.float32)
        scanned = (jnp.arange(NQB, dtype=jnp.int32), normed_queries.reshape(NQB, BS, H, DH), weight_rows.astype(jnp.float32).reshape(NQB, BS, H), mass_rows.astype(jnp.float32).reshape(NQB, BS, SLOTS), block_list)
        grad_blocks, (divergences, query_grads, weight_grads) = lax.scan(block_step, initial, scanned)
        query_grads = query_grads.reshape(NQ, H, DH)
        grad_query_rows = (query_grads - query_hat * lax.optimization_barrier(jnp.mean(query_grads * query_hat, -1, keepdims=True))) * query_scale
        key_grad = grad_blocks.reshape(SEQLEN, DH)
        gain_part = lax.optimization_barrier(jnp.sum(key_grad * key_hat, 0))
        bias_part = lax.optimization_barrier(jnp.sum(key_grad, 0))
        scaled_grad = key_grad * key_gain
        grad_key_rows = (scaled_grad - lax.optimization_barrier(jnp.mean(scaled_grad, -1, keepdims=True)) - key_hat * lax.optimization_barrier(jnp.mean(scaled_grad * key_hat, -1, keepdims=True))) * key_scale
        return (jnp.sum(divergences) / NQ, grad_query_rows.reshape(NQ, H * DH), weight_grads.reshape(NQ, H), grad_key_rows, gain_part, bias_part)
    seq_loss, grad_queries, grad_head_weights, grad_keys, gain_parts, bias_parts = lax.map(one_sequence, (queries, keys, head_weights, block_ids, target_mass))
    return (seq_loss, grad_queries, grad_head_weights, grad_keys, lax.optimization_barrier(jnp.sum(gain_parts, 0)), lax.optimization_barrier(jnp.sum(bias_parts, 0)))
```

```python
import functools
import jax
import jax.numpy as jnp
from jax import lax
from jax.experimental import pallas as pl
from jax.experimental.pallas import tpu as pltpu
from jax.sharding import PartitionSpec as P

H = 32
DH = 128
BS = 64
NSEL = 32
QD = 128
KD = 1024

epsilon = 1e-06
soft_cap = 20.0

HEAD_GROUP = 4
CHUNK = 512


def key_norm(key_rows, key_gain, key_bias):
    key_float = key_rows.astype(jnp.float32)
    key_mean = jnp.mean(key_float, -1, keepdims=True)
    centered = key_float - key_mean
    key_var = jnp.mean(centered * centered, -1, keepdims=True)
    key_scale = lax.rsqrt(key_var + epsilon)
    key_hat = centered * key_scale
    normed_keys = (key_hat * key_gain + key_bias).astype(jnp.bfloat16)
    return (key_hat, key_scale, normed_keys)


def query_norm(query_rows):
    query_float = query_rows.astype(jnp.float32).reshape(query_rows.shape[0], H, DH)
    query_scale = lax.rsqrt(jnp.mean(query_float * query_float, -1, keepdims=True) + epsilon)
    query_hat = query_float * query_scale
    return (query_hat, query_scale, query_hat.astype(jnp.bfloat16))


def score_kernel(qr_ref, qt_ref, k_ref, kt_ref, w_ref, mass_ref, spos_ref, qpos_ref,
                 qg_ref, wg_ref, sgt_ref, div_ref, mix_ref, mg_ref):
    f32 = jnp.float32
    inv_root = DH ** (-0.5)
    rows = HEAD_GROUP * BS
    groups = H // HEAD_GROUP
    slots = kt_ref.shape[1]
    chunks = slots // CHUNK

    mix_ref[...] = jnp.zeros_like(mix_ref)

    def first_pass(g, carry):
        r0 = pl.multiple_of(g * rows, rows)
        q = qr_ref[pl.ds(r0, rows), :]
        wcol = w_ref[pl.ds(r0, rows), :]
        for c in range(chunks):
            cs = slice(c * CHUNK, (c + 1) * CHUNK)
            s = jnp.dot(q, kt_ref[:, cs], preferred_element_type=f32) * inv_root
            sp = jnp.maximum(s, 0.0) + jnp.log1p(jnp.exp(-jnp.abs(s)))
            ws = (wcol * sp).reshape(HEAD_GROUP, BS, CHUNK)
            mix_ref[:, cs] += jnp.sum(ws, 0)
        return carry

    lax.fori_loop(0, groups, first_pass, 0)

    mixture = mix_ref[...]
    squashed = jnp.tanh(mixture / soft_cap)
    logits = soft_cap * squashed
    is_valid = spos_ref[...] <= qpos_ref[...]
    exp_terms = jnp.where(is_valid, jnp.exp(logits - soft_cap), 0.0)
    denominator = jnp.sum(exp_terms, 1, keepdims=True)
    log_prob = logits - soft_cap - jnp.log(denominator)
    kept_mass = jnp.where(is_valid, mass_ref[...].astype(f32), 0.0)
    target = kept_mass / jnp.sum(kept_mass, 1, keepdims=True)
    div_ref[...] = jnp.sum(
        jnp.where(is_valid, target * (jnp.log(jnp.where(is_valid, target, 1.0)) - log_prob), 0.0),
        1, keepdims=True)
    mg_ref[...] = (exp_terms / denominator - target) * (1.0 - squashed * squashed)

    sgt_ref[...] = jnp.zeros_like(sgt_ref)

    def second_pass(g, carry):
        r0 = pl.multiple_of(g * rows, rows)
        q = qr_ref[pl.ds(r0, rows), :]
        qt = qt_ref[:, pl.ds(r0, rows)]
        wcol = w_ref[pl.ds(r0, rows), :]
        qg_acc = jnp.zeros((rows, DH), f32)
        wg_acc = jnp.zeros((rows, 1), f32)
        for c in range(chunks):
            cs = slice(c * CHUNK, (c + 1) * CHUNK)
            s = jnp.dot(q, kt_ref[:, cs], preferred_element_type=f32) * inv_root
            e = jnp.exp(-jnp.abs(s))
            sp = jnp.maximum(s, 0.0) + jnp.log1p(e)
            r = 1.0 / (1.0 + e)
            sig = jnp.where(s >= 0.0, r, e * r)
            mgc = mg_ref[:, cs]
            mg4 = jnp.broadcast_to(mgc[None], (HEAD_GROUP, BS, CHUNK)).reshape(rows, CHUNK)
            sg = (mg4 * wcol * sig).astype(jnp.bfloat16)
            wg_acc = wg_acc + jnp.sum(mg4 * sp, 1, keepdims=True)
            qg_acc = qg_acc + jnp.dot(sg, k_ref[cs, :], preferred_element_type=f32)
            sgt_ref[:, cs] += jnp.dot(qt, sg, preferred_element_type=f32)
        qg_ref[pl.ds(r0, rows), :] = qg_acc * inv_root
        wg_ref[pl.ds(r0, rows), :] = wg_acc
        return carry

    lax.fori_loop(0, groups, second_pass, 0)
    sgt_ref[...] = sgt_ref[...] * inv_root


def score_blocks(qr, qt, k, kt, wcol, mass, spos, qpos):
    nblk, nrows, _ = qr.shape
    slots = k.shape[1]
    f32 = jnp.float32

    def blk(*shape):
        return pl.BlockSpec((None,) + shape, lambda b: (b,) + (0,) * len(shape))

    flops = nblk * (4 * 2 * nrows * slots * DH)
    return pl.pallas_call(
        score_kernel,
        grid=(nblk,),
        in_specs=[
            blk(nrows, DH), blk(DH, nrows), blk(slots, DH), blk(DH, slots),
            blk(nrows, 1), blk(BS, slots), blk(1, slots), blk(BS, 1),
        ],
        out_specs=[blk(nrows, DH), blk(nrows, 1), blk(DH, slots), blk(BS, 1)],
        out_shape=[
            jax.ShapeDtypeStruct((nblk, nrows, DH), f32),
            jax.ShapeDtypeStruct((nblk, nrows, 1), f32),
            jax.ShapeDtypeStruct((nblk, DH, slots), f32),
            jax.ShapeDtypeStruct((nblk, BS, 1), f32),
        ],
        scratch_shapes=[pltpu.VMEM((BS, slots), f32), pltpu.VMEM((BS, slots), f32)],
        compiler_params=pltpu.CompilerParams(dimension_semantics=("arbitrary",)),
        cost_estimate=pl.CostEstimate(
            flops=flops, transcendentals=nblk * nrows * slots * 5,
            bytes_accessed=nblk * (nrows * DH * 4 + slots * DH * 4 + nrows * DH * 4 + DH * slots * 4)),
    )(qr, qt, k, kt, wcol, mass, spos, qpos)


def per_device(queries, keys, head_weights, block_ids, target_mass, key_gain, key_bias):
    ctx_count = lax.axis_size("ctx")
    ctx_index = lax.axis_index("ctx")
    dp_count = lax.axis_size("dp")
    dp_index = lax.axis_index("dp")
    key_count = KD // BS
    query_count = QD // BS
    capacity = 2 * query_count
    request_count = query_count * NSEL
    slot_count = NSEL * BS
    key_hat, key_scale, normed_keys = key_norm(keys[0], key_gain, key_bias)
    listed_ids = block_ids[0].reshape(request_count)
    is_listed = listed_ids >= 0
    block_safe = jnp.maximum(listed_ids, 0)
    owner_index = block_safe // key_count
    local_block = block_safe % key_count
    owner_hits = (
        (owner_index[:, None] == jnp.arange(ctx_count, dtype=jnp.int32)[None, :])
        & is_listed[:, None]
    ).astype(jnp.int32)
    earlier = jnp.cumsum(owner_hits, 0) - owner_hits
    rank_slot = jnp.sum(earlier * owner_hits, 1)
    target_slot = jnp.where(is_listed, owner_index * capacity + rank_slot, 0)
    placement = (
        target_slot[:, None] == jnp.arange(ctx_count * capacity, dtype=jnp.int32)[None, :]
    ) & is_listed[:, None]
    request_table = jnp.sum(jnp.where(placement, local_block[:, None] + 1, 0), 0) - 1
    request_table = request_table.reshape(ctx_count, capacity)
    initial_slots = jnp.zeros((request_count, BS, DH), jnp.bfloat16)
    shard_rows = lax.all_gather(normed_keys, "ctx", axis=0, tiled=True)
    block_rows = shard_rows.shape[0] // BS
    relative = block_safe * BS
    inside = is_listed & (relative >= 0) & (relative < shard_rows.shape[0])
    picked = shard_rows.reshape(block_rows, BS, DH)[jnp.clip(relative // BS, 0, block_rows - 1)]
    slot_keys = jnp.where(inside[:, None, None], picked, initial_slots)
    slot_keys = slot_keys.reshape(query_count, slot_count, DH)
    slot_positions = (block_safe[:, None] * BS + jnp.arange(BS, dtype=jnp.int32)[None, :]).reshape(
        query_count, slot_count
    )
    slot_lives = jnp.repeat(is_listed, BS).reshape(query_count, slot_count)
    never = jnp.iinfo(jnp.int32).max
    slot_limit = jnp.where(slot_lives, slot_positions, never).reshape(query_count, 1, slot_count)
    query_hat, query_scale, normed_queries = query_norm(queries[0])
    first_pos = ctx_index * KD + KD - QD
    query_pos = (first_pos + jnp.arange(QD, dtype=jnp.int32)).reshape(query_count, BS, 1)

    head_rows = (
        normed_queries.reshape(query_count, BS, H, DH).transpose(0, 2, 1, 3).reshape(query_count, H * BS, DH)
    )
    head_cols = head_rows.transpose(0, 2, 1)
    key_cols = slot_keys.transpose(0, 2, 1)
    weight_col = (
        head_weights[0].astype(jnp.float32).reshape(query_count, BS, H).transpose(0, 2, 1)
        .reshape(query_count, H * BS, 1)
    )
    mass_rows = target_mass[0].reshape(query_count, BS, slot_count)
    qg_rows, wg_rows, slot_grad_t, div_rows = score_blocks(
        head_rows, head_cols, slot_keys, key_cols, weight_col, mass_rows, slot_limit, query_pos
    )
    divergence_total = jnp.sum(div_rows)
    query_grads = qg_rows.reshape(query_count, H, BS, DH).transpose(0, 2, 1, 3).reshape(QD, H, DH)
    weight_grads = wg_rows.reshape(query_count, H, BS).transpose(0, 2, 1).reshape(QD, H)
    grad_slots = slot_grad_t.transpose(0, 2, 1)

    grad_query_rows = (
        query_grads - query_hat * jnp.mean(query_grads * query_hat, -1, keepdims=True)
    ) * query_scale
    slot_flat = grad_slots.reshape(request_count, BS * DH)
    outbound = jnp.dot(placement.T.astype(jnp.float32), slot_flat, precision=lax.Precision.HIGHEST)
    returned, asked_back = (
        lax.all_to_all(
            outbound.reshape(ctx_count, capacity, BS * DH),
            "ctx",
            split_axis=0,
            concat_axis=0,
            tiled=True,
        ),
        lax.all_to_all(request_table, "ctx", split_axis=0, concat_axis=0, tiled=True),
    )
    own_rows = (
        asked_back.reshape(ctx_count * capacity)[None, :]
        == jnp.arange(key_count, dtype=jnp.int32)[:, None]
    ).astype(jnp.float32)
    key_grad = jnp.dot(
        own_rows, returned.reshape(ctx_count * capacity, BS * DH), precision=lax.Precision.HIGHEST
    ).reshape(KD, DH)
    gain_part = jnp.sum(key_grad * key_hat, 0)
    bias_part = jnp.sum(key_grad, 0)
    scaled_grad = key_grad * key_gain
    grad_key_rows = (
        scaled_grad
        - jnp.mean(scaled_grad, -1, keepdims=True)
        - key_hat * jnp.mean(scaled_grad * key_hat, -1, keepdims=True)
    ) * key_scale
    loss_slots = jnp.where(jnp.arange(dp_count) == dp_index, divergence_total, 0.0)
    packed = lax.psum(jnp.concatenate([gain_part, bias_part, loss_slots]), ("dp", "ctx"))
    grad_gain = packed[:DH]
    grad_bias = packed[DH:2 * DH]
    loss_total = lax.dynamic_index_in_dim(packed, 2 * DH + dp_index, 0, keepdims=False)
    seq_loss = jnp.reshape(loss_total / (QD * ctx_count), (1,))
    return (
        seq_loss,
        grad_query_rows.reshape(1, QD, H * DH),
        weight_grads.reshape(1, QD, H),
        grad_key_rows.reshape(1, KD, DH),
        grad_gain,
        grad_bias,
    )


def solution(mesh):
    in_specs = (
        P("dp", "ctx", None),
        P("dp", "ctx", None),
        P("dp", "ctx", None),
        P("dp", "ctx", None),
        P("dp", "ctx", None),
        P(),
        P(),
    )
    out_specs = (
        P("dp"),
        P("dp", "ctx", None),
        P("dp", "ctx", None),
        P("dp", "ctx", None),
        P(),
        P(),
    )
    return jax.shard_map(
        per_device, mesh=mesh, in_specs=in_specs, out_specs=out_specs, check_vma=False
    )
```

```python
import functools
import jax
import jax.numpy as jnp
from jax import lax
from jax.experimental import pallas as pl
from jax.experimental.pallas import tpu as pltpu
from jax.sharding import PartitionSpec as P

H = 32
DH = 128
BS = 64
NSEL = 32
QD = 128
KD = 1024

epsilon = 1e-06
soft_cap = 20.0

HEAD_GROUP = 4
CHUNK = 512


def key_norm(key_rows, key_gain, key_bias):
    key_float = key_rows.astype(jnp.float32)
    key_mean = jnp.mean(key_float, -1, keepdims=True)
    centered = key_float - key_mean
    key_var = jnp.mean(centered * centered, -1, keepdims=True)
    key_scale = lax.rsqrt(key_var + epsilon)
    key_hat = centered * key_scale
    normed_keys = (key_hat * key_gain + key_bias).astype(jnp.bfloat16)
    return (key_hat, key_scale, normed_keys)


def query_norm(query_rows):
    query_float = query_rows.astype(jnp.float32).reshape(query_rows.shape[0], H, DH)
    query_scale = lax.rsqrt(jnp.mean(query_float * query_float, -1, keepdims=True) + epsilon)
    query_hat = query_float * query_scale
    return (query_hat, query_scale, query_hat.astype(jnp.bfloat16))


def score_kernel(qr_ref, qt_ref, k_ref, kt_ref, w_ref, mass_ref, spos_ref, qpos_ref,
                 qg_ref, wg_ref, sgt_ref, div_ref, mix_ref, mg_ref):
    f32 = jnp.float32
    inv_root = DH ** (-0.5)
    rows = HEAD_GROUP * BS
    groups = H // HEAD_GROUP
    slots = kt_ref.shape[1]
    chunks = slots // CHUNK

    mix_ref[...] = jnp.zeros_like(mix_ref)

    def first_pass(g, carry):
        r0 = pl.multiple_of(g * rows, rows)
        q = qr_ref[pl.ds(r0, rows), :]
        wcol = w_ref[pl.ds(r0, rows), :]
        for c in range(chunks):
            cs = slice(c * CHUNK, (c + 1) * CHUNK)
            s = jnp.dot(q, kt_ref[:, cs], preferred_element_type=f32) * inv_root
            sp = jnp.maximum(s, 0.0) + jnp.log1p(jnp.exp(-jnp.abs(s)))
            ws = (wcol * sp).reshape(HEAD_GROUP, BS, CHUNK)
            mix_ref[:, cs] += jnp.sum(ws, 0)
        return carry

    lax.fori_loop(0, groups, first_pass, 0)

    mixture = mix_ref[...]
    squashed = jnp.tanh(mixture / soft_cap)
    logits = soft_cap * squashed
    is_valid = spos_ref[...] <= qpos_ref[...]
    exp_terms = jnp.where(is_valid, jnp.exp(logits - soft_cap), 0.0)
    denominator = jnp.sum(exp_terms, 1, keepdims=True)
    log_prob = logits - soft_cap - jnp.log(denominator)
    kept_mass = jnp.where(is_valid, mass_ref[...].astype(f32), 0.0)
    target = kept_mass / jnp.sum(kept_mass, 1, keepdims=True)
    div_ref[...] = jnp.sum(
        jnp.where(is_valid, target * (jnp.log(jnp.where(is_valid, target, 1.0)) - log_prob), 0.0),
        1, keepdims=True)
    mg_ref[...] = (exp_terms / denominator - target) * (1.0 - squashed * squashed)

    sgt_ref[...] = jnp.zeros_like(sgt_ref)

    def second_pass(g, carry):
        r0 = pl.multiple_of(g * rows, rows)
        q = qr_ref[pl.ds(r0, rows), :]
        qt = qt_ref[:, pl.ds(r0, rows)]
        wcol = w_ref[pl.ds(r0, rows), :]
        qg_acc = jnp.zeros((rows, DH), f32)
        wg_acc = jnp.zeros((rows, 1), f32)
        for c in range(chunks):
            cs = slice(c * CHUNK, (c + 1) * CHUNK)
            s = jnp.dot(q, kt_ref[:, cs], preferred_element_type=f32) * inv_root
            e = jnp.exp(-jnp.abs(s))
            sp = jnp.maximum(s, 0.0) + jnp.log1p(e)
            r = 1.0 / (1.0 + e)
            sig = jnp.where(s >= 0.0, r, e * r)
            mgc = mg_ref[:, cs]
            mg4 = jnp.broadcast_to(mgc[None], (HEAD_GROUP, BS, CHUNK)).reshape(rows, CHUNK)
            sg = (mg4 * wcol * sig).astype(jnp.bfloat16)
            wg_acc = wg_acc + jnp.sum(mg4 * sp, 1, keepdims=True)
            qg_acc = qg_acc + jnp.dot(sg, k_ref[cs, :], preferred_element_type=f32)
            sgt_ref[:, cs] += jnp.dot(qt, sg, preferred_element_type=f32)
        qg_ref[pl.ds(r0, rows), :] = qg_acc * inv_root
        wg_ref[pl.ds(r0, rows), :] = wg_acc
        return carry

    lax.fori_loop(0, groups, second_pass, 0)
    sgt_ref[...] = sgt_ref[...] * inv_root


def score_blocks(qr, qt, k, kt, wcol, mass, spos, qpos):
    nblk, nrows, _ = qr.shape
    slots = k.shape[1]
    f32 = jnp.float32

    def blk(*shape):
        return pl.BlockSpec((None,) + shape, lambda b: (b,) + (0,) * len(shape))

    flops = nblk * (4 * 2 * nrows * slots * DH)
    return pl.pallas_call(
        score_kernel,
        grid=(nblk,),
        in_specs=[
            blk(nrows, DH), blk(DH, nrows), blk(slots, DH), blk(DH, slots),
            blk(nrows, 1), blk(BS, slots), blk(1, slots), blk(BS, 1),
        ],
        out_specs=[blk(nrows, DH), blk(nrows, 1), blk(DH, slots), blk(BS, 1)],
        out_shape=[
            jax.ShapeDtypeStruct((nblk, nrows, DH), f32),
            jax.ShapeDtypeStruct((nblk, nrows, 1), f32),
            jax.ShapeDtypeStruct((nblk, DH, slots), f32),
            jax.ShapeDtypeStruct((nblk, BS, 1), f32),
        ],
        scratch_shapes=[pltpu.VMEM((BS, slots), f32), pltpu.VMEM((BS, slots), f32)],
        compiler_params=pltpu.CompilerParams(dimension_semantics=("arbitrary",)),
        cost_estimate=pl.CostEstimate(
            flops=flops, transcendentals=nblk * nrows * slots * 5,
            bytes_accessed=nblk * (nrows * DH * 4 + slots * DH * 4 + nrows * DH * 4 + DH * slots * 4)),
    )(qr, qt, k, kt, wcol, mass, spos, qpos)


def per_device(queries, keys, head_weights, block_ids, target_mass, key_gain, key_bias):
    ctx_count = lax.axis_size("ctx")
    ctx_index = lax.axis_index("ctx")
    dp_count = lax.axis_size("dp")
    dp_index = lax.axis_index("dp")
    key_count = KD // BS
    query_count = QD // BS
    capacity = 2 * query_count
    request_count = query_count * NSEL
    slot_count = NSEL * BS
    key_hat, key_scale, normed_keys = key_norm(keys[0], key_gain, key_bias)
    listed_ids = block_ids[0].reshape(request_count)
    is_listed = listed_ids >= 0
    block_safe = jnp.maximum(listed_ids, 0)
    owner_index = block_safe // key_count
    local_block = block_safe % key_count
    owner_hits = (
        (owner_index[:, None] == jnp.arange(ctx_count, dtype=jnp.int32)[None, :])
        & is_listed[:, None]
    ).astype(jnp.int32)
    earlier = jnp.cumsum(owner_hits, 0) - owner_hits
    rank_slot = jnp.sum(earlier * owner_hits, 1)
    target_slot = jnp.where(is_listed, owner_index * capacity + rank_slot, 0)
    placement = (
        target_slot[:, None] == jnp.arange(ctx_count * capacity, dtype=jnp.int32)[None, :]
    ) & is_listed[:, None]
    request_table = jnp.sum(jnp.where(placement, local_block[:, None] + 1, 0), 0) - 1
    request_table = request_table.reshape(ctx_count, capacity)
    initial_slots = jnp.zeros((request_count, BS, DH), jnp.bfloat16)
    shard_rows = lax.all_gather(normed_keys, "ctx", axis=0, tiled=True)
    block_rows = shard_rows.shape[0] // BS
    relative = block_safe * BS
    inside = is_listed & (relative >= 0) & (relative < shard_rows.shape[0])
    picked = shard_rows.reshape(block_rows, BS, DH)[jnp.clip(relative // BS, 0, block_rows - 1)]
    slot_keys = jnp.where(inside[:, None, None], picked, initial_slots)
    slot_keys = slot_keys.reshape(query_count, slot_count, DH)
    slot_positions = (block_safe[:, None] * BS + jnp.arange(BS, dtype=jnp.int32)[None, :]).reshape(
        query_count, slot_count
    )
    slot_lives = jnp.repeat(is_listed, BS).reshape(query_count, slot_count)
    never = jnp.iinfo(jnp.int32).max
    slot_limit = jnp.where(slot_lives, slot_positions, never).reshape(query_count, 1, slot_count)
    query_hat, query_scale, normed_queries = query_norm(queries[0])
    first_pos = ctx_index * KD + KD - QD
    query_pos = (first_pos + jnp.arange(QD, dtype=jnp.int32)).reshape(query_count, BS, 1)

    head_rows = (
        normed_queries.reshape(query_count, BS, H, DH).transpose(0, 2, 1, 3).reshape(query_count, H * BS, DH)
    )
    head_cols = head_rows.transpose(0, 2, 1)
    key_cols = slot_keys.transpose(0, 2, 1)
    weight_col = (
        head_weights[0].astype(jnp.float32).reshape(query_count, BS, H).transpose(0, 2, 1)
        .reshape(query_count, H * BS, 1)
    )
    mass_rows = target_mass[0].reshape(query_count, BS, slot_count)
    qg_rows, wg_rows, slot_grad_t, div_rows = score_blocks(
        head_rows, head_cols, slot_keys, key_cols, weight_col, mass_rows, slot_limit, query_pos
    )
    divergence_total = jnp.sum(div_rows)
    query_grads = qg_rows.reshape(query_count, H, BS, DH).transpose(0, 2, 1, 3).reshape(QD, H, DH)
    weight_grads = wg_rows.reshape(query_count, H, BS).transpose(0, 2, 1).reshape(QD, H)
    grad_slots = slot_grad_t.transpose(0, 2, 1)

    grad_query_rows = (
        query_grads - query_hat * jnp.mean(query_grads * query_hat, -1, keepdims=True)
    ) * query_scale
    slot_flat = grad_slots.reshape(request_count, BS * DH)
    outbound = jnp.dot(placement.T.astype(jnp.float32), slot_flat, precision=lax.Precision.HIGHEST)
    returned, asked_back = (
        lax.all_to_all(
            outbound.reshape(ctx_count, capacity, BS * DH),
            "ctx",
            split_axis=0,
            concat_axis=0,
            tiled=True,
        ),
        lax.all_to_all(request_table, "ctx", split_axis=0, concat_axis=0, tiled=True),
    )
    own_rows = (
        asked_back.reshape(ctx_count * capacity)[None, :]
        == jnp.arange(key_count, dtype=jnp.int32)[:, None]
    ).astype(jnp.float32)
    key_grad = jnp.dot(
        own_rows, returned.reshape(ctx_count * capacity, BS * DH), precision=lax.Precision.HIGHEST
    ).reshape(KD, DH)
    gain_part = jnp.sum(key_grad * key_hat, 0)
    bias_part = jnp.sum(key_grad, 0)
    scaled_grad = key_grad * key_gain
    grad_key_rows = (
        scaled_grad
        - jnp.mean(scaled_grad, -1, keepdims=True)
        - key_hat * jnp.mean(scaled_grad * key_hat, -1, keepdims=True)
    ) * key_scale
    loss_slots = jnp.where(jnp.arange(dp_count) == dp_index, divergence_total, 0.0)
    packed = jnp.concatenate([gain_part, bias_part, loss_slots])
    packed = lax.psum(jnp.pad(packed, (0, max(16384, packed.shape[0]) - packed.shape[0])), ("dp", "ctx"))
    grad_gain = packed[:DH]
    grad_bias = packed[DH:2 * DH]
    loss_total = lax.dynamic_index_in_dim(packed, 2 * DH + dp_index, 0, keepdims=False)
    seq_loss = jnp.reshape(loss_total / (QD * ctx_count), (1,))
    return (
        seq_loss,
        grad_query_rows.reshape(1, QD, H * DH),
        weight_grads.reshape(1, QD, H),
        grad_key_rows.reshape(1, KD, DH),
        grad_gain,
        grad_bias,
    )


def solution(mesh):
    in_specs = (
        P("dp", "ctx", None),
        P("dp", "ctx", None),
        P("dp", "ctx", None),
        P("dp", "ctx", None),
        P("dp", "ctx", None),
        P(),
        P(),
    )
    out_specs = (
        P("dp"),
        P("dp", "ctx", None),
        P("dp", "ctx", None),
        P("dp", "ctx", None),
        P(),
        P(),
    )
    return jax.shard_map(
        per_device, mesh=mesh, in_specs=in_specs, out_specs=out_specs, check_vma=False
    )
```

```python
import functools
import jax
import jax.numpy as jnp
from jax import lax
from jax.experimental import pallas as pl
from jax.experimental.pallas import tpu as pltpu
from jax.sharding import PartitionSpec as P

H = 32
DH = 128
BS = 64
NSEL = 32
QD = 128
KD = 1024

epsilon = 1e-06
soft_cap = 20.0

HEAD_GROUP = 4
CHUNK = 512


def key_norm(key_rows, key_gain, key_bias):
    key_float = key_rows.astype(jnp.float32)
    key_mean = jnp.mean(key_float, -1, keepdims=True)
    centered = key_float - key_mean
    key_var = jnp.mean(centered * centered, -1, keepdims=True)
    key_scale = lax.rsqrt(key_var + epsilon)
    key_hat = centered * key_scale
    normed_keys = (key_hat * key_gain + key_bias).astype(jnp.bfloat16)
    return (key_hat, key_scale, normed_keys)


def query_norm(query_rows):
    query_float = query_rows.astype(jnp.float32).reshape(query_rows.shape[0], H, DH)
    query_scale = lax.rsqrt(jnp.mean(query_float * query_float, -1, keepdims=True) + epsilon)
    query_hat = query_float * query_scale
    return (query_hat, query_scale, query_hat.astype(jnp.bfloat16))


def score_kernel(qr_ref, qt_ref, k_ref, kt_ref, w_ref, mass_ref, spos_ref, qpos_ref,
                 qg_ref, wg_ref, sgt_ref, div_ref, mix_ref, mg_ref):
    f32 = jnp.float32
    inv_root = DH ** (-0.5)
    rows = HEAD_GROUP * BS
    groups = H // HEAD_GROUP
    slots = kt_ref.shape[1]
    chunks = slots // CHUNK

    mix_ref[...] = jnp.zeros_like(mix_ref)

    def first_pass(g, carry):
        r0 = pl.multiple_of(g * rows, rows)
        q = qr_ref[pl.ds(r0, rows), :]
        wcol = w_ref[pl.ds(r0, rows), :]
        for c in range(chunks):
            cs = slice(c * CHUNK, (c + 1) * CHUNK)
            s = jnp.dot(q, kt_ref[:, cs], preferred_element_type=f32) * inv_root
            sp = jnp.maximum(s, 0.0) + jnp.log1p(jnp.exp(-jnp.abs(s)))
            ws = (wcol * sp).reshape(HEAD_GROUP, BS, CHUNK)
            mix_ref[:, cs] += jnp.sum(ws, 0)
        return carry

    lax.fori_loop(0, groups, first_pass, 0)

    mixture = mix_ref[...]
    squashed = jnp.tanh(mixture / soft_cap)
    logits = soft_cap * squashed
    is_valid = spos_ref[...] <= qpos_ref[...]
    exp_terms = jnp.where(is_valid, jnp.exp(logits - soft_cap), 0.0)
    denominator = jnp.sum(exp_terms, 1, keepdims=True)
    log_prob = logits - soft_cap - jnp.log(denominator)
    kept_mass = jnp.where(is_valid, mass_ref[...].astype(f32), 0.0)
    target = kept_mass / jnp.sum(kept_mass, 1, keepdims=True)
    div_ref[...] = jnp.sum(
        jnp.where(is_valid, target * (jnp.log(jnp.where(is_valid, target, 1.0)) - log_prob), 0.0),
        1, keepdims=True)
    mg_ref[...] = (exp_terms / denominator - target) * (1.0 - squashed * squashed)

    sgt_ref[...] = jnp.zeros_like(sgt_ref)

    def second_pass(g, carry):
        r0 = pl.multiple_of(g * rows, rows)
        q = qr_ref[pl.ds(r0, rows), :]
        qt = qt_ref[:, pl.ds(r0, rows)]
        wcol = w_ref[pl.ds(r0, rows), :]
        qg_acc = jnp.zeros((rows, DH), f32)
        wg_acc = jnp.zeros((rows, 1), f32)
        for c in range(chunks):
            cs = slice(c * CHUNK, (c + 1) * CHUNK)
            s = jnp.dot(q, kt_ref[:, cs], preferred_element_type=f32) * inv_root
            e = jnp.exp(-jnp.abs(s))
            sp = jnp.maximum(s, 0.0) + jnp.log1p(e)
            r = 1.0 / (1.0 + e)
            sig = jnp.where(s >= 0.0, r, e * r)
            mgc = mg_ref[:, cs]
            mg4 = jnp.broadcast_to(mgc[None], (HEAD_GROUP, BS, CHUNK)).reshape(rows, CHUNK)
            sg = (mg4 * wcol * sig).astype(jnp.bfloat16)
            wg_acc = wg_acc + jnp.sum(mg4 * sp, 1, keepdims=True)
            qg_acc = qg_acc + jnp.dot(sg, k_ref[cs, :], preferred_element_type=f32)
            sgt_ref[:, cs] += jnp.dot(qt, sg, preferred_element_type=f32)
        qg_ref[pl.ds(r0, rows), :] = qg_acc * inv_root
        wg_ref[pl.ds(r0, rows), :] = wg_acc
        return carry

    lax.fori_loop(0, groups, second_pass, 0)
    sgt_ref[...] = sgt_ref[...] * inv_root


def score_blocks(qr, qt, k, kt, wcol, mass, spos, qpos):
    nblk, nrows, _ = qr.shape
    slots = k.shape[1]
    f32 = jnp.float32

    def blk(*shape):
        return pl.BlockSpec((None,) + shape, lambda b: (b,) + (0,) * len(shape))

    flops = nblk * (4 * 2 * nrows * slots * DH)
    return pl.pallas_call(
        score_kernel,
        grid=(nblk,),
        in_specs=[
            blk(nrows, DH), blk(DH, nrows), blk(slots, DH), blk(DH, slots),
            blk(nrows, 1), blk(BS, slots), blk(1, slots), blk(BS, 1),
        ],
        out_specs=[blk(nrows, DH), blk(nrows, 1), blk(DH, slots), blk(BS, 1)],
        out_shape=[
            jax.ShapeDtypeStruct((nblk, nrows, DH), f32),
            jax.ShapeDtypeStruct((nblk, nrows, 1), f32),
            jax.ShapeDtypeStruct((nblk, DH, slots), f32),
            jax.ShapeDtypeStruct((nblk, BS, 1), f32),
        ],
        scratch_shapes=[pltpu.VMEM((BS, slots), f32), pltpu.VMEM((BS, slots), f32)],
        compiler_params=pltpu.CompilerParams(dimension_semantics=("arbitrary",)),
        cost_estimate=pl.CostEstimate(
            flops=flops, transcendentals=nblk * nrows * slots * 5,
            bytes_accessed=nblk * (nrows * DH * 4 + slots * DH * 4 + nrows * DH * 4 + DH * slots * 4)),
    )(qr, qt, k, kt, wcol, mass, spos, qpos)


def butterfly_sum(value, axes):
    count = 1
    for axis in axes:
        count *= lax.axis_size(axis)
    if count & (count - 1):
        return lax.psum(value, axes)
    stride = 1
    while stride < count:
        pairs = [(i, i ^ stride) for i in range(count)]
        value = value + lax.ppermute(value, axes, pairs)
        stride *= 2
    return value


def per_device(queries, keys, head_weights, block_ids, target_mass, key_gain, key_bias):
    ctx_count = lax.axis_size("ctx")
    ctx_index = lax.axis_index("ctx")
    dp_count = lax.axis_size("dp")
    dp_index = lax.axis_index("dp")
    key_count = KD // BS
    query_count = QD // BS
    capacity = 2 * query_count
    request_count = query_count * NSEL
    slot_count = NSEL * BS
    key_hat, key_scale, normed_keys = key_norm(keys[0], key_gain, key_bias)
    listed_ids = block_ids[0].reshape(request_count)
    is_listed = listed_ids >= 0
    block_safe = jnp.maximum(listed_ids, 0)
    owner_index = block_safe // key_count
    local_block = block_safe % key_count
    owner_hits = (
        (owner_index[:, None] == jnp.arange(ctx_count, dtype=jnp.int32)[None, :])
        & is_listed[:, None]
    ).astype(jnp.int32)
    earlier = jnp.cumsum(owner_hits, 0) - owner_hits
    rank_slot = jnp.sum(earlier * owner_hits, 1)
    target_slot = jnp.where(is_listed, owner_index * capacity + rank_slot, 0)
    placement = (
        target_slot[:, None] == jnp.arange(ctx_count * capacity, dtype=jnp.int32)[None, :]
    ) & is_listed[:, None]
    request_table = jnp.sum(jnp.where(placement, local_block[:, None] + 1, 0), 0) - 1
    request_table = request_table.reshape(ctx_count, capacity)
    initial_slots = jnp.zeros((request_count, BS, DH), jnp.bfloat16)
    shard_rows = lax.all_gather(normed_keys, "ctx", axis=0, tiled=True)
    block_rows = shard_rows.shape[0] // BS
    relative = block_safe * BS
    inside = is_listed & (relative >= 0) & (relative < shard_rows.shape[0])
    picked = shard_rows.reshape(block_rows, BS, DH)[jnp.clip(relative // BS, 0, block_rows - 1)]
    slot_keys = jnp.where(inside[:, None, None], picked, initial_slots)
    slot_keys = slot_keys.reshape(query_count, slot_count, DH)
    slot_positions = (block_safe[:, None] * BS + jnp.arange(BS, dtype=jnp.int32)[None, :]).reshape(
        query_count, slot_count
    )
    slot_lives = jnp.repeat(is_listed, BS).reshape(query_count, slot_count)
    never = jnp.iinfo(jnp.int32).max
    slot_limit = jnp.where(slot_lives, slot_positions, never).reshape(query_count, 1, slot_count)
    query_hat, query_scale, normed_queries = query_norm(queries[0])
    first_pos = ctx_index * KD + KD - QD
    query_pos = (first_pos + jnp.arange(QD, dtype=jnp.int32)).reshape(query_count, BS, 1)

    head_rows = (
        normed_queries.reshape(query_count, BS, H, DH).transpose(0, 2, 1, 3).reshape(query_count, H * BS, DH)
    )
    head_cols = head_rows.transpose(0, 2, 1)
    key_cols = slot_keys.transpose(0, 2, 1)
    weight_col = (
        head_weights[0].astype(jnp.float32).reshape(query_count, BS, H).transpose(0, 2, 1)
        .reshape(query_count, H * BS, 1)
    )
    mass_rows = target_mass[0].reshape(query_count, BS, slot_count)
    qg_rows, wg_rows, slot_grad_t, div_rows = score_blocks(
        head_rows, head_cols, slot_keys, key_cols, weight_col, mass_rows, slot_limit, query_pos
    )
    divergence_total = jnp.sum(div_rows)
    query_grads = qg_rows.reshape(query_count, H, BS, DH).transpose(0, 2, 1, 3).reshape(QD, H, DH)
    weight_grads = wg_rows.reshape(query_count, H, BS).transpose(0, 2, 1).reshape(QD, H)
    grad_slots = slot_grad_t.transpose(0, 2, 1)

    grad_query_rows = (
        query_grads - query_hat * jnp.mean(query_grads * query_hat, -1, keepdims=True)
    ) * query_scale
    slot_flat = grad_slots.reshape(request_count, BS * DH)
    outbound = jnp.dot(placement.T.astype(jnp.float32), slot_flat, precision=lax.Precision.HIGHEST)
    returned, asked_back = (
        lax.all_to_all(
            outbound.reshape(ctx_count, capacity, BS * DH),
            "ctx",
            split_axis=0,
            concat_axis=0,
            tiled=True,
        ),
        lax.all_to_all(request_table, "ctx", split_axis=0, concat_axis=0, tiled=True),
    )
    own_rows = (
        asked_back.reshape(ctx_count * capacity)[None, :]
        == jnp.arange(key_count, dtype=jnp.int32)[:, None]
    ).astype(jnp.float32)
    key_grad = jnp.dot(
        own_rows, returned.reshape(ctx_count * capacity, BS * DH), precision=lax.Precision.HIGHEST
    ).reshape(KD, DH)
    gain_part = jnp.sum(key_grad * key_hat, 0)
    bias_part = jnp.sum(key_grad, 0)
    scaled_grad = key_grad * key_gain
    grad_key_rows = (
        scaled_grad
        - jnp.mean(scaled_grad, -1, keepdims=True)
        - key_hat * jnp.mean(scaled_grad * key_hat, -1, keepdims=True)
    ) * key_scale
    loss_slots = jnp.where(jnp.arange(dp_count) == dp_index, divergence_total, 0.0)
    packed = butterfly_sum(jnp.concatenate([gain_part, bias_part, loss_slots]), ("dp", "ctx"))
    grad_gain = packed[:DH]
    grad_bias = packed[DH:2 * DH]
    loss_total = lax.dynamic_index_in_dim(packed, 2 * DH + dp_index, 0, keepdims=False)
    seq_loss = jnp.reshape(loss_total / (QD * ctx_count), (1,))
    return (
        seq_loss,
        grad_query_rows.reshape(1, QD, H * DH),
        weight_grads.reshape(1, QD, H),
        grad_key_rows.reshape(1, KD, DH),
        grad_gain,
        grad_bias,
    )


def solution(mesh):
    in_specs = (
        P("dp", "ctx", None),
        P("dp", "ctx", None),
        P("dp", "ctx", None),
        P("dp", "ctx", None),
        P("dp", "ctx", None),
        P(),
        P(),
    )
    out_specs = (
        P("dp"),
        P("dp", "ctx", None),
        P("dp", "ctx", None),
        P("dp", "ctx", None),
        P(),
        P(),
    )
    return jax.shard_map(
        per_device, mesh=mesh, in_specs=in_specs, out_specs=out_specs, check_vma=False
    )
```

```python
import functools
import jax
import jax.numpy as jnp
from jax import lax
from jax.experimental import pallas as pl
from jax.experimental.pallas import tpu as pltpu
from jax.sharding import PartitionSpec as P

H = 32
DH = 128
BS = 64
NSEL = 32
QD = 128
KD = 1024

epsilon = 1e-06
soft_cap = 20.0

HEAD_GROUP = 4
CHUNK = 512


def key_norm(key_rows, key_gain, key_bias):
    key_float = key_rows.astype(jnp.float32)
    key_mean = jnp.mean(key_float, -1, keepdims=True)
    centered = key_float - key_mean
    key_var = jnp.mean(centered * centered, -1, keepdims=True)
    key_scale = lax.rsqrt(key_var + epsilon)
    key_hat = centered * key_scale
    normed_keys = (key_hat * key_gain + key_bias).astype(jnp.bfloat16)
    return (key_hat, key_scale, normed_keys)


def query_norm(query_rows):
    query_float = query_rows.astype(jnp.float32).reshape(query_rows.shape[0], H, DH)
    query_scale = lax.rsqrt(jnp.mean(query_float * query_float, -1, keepdims=True) + epsilon)
    query_hat = query_float * query_scale
    return (query_hat, query_scale, query_hat.astype(jnp.bfloat16))


def score_kernel(qr_ref, qt_ref, k_ref, kt_ref, w_ref, mass_ref, spos_ref, qpos_ref,
                 qg_ref, wg_ref, sgt_ref, div_ref, mix_ref, mg_ref, sp_ref):
    f32 = jnp.float32
    inv_root = DH ** (-0.5)
    rows = HEAD_GROUP * BS
    groups = H // HEAD_GROUP
    slots = kt_ref.shape[1]
    chunks = slots // CHUNK

    mix_ref[...] = jnp.zeros_like(mix_ref)

    def first_pass(g, carry):
        r0 = pl.multiple_of(g * rows, rows)
        q = qr_ref[pl.ds(r0, rows), :]
        wcol = w_ref[pl.ds(r0, rows), :]
        for c in range(chunks):
            cs = slice(c * CHUNK, (c + 1) * CHUNK)
            s = jnp.dot(q, kt_ref[:, cs], preferred_element_type=f32) * inv_root
            sp = jnp.maximum(s, 0.0) + jnp.log1p(jnp.exp(-jnp.abs(s)))
            sp_ref[pl.ds(r0, rows), cs] = sp
            ws = (wcol * sp).reshape(HEAD_GROUP, BS, CHUNK)
            mix_ref[:, cs] += jnp.sum(ws, 0)
        return carry

    lax.fori_loop(0, groups, first_pass, 0)

    mixture = mix_ref[...]
    squashed = jnp.tanh(mixture / soft_cap)
    logits = soft_cap * squashed
    is_valid = spos_ref[...] <= qpos_ref[...]
    exp_terms = jnp.where(is_valid, jnp.exp(logits - soft_cap), 0.0)
    denominator = jnp.sum(exp_terms, 1, keepdims=True)
    log_prob = logits - soft_cap - jnp.log(denominator)
    kept_mass = jnp.where(is_valid, mass_ref[...].astype(f32), 0.0)
    target = kept_mass / jnp.sum(kept_mass, 1, keepdims=True)
    div_ref[...] = jnp.sum(
        jnp.where(is_valid, target * (jnp.log(jnp.where(is_valid, target, 1.0)) - log_prob), 0.0),
        1, keepdims=True)
    mg_ref[...] = (exp_terms / denominator - target) * (1.0 - squashed * squashed)

    sgt_ref[...] = jnp.zeros_like(sgt_ref)

    def second_pass(g, carry):
        r0 = pl.multiple_of(g * rows, rows)
        q = qr_ref[pl.ds(r0, rows), :]
        qt = qt_ref[:, pl.ds(r0, rows)]
        wcol = w_ref[pl.ds(r0, rows), :]
        qg_acc = jnp.zeros((rows, DH), f32)
        wg_acc = jnp.zeros((rows, 1), f32)
        for c in range(chunks):
            cs = slice(c * CHUNK, (c + 1) * CHUNK)
            s = jnp.dot(q, kt_ref[:, cs], preferred_element_type=f32) * inv_root
            sp = sp_ref[pl.ds(r0, rows), cs]
            sig = jnp.exp(s - sp)
            mgc = mg_ref[:, cs]
            mg4 = jnp.broadcast_to(mgc[None], (HEAD_GROUP, BS, CHUNK)).reshape(rows, CHUNK)
            sg = (mg4 * wcol * sig).astype(jnp.bfloat16)
            wg_acc = wg_acc + jnp.sum(mg4 * sp, 1, keepdims=True)
            qg_acc = qg_acc + jnp.dot(sg, k_ref[cs, :], preferred_element_type=f32)
            sgt_ref[:, cs] += jnp.dot(qt, sg, preferred_element_type=f32)
        qg_ref[pl.ds(r0, rows), :] = qg_acc * inv_root
        wg_ref[pl.ds(r0, rows), :] = wg_acc
        return carry

    lax.fori_loop(0, groups, second_pass, 0)
    sgt_ref[...] = sgt_ref[...] * inv_root


def score_blocks(qr, qt, k, kt, wcol, mass, spos, qpos):
    nblk, nrows, _ = qr.shape
    slots = k.shape[1]
    f32 = jnp.float32

    def blk(*shape):
        return pl.BlockSpec((None,) + shape, lambda b: (b,) + (0,) * len(shape))

    flops = nblk * (4 * 2 * nrows * slots * DH)
    return pl.pallas_call(
        score_kernel,
        grid=(nblk,),
        in_specs=[
            blk(nrows, DH), blk(DH, nrows), blk(slots, DH), blk(DH, slots),
            blk(nrows, 1), blk(BS, slots), blk(1, slots), blk(BS, 1),
        ],
        out_specs=[blk(nrows, DH), blk(nrows, 1), blk(DH, slots), blk(BS, 1)],
        out_shape=[
            jax.ShapeDtypeStruct((nblk, nrows, DH), f32),
            jax.ShapeDtypeStruct((nblk, nrows, 1), f32),
            jax.ShapeDtypeStruct((nblk, DH, slots), f32),
            jax.ShapeDtypeStruct((nblk, BS, 1), f32),
        ],
        scratch_shapes=[
            pltpu.VMEM((BS, slots), f32), pltpu.VMEM((BS, slots), f32), pltpu.VMEM((nrows, slots), f32)
        ],
        compiler_params=pltpu.CompilerParams(
            dimension_semantics=("arbitrary",), vmem_limit_bytes=60 * 1024 * 1024
        ),
        cost_estimate=pl.CostEstimate(
            flops=flops, transcendentals=nblk * nrows * slots * 3,
            bytes_accessed=nblk * (nrows * DH * 4 + slots * DH * 4 + nrows * DH * 4 + DH * slots * 4)),
    )(qr, qt, k, kt, wcol, mass, spos, qpos)


def butterfly_sum(value, axes):
    count = 1
    for axis in axes:
        count *= lax.axis_size(axis)
    if count & (count - 1):
        return lax.psum(value, axes)
    stride = 1
    while stride < count:
        pairs = [(i, i ^ stride) for i in range(count)]
        value = value + lax.ppermute(value, axes, pairs)
        stride *= 2
    return value


def per_device(queries, keys, head_weights, block_ids, target_mass, key_gain, key_bias):
    ctx_count = lax.axis_size("ctx")
    ctx_index = lax.axis_index("ctx")
    dp_count = lax.axis_size("dp")
    dp_index = lax.axis_index("dp")
    key_count = KD // BS
    query_count = QD // BS
    capacity = 2 * query_count
    request_count = query_count * NSEL
    slot_count = NSEL * BS
    key_hat, key_scale, normed_keys = key_norm(keys[0], key_gain, key_bias)
    listed_ids = block_ids[0].reshape(request_count)
    is_listed = listed_ids >= 0
    block_safe = jnp.maximum(listed_ids, 0)
    owner_index = block_safe // key_count
    local_block = block_safe % key_count
    owner_hits = (
        (owner_index[:, None] == jnp.arange(ctx_count, dtype=jnp.int32)[None, :])
        & is_listed[:, None]
    ).astype(jnp.int32)
    earlier = jnp.cumsum(owner_hits, 0) - owner_hits
    rank_slot = jnp.sum(earlier * owner_hits, 1)
    target_slot = jnp.where(is_listed, owner_index * capacity + rank_slot, 0)
    placement = (
        target_slot[:, None] == jnp.arange(ctx_count * capacity, dtype=jnp.int32)[None, :]
    ) & is_listed[:, None]
    request_table = jnp.sum(jnp.where(placement, local_block[:, None] + 1, 0), 0) - 1
    request_table = request_table.reshape(ctx_count, capacity)
    initial_slots = jnp.zeros((request_count, BS, DH), jnp.bfloat16)
    shard_rows = lax.all_gather(normed_keys, "ctx", axis=0, tiled=True)
    block_rows = shard_rows.shape[0] // BS
    relative = block_safe * BS
    inside = is_listed & (relative >= 0) & (relative < shard_rows.shape[0])
    picked = shard_rows.reshape(block_rows, BS, DH)[jnp.clip(relative // BS, 0, block_rows - 1)]
    slot_keys = jnp.where(inside[:, None, None], picked, initial_slots)
    slot_keys = slot_keys.reshape(query_count, slot_count, DH)
    slot_positions = (block_safe[:, None] * BS + jnp.arange(BS, dtype=jnp.int32)[None, :]).reshape(
        query_count, slot_count
    )
    slot_lives = jnp.repeat(is_listed, BS).reshape(query_count, slot_count)
    never = jnp.iinfo(jnp.int32).max
    slot_limit = jnp.where(slot_lives, slot_positions, never).reshape(query_count, 1, slot_count)
    query_hat, query_scale, normed_queries = query_norm(queries[0])
    first_pos = ctx_index * KD + KD - QD
    query_pos = (first_pos + jnp.arange(QD, dtype=jnp.int32)).reshape(query_count, BS, 1)

    head_rows = (
        normed_queries.reshape(query_count, BS, H, DH).transpose(0, 2, 1, 3).reshape(query_count, H * BS, DH)
    )
    head_cols = head_rows.transpose(0, 2, 1)
    key_cols = slot_keys.transpose(0, 2, 1)
    weight_col = (
        head_weights[0].astype(jnp.float32).reshape(query_count, BS, H).transpose(0, 2, 1)
        .reshape(query_count, H * BS, 1)
    )
    mass_rows = target_mass[0].reshape(query_count, BS, slot_count)
    qg_rows, wg_rows, slot_grad_t, div_rows = score_blocks(
        head_rows, head_cols, slot_keys, key_cols, weight_col, mass_rows, slot_limit, query_pos
    )
    divergence_total = jnp.sum(div_rows)
    query_grads = qg_rows.reshape(query_count, H, BS, DH).transpose(0, 2, 1, 3).reshape(QD, H, DH)
    weight_grads = wg_rows.reshape(query_count, H, BS).transpose(0, 2, 1).reshape(QD, H)
    grad_slots = slot_grad_t.transpose(0, 2, 1)

    grad_query_rows = (
        query_grads - query_hat * jnp.mean(query_grads * query_hat, -1, keepdims=True)
    ) * query_scale
    slot_flat = grad_slots.reshape(request_count, BS * DH)
    outbound = jnp.dot(placement.T.astype(jnp.float32), slot_flat, precision=lax.Precision.HIGHEST)
    returned, asked_back = (
        lax.all_to_all(
            outbound.reshape(ctx_count, capacity, BS * DH),
            "ctx",
            split_axis=0,
            concat_axis=0,
            tiled=True,
        ),
        lax.all_to_all(request_table, "ctx", split_axis=0, concat_axis=0, tiled=True),
    )
    own_rows = (
        asked_back.reshape(ctx_count * capacity)[None, :]
        == jnp.arange(key_count, dtype=jnp.int32)[:, None]
    ).astype(jnp.float32)
    key_grad = jnp.dot(
        own_rows, returned.reshape(ctx_count * capacity, BS * DH), precision=lax.Precision.HIGHEST
    ).reshape(KD, DH)
    gain_part = jnp.sum(key_grad * key_hat, 0)
    bias_part = jnp.sum(key_grad, 0)
    scaled_grad = key_grad * key_gain
    grad_key_rows = (
        scaled_grad
        - jnp.mean(scaled_grad, -1, keepdims=True)
        - key_hat * jnp.mean(scaled_grad * key_hat, -1, keepdims=True)
    ) * key_scale
    loss_slots = jnp.where(jnp.arange(dp_count) == dp_index, divergence_total, 0.0)
    packed = butterfly_sum(jnp.concatenate([gain_part, bias_part, loss_slots]), ("dp", "ctx"))
    grad_gain = packed[:DH]
    grad_bias = packed[DH:2 * DH]
    loss_total = lax.dynamic_index_in_dim(packed, 2 * DH + dp_index, 0, keepdims=False)
    seq_loss = jnp.reshape(loss_total / (QD * ctx_count), (1,))
    return (
        seq_loss,
        grad_query_rows.reshape(1, QD, H * DH),
        weight_grads.reshape(1, QD, H),
        grad_key_rows.reshape(1, KD, DH),
        grad_gain,
        grad_bias,
    )


def solution(mesh):
    in_specs = (
        P("dp", "ctx", None),
        P("dp", "ctx", None),
        P("dp", "ctx", None),
        P("dp", "ctx", None),
        P("dp", "ctx", None),
        P(),
        P(),
    )
    out_specs = (
        P("dp"),
        P("dp", "ctx", None),
        P("dp", "ctx", None),
        P("dp", "ctx", None),
        P(),
        P(),
    )
    return jax.shard_map(
        per_device, mesh=mesh, in_specs=in_specs, out_specs=out_specs, check_vma=False
    )
```

```python
import functools
import jax
import jax.numpy as jnp
from jax import lax
from jax.experimental import pallas as pl
from jax.experimental.pallas import tpu as pltpu
from jax.sharding import PartitionSpec as P

H = 32
DH = 128
BS = 64
NSEL = 32
QD = 128
KD = 1024

epsilon = 1e-06
soft_cap = 20.0

HEAD_GROUP = 4
CHUNK = 512


def key_norm(key_rows, key_gain, key_bias):
    key_float = key_rows.astype(jnp.float32)
    key_mean = jnp.mean(key_float, -1, keepdims=True)
    centered = key_float - key_mean
    key_var = jnp.mean(centered * centered, -1, keepdims=True)
    key_scale = lax.rsqrt(key_var + epsilon)
    key_hat = centered * key_scale
    normed_keys = (key_hat * key_gain + key_bias).astype(jnp.bfloat16)
    return (key_hat, key_scale, normed_keys)


def query_norm(query_rows):
    query_float = query_rows.astype(jnp.float32).reshape(query_rows.shape[0], H, DH)
    query_scale = lax.rsqrt(jnp.mean(query_float * query_float, -1, keepdims=True) + epsilon)
    query_hat = query_float * query_scale
    return (query_hat, query_scale, query_hat.astype(jnp.bfloat16))


def score_kernel(qr_ref, qt_ref, k_ref, kt_ref, w_ref, mass_ref, spos_ref, qpos_ref,
                 qg_ref, wg_ref, sgt_ref, div_ref, mix_ref, mg_ref, sp_ref):
    f32 = jnp.float32
    inv_root = DH ** (-0.5)
    rows = HEAD_GROUP * BS
    groups = H // HEAD_GROUP
    slots = kt_ref.shape[1]
    chunks = slots // CHUNK

    mix_ref[...] = jnp.zeros_like(mix_ref)

    def first_pass(g, carry):
        r0 = pl.multiple_of(g * rows, rows)
        q = qr_ref[pl.ds(r0, rows), :]
        wcol = w_ref[pl.ds(r0, rows), :]
        for c in range(chunks):
            cs = slice(c * CHUNK, (c + 1) * CHUNK)
            s = jnp.dot(q, kt_ref[:, cs], preferred_element_type=f32) * inv_root
            sp = jnp.maximum(s, 0.0) + jnp.log1p(jnp.exp(-jnp.abs(s)))
            sp_ref[pl.ds(r0, rows), cs] = sp
            ws = (wcol * sp).reshape(HEAD_GROUP, BS, CHUNK)
            mix_ref[:, cs] += jnp.sum(ws, 0)
        return carry

    lax.fori_loop(0, groups, first_pass, 0)

    mixture = mix_ref[...]
    squashed = jnp.tanh(mixture / soft_cap)
    logits = soft_cap * squashed
    is_valid = spos_ref[...] <= qpos_ref[...]
    exp_terms = jnp.where(is_valid, jnp.exp(logits - soft_cap), 0.0)
    denominator = jnp.sum(exp_terms, 1, keepdims=True)
    log_prob = logits - soft_cap - jnp.log(denominator)
    kept_mass = jnp.where(is_valid, mass_ref[...].astype(f32), 0.0)
    target = kept_mass / jnp.sum(kept_mass, 1, keepdims=True)
    div_ref[...] = jnp.sum(
        jnp.where(is_valid, target * (jnp.log(jnp.where(is_valid, target, 1.0)) - log_prob), 0.0),
        1, keepdims=True)
    mg_ref[...] = (exp_terms / denominator - target) * (1.0 - squashed * squashed)

    sgt_ref[...] = jnp.zeros_like(sgt_ref)

    def second_pass(g, carry):
        r0 = pl.multiple_of(g * rows, rows)
        q = qr_ref[pl.ds(r0, rows), :]
        qt = qt_ref[:, pl.ds(r0, rows)]
        wcol = w_ref[pl.ds(r0, rows), :]
        qg_acc = jnp.zeros((rows, DH), f32)
        wg_acc = jnp.zeros((rows, 1), f32)
        for c in range(chunks):
            cs = slice(c * CHUNK, (c + 1) * CHUNK)
            s = jnp.dot(q, kt_ref[:, cs], preferred_element_type=f32) * inv_root
            sp = sp_ref[pl.ds(r0, rows), cs]
            sig = jnp.exp(s - sp)
            mgc = mg_ref[:, cs]
            mg4 = jnp.broadcast_to(mgc[None], (HEAD_GROUP, BS, CHUNK)).reshape(rows, CHUNK)
            sg = (mg4 * wcol * sig).astype(jnp.bfloat16)
            wg_acc = wg_acc + jnp.sum(mg4 * sp, 1, keepdims=True)
            qg_acc = qg_acc + jnp.dot(sg, k_ref[cs, :], preferred_element_type=f32)
            sgt_ref[:, cs] += jnp.dot(qt, sg, preferred_element_type=f32)
        qg_ref[pl.ds(r0, rows), :] = qg_acc * inv_root
        wg_ref[pl.ds(r0, rows), :] = wg_acc
        return carry

    lax.fori_loop(0, groups, second_pass, 0)
    sgt_ref[...] = sgt_ref[...] * inv_root


def score_blocks(qr, qt, k, kt, wcol, mass, spos, qpos):
    nblk, nrows, _ = qr.shape
    slots = k.shape[1]
    f32 = jnp.float32

    def blk(*shape):
        return pl.BlockSpec((None,) + shape, lambda b: (b,) + (0,) * len(shape))

    flops = nblk * (4 * 2 * nrows * slots * DH)
    return pl.pallas_call(
        score_kernel,
        grid=(nblk,),
        in_specs=[
            blk(nrows, DH), blk(DH, nrows), blk(slots, DH), blk(DH, slots),
            blk(nrows, 1), blk(BS, slots), blk(1, slots), blk(BS, 1),
        ],
        out_specs=[blk(nrows, DH), blk(nrows, 1), blk(DH, slots), blk(BS, 1)],
        out_shape=[
            jax.ShapeDtypeStruct((nblk, nrows, DH), f32),
            jax.ShapeDtypeStruct((nblk, nrows, 1), f32),
            jax.ShapeDtypeStruct((nblk, DH, slots), f32),
            jax.ShapeDtypeStruct((nblk, BS, 1), f32),
        ],
        scratch_shapes=[
            pltpu.VMEM((BS, slots), f32), pltpu.VMEM((BS, slots), f32), pltpu.VMEM((nrows, slots), f32)
        ],
        compiler_params=pltpu.CompilerParams(
            dimension_semantics=("arbitrary",), vmem_limit_bytes=60 * 1024 * 1024
        ),
        cost_estimate=pl.CostEstimate(
            flops=flops, transcendentals=nblk * nrows * slots * 3,
            bytes_accessed=nblk * (nrows * DH * 4 + slots * DH * 4 + nrows * DH * 4 + DH * slots * 4)),
    )(qr, qt, k, kt, wcol, mass, spos, qpos)


def butterfly_sum(value, axes):
    count = 1
    for axis in axes:
        count *= lax.axis_size(axis)
    if count & (count - 1):
        return lax.psum(value, axes)
    stride = 1
    while stride < count:
        pairs = [(i, i ^ stride) for i in range(count)]
        value = value + lax.ppermute(value, axes, pairs)
        stride *= 2
    return value


def per_device(queries, keys, head_weights, block_ids, target_mass, key_gain, key_bias):
    ctx_count = lax.axis_size("ctx")
    ctx_index = lax.axis_index("ctx")
    dp_count = lax.axis_size("dp")
    dp_index = lax.axis_index("dp")
    key_count = KD // BS
    query_count = QD // BS
    capacity = 2 * query_count
    request_count = query_count * NSEL
    slot_count = NSEL * BS
    key_hat, key_scale, normed_keys = key_norm(keys[0], key_gain, key_bias)
    listed_ids = block_ids[0].reshape(request_count)
    is_listed = listed_ids >= 0
    block_safe = jnp.maximum(listed_ids, 0)
    owner_index = block_safe // key_count
    local_block = block_safe % key_count
    owner_hits = (
        (owner_index[:, None] == jnp.arange(ctx_count, dtype=jnp.int32)[None, :])
        & is_listed[:, None]
    ).astype(jnp.int32)
    earlier = jnp.cumsum(owner_hits, 0) - owner_hits
    rank_slot = jnp.sum(earlier * owner_hits, 1)
    target_slot = jnp.where(is_listed, owner_index * capacity + rank_slot, 0)
    placement = (
        target_slot[:, None] == jnp.arange(ctx_count * capacity, dtype=jnp.int32)[None, :]
    ) & is_listed[:, None]
    request_table = jnp.sum(jnp.where(placement, local_block[:, None] + 1, 0), 0) - 1
    request_table = request_table.reshape(ctx_count, capacity)
    shard_rows = lax.all_gather(normed_keys, "ctx", axis=0, tiled=True)
    block_rows = shard_rows.shape[0] // BS
    picked = shard_rows.reshape(block_rows, BS, DH)[jnp.clip(block_safe, 0, block_rows - 1)]
    slot_keys = picked.reshape(query_count, slot_count, DH)
    slot_positions = (block_safe[:, None] * BS + jnp.arange(BS, dtype=jnp.int32)[None, :]).reshape(
        query_count, slot_count
    )
    slot_lives = jnp.repeat(is_listed, BS).reshape(query_count, slot_count)
    never = jnp.iinfo(jnp.int32).max
    slot_limit = jnp.where(slot_lives, slot_positions, never).reshape(query_count, 1, slot_count)
    query_hat, query_scale, normed_queries = query_norm(queries[0])
    first_pos = ctx_index * KD + KD - QD
    query_pos = (first_pos + jnp.arange(QD, dtype=jnp.int32)).reshape(query_count, BS, 1)

    head_rows = (
        normed_queries.reshape(query_count, BS, H, DH).transpose(0, 2, 1, 3).reshape(query_count, H * BS, DH)
    )
    head_cols = head_rows.transpose(0, 2, 1)
    key_cols = slot_keys.transpose(0, 2, 1)
    weight_col = (
        head_weights[0].astype(jnp.float32).reshape(query_count, BS, H).transpose(0, 2, 1)
        .reshape(query_count, H * BS, 1)
    )
    mass_rows = target_mass[0].reshape(query_count, BS, slot_count)
    qg_rows, wg_rows, slot_grad_t, div_rows = score_blocks(
        head_rows, head_cols, slot_keys, key_cols, weight_col, mass_rows, slot_limit, query_pos
    )
    divergence_total = jnp.sum(div_rows)
    query_grads = qg_rows.reshape(query_count, H, BS, DH).transpose(0, 2, 1, 3).reshape(QD, H, DH)
    weight_grads = wg_rows.reshape(query_count, H, BS).transpose(0, 2, 1).reshape(QD, H)
    grad_slots = slot_grad_t.transpose(0, 2, 1)

    grad_query_rows = (
        query_grads - query_hat * jnp.mean(query_grads * query_hat, -1, keepdims=True)
    ) * query_scale
    slot_flat = grad_slots.reshape(request_count, BS * DH)
    outbound = jnp.dot(placement.T.astype(jnp.float32), slot_flat, precision=lax.Precision.HIGHEST)
    id_lanes = jnp.broadcast_to(request_table.astype(jnp.float32)[:, :, None], (ctx_count, capacity, 128))
    combined = lax.all_to_all(
        jnp.concatenate([outbound.reshape(ctx_count, capacity, BS * DH), id_lanes], -1),
        "ctx",
        split_axis=0,
        concat_axis=0,
        tiled=True,
    )
    returned = combined[:, :, : BS * DH]
    asked_back = combined[:, :, BS * DH].astype(jnp.int32)
    own_rows = (
        asked_back.reshape(ctx_count * capacity)[None, :]
        == jnp.arange(key_count, dtype=jnp.int32)[:, None]
    ).astype(jnp.float32)
    key_grad = jnp.dot(
        own_rows, returned.reshape(ctx_count * capacity, BS * DH), precision=lax.Precision.HIGHEST
    ).reshape(KD, DH)
    gain_part = jnp.sum(key_grad * key_hat, 0)
    bias_part = jnp.sum(key_grad, 0)
    scaled_grad = key_grad * key_gain
    grad_key_rows = (
        scaled_grad
        - jnp.mean(scaled_grad, -1, keepdims=True)
        - key_hat * jnp.mean(scaled_grad * key_hat, -1, keepdims=True)
    ) * key_scale
    loss_slots = jnp.where(jnp.arange(dp_count) == dp_index, divergence_total, 0.0)
    packed = butterfly_sum(jnp.concatenate([gain_part, bias_part, loss_slots]), ("dp", "ctx"))
    grad_gain = packed[:DH]
    grad_bias = packed[DH:2 * DH]
    loss_total = lax.dynamic_index_in_dim(packed, 2 * DH + dp_index, 0, keepdims=False)
    seq_loss = jnp.reshape(loss_total / (QD * ctx_count), (1,))
    return (
        seq_loss,
        grad_query_rows.reshape(1, QD, H * DH),
        weight_grads.reshape(1, QD, H),
        grad_key_rows.reshape(1, KD, DH),
        grad_gain,
        grad_bias,
    )


def solution(mesh):
    in_specs = (
        P("dp", "ctx", None),
        P("dp", "ctx", None),
        P("dp", "ctx", None),
        P("dp", "ctx", None),
        P("dp", "ctx", None),
        P(),
        P(),
    )
    out_specs = (
        P("dp"),
        P("dp", "ctx", None),
        P("dp", "ctx", None),
        P("dp", "ctx", None),
        P(),
        P(),
    )
    return jax.shard_map(
        per_device, mesh=mesh, in_specs=in_specs, out_specs=out_specs, check_vma=False
    )
```

```python
import functools
import jax
import jax.numpy as jnp
from jax import lax
from jax.experimental import pallas as pl
from jax.experimental.pallas import tpu as pltpu
from jax.sharding import PartitionSpec as P

H = 32
DH = 128
BS = 64
NSEL = 32
QD = 128
KD = 1024

epsilon = 1e-06
soft_cap = 20.0

HEAD_GROUP = 4
CHUNK = 512


def key_norm(key_rows, key_gain, key_bias):
    key_float = key_rows.astype(jnp.float32)
    key_mean = jnp.mean(key_float, -1, keepdims=True)
    centered = key_float - key_mean
    key_var = jnp.mean(centered * centered, -1, keepdims=True)
    key_scale = lax.rsqrt(key_var + epsilon)
    key_hat = centered * key_scale
    normed_keys = (key_hat * key_gain + key_bias).astype(jnp.bfloat16)
    return (key_hat, key_scale, normed_keys)


def query_norm(query_rows):
    query_float = query_rows.astype(jnp.float32).reshape(query_rows.shape[0], H, DH)
    query_scale = lax.rsqrt(jnp.mean(query_float * query_float, -1, keepdims=True) + epsilon)
    query_hat = query_float * query_scale
    return (query_hat, query_scale, query_hat.astype(jnp.bfloat16))


def score_kernel(qr_ref, qt_ref, k_ref, kt_ref, w_ref, mass_ref, spos_ref, qpos_ref,
                 qg_ref, wg_ref, sgt_ref, div_ref, mix_ref, mg_ref, sp_ref):
    f32 = jnp.float32
    inv_root = DH ** (-0.5)
    rows = HEAD_GROUP * BS
    groups = H // HEAD_GROUP
    slots = kt_ref.shape[1]
    chunks = slots // CHUNK

    mix_ref[...] = jnp.zeros_like(mix_ref)

    def first_pass(g, carry):
        r0 = pl.multiple_of(g * rows, rows)
        q = qr_ref[pl.ds(r0, rows), :]
        wcol = w_ref[pl.ds(r0, rows), :]
        for c in range(chunks):
            cs = slice(c * CHUNK, (c + 1) * CHUNK)
            s = jnp.dot(q, kt_ref[:, cs], preferred_element_type=f32) * inv_root
            sp = jnp.maximum(s, 0.0) + jnp.log1p(jnp.exp(-jnp.abs(s)))
            sp_ref[pl.ds(r0, rows), cs] = sp
            ws = (wcol * sp).reshape(HEAD_GROUP, BS, CHUNK)
            mix_ref[:, cs] += jnp.sum(ws, 0)
        return carry

    lax.fori_loop(0, groups, first_pass, 0)

    mixture = mix_ref[...]
    squashed = jnp.tanh(mixture / soft_cap)
    logits = soft_cap * squashed
    is_valid = spos_ref[...] <= qpos_ref[...]
    exp_terms = jnp.where(is_valid, jnp.exp(logits - soft_cap), 0.0)
    denominator = jnp.sum(exp_terms, 1, keepdims=True)
    log_prob = logits - soft_cap - jnp.log(denominator)
    kept_mass = jnp.where(is_valid, mass_ref[...].astype(f32), 0.0)
    target = kept_mass / jnp.sum(kept_mass, 1, keepdims=True)
    div_ref[...] = jnp.sum(
        jnp.where(is_valid, target * (jnp.log(jnp.where(is_valid, target, 1.0)) - log_prob), 0.0),
        1, keepdims=True)
    mg_ref[...] = (exp_terms / denominator - target) * (1.0 - squashed * squashed)

    sgt_ref[...] = jnp.zeros_like(sgt_ref)

    def second_pass(g, carry):
        r0 = pl.multiple_of(g * rows, rows)
        q = qr_ref[pl.ds(r0, rows), :]
        qt = qt_ref[:, pl.ds(r0, rows)]
        wcol = w_ref[pl.ds(r0, rows), :]
        qg_acc = jnp.zeros((rows, DH), f32)
        wg_acc = jnp.zeros((rows, 1), f32)
        for c in range(chunks):
            cs = slice(c * CHUNK, (c + 1) * CHUNK)
            s = jnp.dot(q, kt_ref[:, cs], preferred_element_type=f32) * inv_root
            sp = sp_ref[pl.ds(r0, rows), cs]
            sig = jnp.exp(s - sp)
            mgc = mg_ref[:, cs]
            mg4 = jnp.broadcast_to(mgc[None], (HEAD_GROUP, BS, CHUNK)).reshape(rows, CHUNK)
            sg = (mg4 * wcol * sig).astype(jnp.bfloat16)
            wg_acc = wg_acc + jnp.sum(mg4 * sp, 1, keepdims=True)
            qg_acc = qg_acc + jnp.dot(sg, k_ref[cs, :], preferred_element_type=f32)
            sgt_ref[:, cs] += jnp.dot(qt, sg, preferred_element_type=f32)
        qg_ref[pl.ds(r0, rows), :] = qg_acc * inv_root
        wg_ref[pl.ds(r0, rows), :] = wg_acc
        return carry

    lax.fori_loop(0, groups, second_pass, 0)
    sgt_ref[...] = sgt_ref[...] * inv_root


def score_blocks(qr, qt, k, kt, wcol, mass, spos, qpos):
    nblk, nrows, _ = qr.shape
    slots = k.shape[1]
    f32 = jnp.float32

    def blk(*shape):
        return pl.BlockSpec((None,) + shape, lambda b: (b,) + (0,) * len(shape))

    flops = nblk * (4 * 2 * nrows * slots * DH)
    return pl.pallas_call(
        score_kernel,
        grid=(nblk,),
        in_specs=[
            blk(nrows, DH), blk(DH, nrows), blk(slots, DH), blk(DH, slots),
            blk(nrows, 1), blk(BS, slots), blk(1, slots), blk(BS, 1),
        ],
        out_specs=[blk(nrows, DH), blk(nrows, 1), blk(DH, slots), blk(BS, 1)],
        out_shape=[
            jax.ShapeDtypeStruct((nblk, nrows, DH), f32),
            jax.ShapeDtypeStruct((nblk, nrows, 1), f32),
            jax.ShapeDtypeStruct((nblk, DH, slots), f32),
            jax.ShapeDtypeStruct((nblk, BS, 1), f32),
        ],
        scratch_shapes=[
            pltpu.VMEM((BS, slots), f32), pltpu.VMEM((BS, slots), f32), pltpu.VMEM((nrows, slots), f32)
        ],
        compiler_params=pltpu.CompilerParams(
            dimension_semantics=("arbitrary",), vmem_limit_bytes=60 * 1024 * 1024
        ),
        cost_estimate=pl.CostEstimate(
            flops=flops, transcendentals=nblk * nrows * slots * 3,
            bytes_accessed=nblk * (nrows * DH * 4 + slots * DH * 4 + nrows * DH * 4 + DH * slots * 4)),
    )(qr, qt, k, kt, wcol, mass, spos, qpos)


def butterfly_sum(value, axes):
    count = 1
    for axis in axes:
        count *= lax.axis_size(axis)
    if count & (count - 1):
        return lax.psum(value, axes)
    stride = 1
    while stride < count:
        pairs = [(i, i ^ stride) for i in range(count)]
        value = value + lax.ppermute(value, axes, pairs)
        stride *= 2
    return value


def per_device(queries, keys, head_weights, block_ids, target_mass, key_gain, key_bias):
    ctx_count = lax.axis_size("ctx")
    ctx_index = lax.axis_index("ctx")
    dp_count = lax.axis_size("dp")
    dp_index = lax.axis_index("dp")
    key_count = KD // BS
    query_count = QD // BS
    capacity = 2 * query_count
    request_count = query_count * NSEL
    slot_count = NSEL * BS
    key_hat, key_scale, normed_keys = key_norm(keys[0], key_gain, key_bias)
    listed_ids = block_ids[0].reshape(request_count)
    is_listed = listed_ids >= 0
    block_safe = jnp.maximum(listed_ids, 0)
    owner_index = block_safe // key_count
    local_block = block_safe % key_count
    owner_hits = (
        (owner_index[:, None] == jnp.arange(ctx_count, dtype=jnp.int32)[None, :])
        & is_listed[:, None]
    ).astype(jnp.int32)
    earlier = jnp.cumsum(owner_hits, 0) - owner_hits
    rank_slot = jnp.sum(earlier * owner_hits, 1)
    target_slot = jnp.where(is_listed, owner_index * capacity + rank_slot, 0)
    placement = (
        target_slot[:, None] == jnp.arange(ctx_count * capacity, dtype=jnp.int32)[None, :]
    ) & is_listed[:, None]
    request_table = jnp.sum(jnp.where(placement, local_block[:, None] + 1, 0), 0) - 1
    request_table = request_table.reshape(ctx_count, capacity)
    asked_back = lax.all_to_all(request_table, "ctx", split_axis=0, concat_axis=0, tiled=True)
    sent_keys = normed_keys.reshape(key_count, BS, DH)[jnp.clip(asked_back, 0, key_count - 1)]
    arrived_keys = lax.all_to_all(sent_keys, "ctx", split_axis=0, concat_axis=0, tiled=True)
    picked = arrived_keys.reshape(ctx_count * capacity, BS, DH)[target_slot]
    slot_keys = picked.reshape(query_count, slot_count, DH)
    slot_positions = (block_safe[:, None] * BS + jnp.arange(BS, dtype=jnp.int32)[None, :]).reshape(
        query_count, slot_count
    )
    slot_lives = jnp.repeat(is_listed, BS).reshape(query_count, slot_count)
    never = jnp.iinfo(jnp.int32).max
    slot_limit = jnp.where(slot_lives, slot_positions, never).reshape(query_count, 1, slot_count)
    query_hat, query_scale, normed_queries = query_norm(queries[0])
    first_pos = ctx_index * KD + KD - QD
    query_pos = (first_pos + jnp.arange(QD, dtype=jnp.int32)).reshape(query_count, BS, 1)

    head_rows = (
        normed_queries.reshape(query_count, BS, H, DH).transpose(0, 2, 1, 3).reshape(query_count, H * BS, DH)
    )
    head_cols = head_rows.transpose(0, 2, 1)
    key_cols = slot_keys.transpose(0, 2, 1)
    weight_col = (
        head_weights[0].astype(jnp.float32).reshape(query_count, BS, H).transpose(0, 2, 1)
        .reshape(query_count, H * BS, 1)
    )
    mass_rows = target_mass[0].reshape(query_count, BS, slot_count)
    qg_rows, wg_rows, slot_grad_t, div_rows = score_blocks(
        head_rows, head_cols, slot_keys, key_cols, weight_col, mass_rows, slot_limit, query_pos
    )
    divergence_total = jnp.sum(div_rows)
    query_grads = qg_rows.reshape(query_count, H, BS, DH).transpose(0, 2, 1, 3).reshape(QD, H, DH)
    weight_grads = wg_rows.reshape(query_count, H, BS).transpose(0, 2, 1).reshape(QD, H)
    grad_slots = slot_grad_t.transpose(0, 2, 1)

    grad_query_rows = (
        query_grads - query_hat * jnp.mean(query_grads * query_hat, -1, keepdims=True)
    ) * query_scale
    slot_flat = grad_slots.reshape(request_count, BS * DH)
    outbound = jnp.dot(placement.T.astype(jnp.float32), slot_flat, precision=lax.Precision.HIGHEST)
    returned = lax.all_to_all(
        outbound.reshape(ctx_count, capacity, BS * DH), "ctx", split_axis=0, concat_axis=0, tiled=True
    )
    own_rows = (
        asked_back.reshape(ctx_count * capacity)[None, :]
        == jnp.arange(key_count, dtype=jnp.int32)[:, None]
    ).astype(jnp.float32)
    key_grad = jnp.dot(
        own_rows, returned.reshape(ctx_count * capacity, BS * DH), precision=lax.Precision.HIGHEST
    ).reshape(KD, DH)
    gain_part = jnp.sum(key_grad * key_hat, 0)
    bias_part = jnp.sum(key_grad, 0)
    scaled_grad = key_grad * key_gain
    grad_key_rows = (
        scaled_grad
        - jnp.mean(scaled_grad, -1, keepdims=True)
        - key_hat * jnp.mean(scaled_grad * key_hat, -1, keepdims=True)
    ) * key_scale
    loss_slots = jnp.where(jnp.arange(dp_count) == dp_index, divergence_total, 0.0)
    packed = butterfly_sum(jnp.concatenate([gain_part, bias_part, loss_slots]), ("dp", "ctx"))
    grad_gain = packed[:DH]
    grad_bias = packed[DH:2 * DH]
    loss_total = lax.dynamic_index_in_dim(packed, 2 * DH + dp_index, 0, keepdims=False)
    seq_loss = jnp.reshape(loss_total / (QD * ctx_count), (1,))
    return (
        seq_loss,
        grad_query_rows.reshape(1, QD, H * DH),
        weight_grads.reshape(1, QD, H),
        grad_key_rows.reshape(1, KD, DH),
        grad_gain,
        grad_bias,
    )


def solution(mesh):
    in_specs = (
        P("dp", "ctx", None),
        P("dp", "ctx", None),
        P("dp", "ctx", None),
        P("dp", "ctx", None),
        P("dp", "ctx", None),
        P(),
        P(),
    )
    out_specs = (
        P("dp"),
        P("dp", "ctx", None),
        P("dp", "ctx", None),
        P("dp", "ctx", None),
        P(),
        P(),
    )
    return jax.shard_map(
        per_device, mesh=mesh, in_specs=in_specs, out_specs=out_specs, check_vma=False
    )
```

```python
import functools
import jax
import jax.numpy as jnp
from jax import lax
from jax.experimental import pallas as pl
from jax.experimental.pallas import tpu as pltpu
from jax.sharding import PartitionSpec as P

H = 32
DH = 128
BS = 64
NSEL = 32
QD = 128
KD = 1024

epsilon = 1e-06
soft_cap = 20.0

HEAD_GROUP = 4
CHUNK = 512


def key_norm(key_rows, key_gain, key_bias):
    key_float = key_rows.astype(jnp.float32)
    key_mean = jnp.mean(key_float, -1, keepdims=True)
    centered = key_float - key_mean
    key_var = jnp.mean(centered * centered, -1, keepdims=True)
    key_scale = lax.rsqrt(key_var + epsilon)
    key_hat = centered * key_scale
    normed_keys = (key_hat * key_gain + key_bias).astype(jnp.bfloat16)
    return (key_hat, key_scale, normed_keys)


def query_norm(query_rows):
    query_float = query_rows.astype(jnp.float32).reshape(query_rows.shape[0], H, DH)
    query_scale = lax.rsqrt(jnp.mean(query_float * query_float, -1, keepdims=True) + epsilon)
    query_hat = query_float * query_scale
    return (query_hat, query_scale, query_hat.astype(jnp.bfloat16))


def score_kernel(q_ref, k_ref, kt_ref, w_ref, mass_ref, spos_ref, qpos_ref,
                 gq_ref, wg_ref, sgt_ref, div_ref, qr_ref, qt_ref, mix_ref, mg_ref, sp_ref):
    f32 = jnp.float32
    inv_root = DH ** (-0.5)
    rows = HEAD_GROUP * BS
    groups = H // HEAD_GROUP
    slots = kt_ref.shape[1]
    chunks = slots // CHUNK

    for h in range(H):
        x = q_ref[:, h * DH:(h + 1) * DH].astype(f32)
        scale = lax.rsqrt(jnp.mean(x * x, -1, keepdims=True) + epsilon)
        nq = (x * scale).astype(jnp.bfloat16)
        qr_ref[h * BS:(h + 1) * BS, :] = nq
        qt_ref[:, h * BS:(h + 1) * BS] = nq.astype(f32).T.astype(jnp.bfloat16)

    head_ids = lax.broadcasted_iota(jnp.int32, (H, HEAD_GROUP), 0)
    pick_ids = lax.broadcasted_iota(jnp.int32, (H, HEAD_GROUP), 1)
    lane_heads = lax.broadcasted_iota(jnp.int32, (1, H), 1)

    def group_weights(g):
        onehot = (head_ids == g * HEAD_GROUP + pick_ids).astype(jnp.bfloat16)
        w4 = jnp.dot(w_ref[...], onehot, preferred_element_type=f32)
        return jnp.concatenate([w4[:, hh:hh + 1] for hh in range(HEAD_GROUP)], 0)

    mix_ref[...] = jnp.zeros_like(mix_ref)

    def first_pass(g, carry):
        r0 = pl.multiple_of(g * rows, rows)
        q = qr_ref[pl.ds(r0, rows), :]
        wcol = group_weights(g)
        for c in range(chunks):
            cs = slice(c * CHUNK, (c + 1) * CHUNK)
            s = jnp.dot(q, kt_ref[:, cs], preferred_element_type=f32) * inv_root
            sp = jnp.maximum(s, 0.0) + jnp.log1p(jnp.exp(-jnp.abs(s)))
            sp_ref[pl.ds(r0, rows), cs] = sp
            ws = (wcol * sp).reshape(HEAD_GROUP, BS, CHUNK)
            mix_ref[:, cs] += jnp.sum(ws, 0)
        return carry

    lax.fori_loop(0, groups, first_pass, 0)

    mixture = mix_ref[...]
    squashed = jnp.tanh(mixture / soft_cap)
    logits = soft_cap * squashed
    is_valid = spos_ref[...] <= qpos_ref[...]
    exp_terms = jnp.where(is_valid, jnp.exp(logits - soft_cap), 0.0)
    denominator = jnp.sum(exp_terms, 1, keepdims=True)
    log_prob = logits - soft_cap - jnp.log(denominator)
    kept_mass = jnp.where(is_valid, mass_ref[...].astype(f32), 0.0)
    target = kept_mass / jnp.sum(kept_mass, 1, keepdims=True)
    div_ref[...] = jnp.sum(
        jnp.where(is_valid, target * (jnp.log(jnp.where(is_valid, target, 1.0)) - log_prob), 0.0),
        1, keepdims=True)
    mg_ref[...] = (exp_terms / denominator - target) * (1.0 - squashed * squashed)

    sgt_ref[...] = jnp.zeros_like(sgt_ref)
    wg_ref[...] = jnp.zeros_like(wg_ref)

    def second_pass(g, carry):
        r0 = pl.multiple_of(g * rows, rows)
        q = qr_ref[pl.ds(r0, rows), :]
        qt = qt_ref[:, pl.ds(r0, rows)]
        wcol = group_weights(g)
        qg_acc = jnp.zeros((rows, DH), f32)
        wg_acc = jnp.zeros((rows, 1), f32)
        for c in range(chunks):
            cs = slice(c * CHUNK, (c + 1) * CHUNK)
            s = jnp.dot(q, kt_ref[:, cs], preferred_element_type=f32) * inv_root
            sp = sp_ref[pl.ds(r0, rows), cs]
            sig = jnp.exp(s - sp)
            mgc = mg_ref[:, cs]
            mg4 = jnp.broadcast_to(mgc[None], (HEAD_GROUP, BS, CHUNK)).reshape(rows, CHUNK)
            sg = (mg4 * wcol * sig).astype(jnp.bfloat16)
            wg_acc = wg_acc + jnp.sum(mg4 * sp, 1, keepdims=True)
            qg_acc = qg_acc + jnp.dot(sg, k_ref[cs, :], preferred_element_type=f32)
            sgt_ref[:, cs] += jnp.dot(qt, sg, preferred_element_type=f32)
        qg_acc = qg_acc * inv_root
        wg_sum = wg_ref[...]
        for hh in range(HEAD_GROUP):
            h = g * HEAD_GROUP + hh
            wg_sum = wg_sum + jnp.where(lane_heads == h, wg_acc[hh * BS:(hh + 1) * BS], 0.0)
            lanes = pl.ds(pl.multiple_of(h * DH, DH), DH)
            x = q_ref[:, lanes].astype(f32)
            scale = lax.rsqrt(jnp.mean(x * x, -1, keepdims=True) + epsilon)
            query_hat = x * scale
            qg = qg_acc[hh * BS:(hh + 1) * BS]
            gq_ref[:, lanes] = (qg - query_hat * jnp.mean(qg * query_hat, -1, keepdims=True)) * scale
        wg_ref[...] = wg_sum
        return carry

    lax.fori_loop(0, groups, second_pass, 0)
    sgt_ref[...] = sgt_ref[...] * inv_root


def score_blocks(q, k, kt, w, mass, spos, qpos):
    nblk = q.shape[0]
    slots = k.shape[1]
    nrows = H * BS
    f32 = jnp.float32

    def blk(*shape):
        return pl.BlockSpec((None,) + shape, lambda b: (b,) + (0,) * len(shape))

    flops = nblk * (4 * 2 * nrows * slots * DH)
    return pl.pallas_call(
        score_kernel,
        grid=(nblk,),
        in_specs=[
            blk(BS, H * DH), blk(slots, DH), blk(DH, slots),
            blk(BS, H), blk(BS, slots), blk(1, slots), blk(BS, 1),
        ],
        out_specs=[blk(BS, H * DH), blk(BS, H), blk(DH, slots), blk(BS, 1)],
        out_shape=[
            jax.ShapeDtypeStruct((nblk, BS, H * DH), f32),
            jax.ShapeDtypeStruct((nblk, BS, H), f32),
            jax.ShapeDtypeStruct((nblk, DH, slots), f32),
            jax.ShapeDtypeStruct((nblk, BS, 1), f32),
        ],
        scratch_shapes=[
            pltpu.VMEM((nrows, DH), jnp.bfloat16), pltpu.VMEM((DH, nrows), jnp.bfloat16),
            pltpu.VMEM((BS, slots), f32), pltpu.VMEM((BS, slots), f32), pltpu.VMEM((nrows, slots), f32)
        ],
        compiler_params=pltpu.CompilerParams(
            dimension_semantics=("arbitrary",), vmem_limit_bytes=60 * 1024 * 1024
        ),
        cost_estimate=pl.CostEstimate(
            flops=flops, transcendentals=nblk * nrows * slots * 3,
            bytes_accessed=nblk * (BS * H * DH * 6 + slots * DH * 4 + DH * slots * 4)),
    )(q, k, kt, w, mass, spos, qpos)


def butterfly_sum(value, axes):
    count = 1
    for axis in axes:
        count *= lax.axis_size(axis)
    if count & (count - 1):
        return lax.psum(value, axes)
    stride = 1
    while stride < count:
        pairs = [(i, i ^ stride) for i in range(count)]
        value = value + lax.ppermute(value, axes, pairs)
        stride *= 2
    return value


def per_device(queries, keys, head_weights, block_ids, target_mass, key_gain, key_bias):
    ctx_count = lax.axis_size("ctx")
    ctx_index = lax.axis_index("ctx")
    dp_count = lax.axis_size("dp")
    dp_index = lax.axis_index("dp")
    key_count = KD // BS
    query_count = QD // BS
    capacity = 2 * query_count
    request_count = query_count * NSEL
    slot_count = NSEL * BS
    key_hat, key_scale, normed_keys = key_norm(keys[0], key_gain, key_bias)
    listed_ids = block_ids[0].reshape(request_count)
    is_listed = listed_ids >= 0
    block_safe = jnp.maximum(listed_ids, 0)
    owner_index = block_safe // key_count
    local_block = block_safe % key_count
    owner_hits = (
        (owner_index[:, None] == jnp.arange(ctx_count, dtype=jnp.int32)[None, :])
        & is_listed[:, None]
    ).astype(jnp.int32)
    earlier = jnp.cumsum(owner_hits, 0) - owner_hits
    rank_slot = jnp.sum(earlier * owner_hits, 1)
    target_slot = jnp.where(is_listed, owner_index * capacity + rank_slot, 0)
    placement = (
        target_slot[:, None] == jnp.arange(ctx_count * capacity, dtype=jnp.int32)[None, :]
    ) & is_listed[:, None]
    request_table = jnp.sum(jnp.where(placement, local_block[:, None] + 1, 0), 0) - 1
    request_table = request_table.reshape(ctx_count, capacity)
    asked_back = lax.all_to_all(request_table, "ctx", split_axis=0, concat_axis=0, tiled=True)
    sent_keys = normed_keys.reshape(key_count, BS, DH)[jnp.clip(asked_back, 0, key_count - 1)]
    arrived_keys = lax.all_to_all(sent_keys, "ctx", split_axis=0, concat_axis=0, tiled=True)
    picked = arrived_keys.reshape(ctx_count * capacity, BS, DH)[target_slot]
    slot_keys = picked.reshape(query_count, slot_count, DH)
    slot_positions = (block_safe[:, None] * BS + jnp.arange(BS, dtype=jnp.int32)[None, :]).reshape(
        query_count, slot_count
    )
    slot_lives = jnp.repeat(is_listed, BS).reshape(query_count, slot_count)
    never = jnp.iinfo(jnp.int32).max
    slot_limit = jnp.where(slot_lives, slot_positions, never).reshape(query_count, 1, slot_count)
    first_pos = ctx_index * KD + KD - QD
    query_pos = (first_pos + jnp.arange(QD, dtype=jnp.int32)).reshape(query_count, BS, 1)

    key_cols = slot_keys.transpose(0, 2, 1)
    mass_rows = target_mass[0].reshape(query_count, BS, slot_count)
    grad_query_rows, weight_grads, slot_grad_t, div_rows = score_blocks(
        queries[0].reshape(query_count, BS, H * DH), slot_keys, key_cols,
        head_weights[0].reshape(query_count, BS, H), mass_rows, slot_limit, query_pos
    )
    divergence_total = jnp.sum(div_rows)
    grad_slots = slot_grad_t.transpose(0, 2, 1)
    slot_flat = grad_slots.reshape(request_count, BS * DH)
    outbound = jnp.dot(placement.T.astype(jnp.float32), slot_flat, precision=lax.Precision.HIGHEST)
    returned = lax.all_to_all(
        outbound.reshape(ctx_count, capacity, BS * DH), "ctx", split_axis=0, concat_axis=0, tiled=True
    )
    own_rows = (
        asked_back.reshape(ctx_count * capacity)[None, :]
        == jnp.arange(key_count, dtype=jnp.int32)[:, None]
    ).astype(jnp.float32)
    key_grad = jnp.dot(
        own_rows, returned.reshape(ctx_count * capacity, BS * DH), precision=lax.Precision.HIGHEST
    ).reshape(KD, DH)
    gain_part = jnp.sum(key_grad * key_hat, 0)
    bias_part = jnp.sum(key_grad, 0)
    scaled_grad = key_grad * key_gain
    grad_key_rows = (
        scaled_grad
        - jnp.mean(scaled_grad, -1, keepdims=True)
        - key_hat * jnp.mean(scaled_grad * key_hat, -1, keepdims=True)
    ) * key_scale
    loss_slots = jnp.where(jnp.arange(dp_count) == dp_index, divergence_total, 0.0)
    packed = butterfly_sum(jnp.concatenate([gain_part, bias_part, loss_slots]), ("dp", "ctx"))
    grad_gain = packed[:DH]
    grad_bias = packed[DH:2 * DH]
    loss_total = lax.dynamic_index_in_dim(packed, 2 * DH + dp_index, 0, keepdims=False)
    seq_loss = jnp.reshape(loss_total / (QD * ctx_count), (1,))
    return (
        seq_loss,
        grad_query_rows.reshape(1, QD, H * DH),
        weight_grads.reshape(1, QD, H),
        grad_key_rows.reshape(1, KD, DH),
        grad_gain,
        grad_bias,
    )


def solution(mesh):
    in_specs = (
        P("dp", "ctx", None),
        P("dp", "ctx", None),
        P("dp", "ctx", None),
        P("dp", "ctx", None),
        P("dp", "ctx", None),
        P(),
        P(),
    )
    out_specs = (
        P("dp"),
        P("dp", "ctx", None),
        P("dp", "ctx", None),
        P("dp", "ctx", None),
        P(),
        P(),
    )
    return jax.shard_map(
        per_device, mesh=mesh, in_specs=in_specs, out_specs=out_specs, check_vma=False
    )
```

```python
import functools
import jax
import jax.numpy as jnp
from jax import lax
from jax.experimental import pallas as pl
from jax.experimental.pallas import tpu as pltpu
from jax.sharding import PartitionSpec as P

H = 32
DH = 128
BS = 64
NSEL = 32
QD = 128
KD = 1024

epsilon = 1e-06
soft_cap = 20.0

HEAD_GROUP = 4
CHUNK = 512


def key_norm(key_rows, key_gain, key_bias):
    key_float = key_rows.astype(jnp.float32)
    key_mean = jnp.mean(key_float, -1, keepdims=True)
    centered = key_float - key_mean
    key_var = jnp.mean(centered * centered, -1, keepdims=True)
    key_scale = lax.rsqrt(key_var + epsilon)
    key_hat = centered * key_scale
    normed_keys = (key_hat * key_gain + key_bias).astype(jnp.bfloat16)
    return (key_hat, key_scale, normed_keys)


def query_norm(query_rows):
    query_float = query_rows.astype(jnp.float32).reshape(query_rows.shape[0], H, DH)
    query_scale = lax.rsqrt(jnp.mean(query_float * query_float, -1, keepdims=True) + epsilon)
    query_hat = query_float * query_scale
    return (query_hat, query_scale, query_hat.astype(jnp.bfloat16))


def score_kernel(q_ref, k_ref, kt_ref, w_ref, mass_ref, spos_ref, qpos_ref,
                 gq_ref, wg_ref, sgt_ref, div_ref, qr_ref, qt_ref, mix_ref, mg_ref, sp_ref):
    f32 = jnp.float32
    inv_root = DH ** (-0.5)
    rows = HEAD_GROUP * BS
    groups = H // HEAD_GROUP
    slots = kt_ref.shape[1]
    chunks = slots // CHUNK

    for h in range(H):
        x = q_ref[:, h * DH:(h + 1) * DH].astype(f32)
        scale = lax.rsqrt(jnp.mean(x * x, -1, keepdims=True) + epsilon)
        nq = (x * scale).astype(jnp.bfloat16)
        qr_ref[h * BS:(h + 1) * BS, :] = nq
        qt_ref[:, h * BS:(h + 1) * BS] = nq.astype(f32).T.astype(jnp.bfloat16)

    head_ids = lax.broadcasted_iota(jnp.int32, (H, HEAD_GROUP), 0)
    pick_ids = lax.broadcasted_iota(jnp.int32, (H, HEAD_GROUP), 1)
    lane_heads = lax.broadcasted_iota(jnp.int32, (1, H), 1)

    def group_weights(g):
        onehot = (head_ids == g * HEAD_GROUP + pick_ids).astype(jnp.bfloat16)
        w4 = jnp.dot(w_ref[...], onehot, preferred_element_type=f32)
        return jnp.concatenate([w4[:, hh:hh + 1] for hh in range(HEAD_GROUP)], 0)

    mix_ref[...] = jnp.zeros_like(mix_ref)
    neg_log2_root = -inv_root * 1.4426950408889634

    def first_pass(g, carry):
        r0 = pl.multiple_of(g * rows, rows)
        q = qr_ref[pl.ds(r0, rows), :]
        wcol = group_weights(g)
        for c in range(chunks):
            cs = slice(c * CHUNK, (c + 1) * CHUNK)
            raw = jnp.dot(q, kt_ref[:, cs], preferred_element_type=f32)
            tail = jnp.exp2(jnp.abs(raw) * neg_log2_root)
            sp = jnp.maximum(raw * inv_root, 0.0) + jnp.log(1.0 + tail)
            sp_ref[pl.ds(r0, rows), cs] = sp
            ws = (wcol * sp).reshape(HEAD_GROUP, BS, CHUNK)
            mix_ref[:, cs] += jnp.sum(ws, 0)
        return carry

    lax.fori_loop(0, groups, first_pass, 0)

    mixture = mix_ref[...]
    squashed = jnp.tanh(mixture / soft_cap)
    logits = soft_cap * squashed
    is_valid = spos_ref[...] <= qpos_ref[...]
    exp_terms = jnp.where(is_valid, jnp.exp(logits - soft_cap), 0.0)
    denominator = jnp.sum(exp_terms, 1, keepdims=True)
    log_prob = logits - soft_cap - jnp.log(denominator)
    kept_mass = jnp.where(is_valid, mass_ref[...].astype(f32), 0.0)
    target = kept_mass / jnp.sum(kept_mass, 1, keepdims=True)
    div_ref[...] = jnp.sum(
        jnp.where(is_valid, target * (jnp.log(jnp.where(is_valid, target, 1.0)) - log_prob), 0.0),
        1, keepdims=True)
    mg_ref[...] = (exp_terms / denominator - target) * (1.0 - squashed * squashed)

    sgt_ref[...] = jnp.zeros_like(sgt_ref)
    wg_ref[...] = jnp.zeros_like(wg_ref)

    def second_pass(g, carry):
        r0 = pl.multiple_of(g * rows, rows)
        q = qr_ref[pl.ds(r0, rows), :]
        qt = qt_ref[:, pl.ds(r0, rows)]
        wcol = group_weights(g)
        qg_acc = jnp.zeros((rows, DH), f32)
        wg_acc = jnp.zeros((rows, 1), f32)
        for c in range(chunks):
            cs = slice(c * CHUNK, (c + 1) * CHUNK)
            s = jnp.dot(q, kt_ref[:, cs], preferred_element_type=f32) * inv_root
            sp = sp_ref[pl.ds(r0, rows), cs]
            sig = jnp.exp(s - sp)
            mgc = mg_ref[:, cs]
            mg4 = jnp.broadcast_to(mgc[None], (HEAD_GROUP, BS, CHUNK)).reshape(rows, CHUNK)
            sg = (mg4 * wcol * sig).astype(jnp.bfloat16)
            wg_acc = wg_acc + jnp.sum(mg4 * sp, 1, keepdims=True)
            qg_acc = qg_acc + jnp.dot(sg, k_ref[cs, :], preferred_element_type=f32)
            sgt_ref[:, cs] += jnp.dot(qt, sg, preferred_element_type=f32)
        qg_acc = qg_acc * inv_root
        wg_sum = wg_ref[...]
        for hh in range(HEAD_GROUP):
            h = g * HEAD_GROUP + hh
            wg_sum = wg_sum + jnp.where(lane_heads == h, wg_acc[hh * BS:(hh + 1) * BS], 0.0)
            lanes = pl.ds(pl.multiple_of(h * DH, DH), DH)
            x = q_ref[:, lanes].astype(f32)
            scale = lax.rsqrt(jnp.mean(x * x, -1, keepdims=True) + epsilon)
            query_hat = x * scale
            qg = qg_acc[hh * BS:(hh + 1) * BS]
            gq_ref[:, lanes] = (qg - query_hat * jnp.mean(qg * query_hat, -1, keepdims=True)) * scale
        wg_ref[...] = wg_sum
        return carry

    lax.fori_loop(0, groups, second_pass, 0)
    sgt_ref[...] = sgt_ref[...] * inv_root


def score_blocks(q, k, kt, w, mass, spos, qpos):
    nblk = q.shape[0]
    slots = k.shape[1]
    nrows = H * BS
    f32 = jnp.float32

    def blk(*shape):
        return pl.BlockSpec((None,) + shape, lambda b: (b,) + (0,) * len(shape))

    flops = nblk * (4 * 2 * nrows * slots * DH)
    return pl.pallas_call(
        score_kernel,
        grid=(nblk,),
        in_specs=[
            blk(BS, H * DH), blk(slots, DH), blk(DH, slots),
            blk(BS, H), blk(BS, slots), blk(1, slots), blk(BS, 1),
        ],
        out_specs=[blk(BS, H * DH), blk(BS, H), blk(DH, slots), blk(BS, 1)],
        out_shape=[
            jax.ShapeDtypeStruct((nblk, BS, H * DH), f32),
            jax.ShapeDtypeStruct((nblk, BS, H), f32),
            jax.ShapeDtypeStruct((nblk, DH, slots), f32),
            jax.ShapeDtypeStruct((nblk, BS, 1), f32),
        ],
        scratch_shapes=[
            pltpu.VMEM((nrows, DH), jnp.bfloat16), pltpu.VMEM((DH, nrows), jnp.bfloat16),
            pltpu.VMEM((BS, slots), f32), pltpu.VMEM((BS, slots), f32), pltpu.VMEM((nrows, slots), f32)
        ],
        compiler_params=pltpu.CompilerParams(
            dimension_semantics=("arbitrary",), vmem_limit_bytes=60 * 1024 * 1024
        ),
        cost_estimate=pl.CostEstimate(
            flops=flops, transcendentals=nblk * nrows * slots * 3,
            bytes_accessed=nblk * (BS * H * DH * 6 + slots * DH * 4 + DH * slots * 4)),
    )(q, k, kt, w, mass, spos, qpos)


def butterfly_sum(value, axes):
    count = 1
    for axis in axes:
        count *= lax.axis_size(axis)
    if count & (count - 1):
        return lax.psum(value, axes)
    stride = 1
    while stride < count:
        pairs = [(i, i ^ stride) for i in range(count)]
        value = value + lax.ppermute(value, axes, pairs)
        stride *= 2
    return value


def per_device(queries, keys, head_weights, block_ids, target_mass, key_gain, key_bias):
    ctx_count = lax.axis_size("ctx")
    ctx_index = lax.axis_index("ctx")
    dp_count = lax.axis_size("dp")
    dp_index = lax.axis_index("dp")
    key_count = KD // BS
    query_count = QD // BS
    capacity = 2 * query_count
    request_count = query_count * NSEL
    slot_count = NSEL * BS
    key_hat, key_scale, normed_keys = key_norm(keys[0], key_gain, key_bias)
    listed_ids = block_ids[0].reshape(request_count)
    is_listed = listed_ids >= 0
    block_safe = jnp.maximum(listed_ids, 0)
    owner_index = block_safe // key_count
    local_block = block_safe % key_count
    owner_hits = (
        (owner_index[:, None] == jnp.arange(ctx_count, dtype=jnp.int32)[None, :])
        & is_listed[:, None]
    ).astype(jnp.int32)
    earlier = jnp.cumsum(owner_hits, 0) - owner_hits
    rank_slot = jnp.sum(earlier * owner_hits, 1)
    target_slot = jnp.where(is_listed, owner_index * capacity + rank_slot, 0)
    placement = (
        target_slot[:, None] == jnp.arange(ctx_count * capacity, dtype=jnp.int32)[None, :]
    ) & is_listed[:, None]
    request_table = jnp.sum(jnp.where(placement, local_block[:, None] + 1, 0), 0) - 1
    request_table = request_table.reshape(ctx_count, capacity)
    asked_back = lax.all_to_all(request_table, "ctx", split_axis=0, concat_axis=0, tiled=True)
    sent_keys = normed_keys.reshape(key_count, BS, DH)[jnp.clip(asked_back, 0, key_count - 1)]
    arrived_keys = lax.all_to_all(sent_keys, "ctx", split_axis=0, concat_axis=0, tiled=True)
    picked = arrived_keys.reshape(ctx_count * capacity, BS, DH)[target_slot]
    slot_keys = picked.reshape(query_count, slot_count, DH)
    slot_positions = (block_safe[:, None] * BS + jnp.arange(BS, dtype=jnp.int32)[None, :]).reshape(
        query_count, slot_count
    )
    slot_lives = jnp.repeat(is_listed, BS).reshape(query_count, slot_count)
    never = jnp.iinfo(jnp.int32).max
    slot_limit = jnp.where(slot_lives, slot_positions, never).reshape(query_count, 1, slot_count)
    first_pos = ctx_index * KD + KD - QD
    query_pos = (first_pos + jnp.arange(QD, dtype=jnp.int32)).reshape(query_count, BS, 1)

    key_cols = slot_keys.transpose(0, 2, 1)
    mass_rows = target_mass[0].reshape(query_count, BS, slot_count)
    grad_query_rows, weight_grads, slot_grad_t, div_rows = score_blocks(
        queries[0].reshape(query_count, BS, H * DH), slot_keys, key_cols,
        head_weights[0].reshape(query_count, BS, H), mass_rows, slot_limit, query_pos
    )
    divergence_total = jnp.sum(div_rows)
    grad_slots = slot_grad_t.transpose(0, 2, 1)
    slot_flat = grad_slots.reshape(request_count, BS * DH)
    outbound = jnp.dot(placement.T.astype(jnp.float32), slot_flat, precision=lax.Precision.HIGHEST)
    returned = lax.all_to_all(
        outbound.reshape(ctx_count, capacity, BS * DH), "ctx", split_axis=0, concat_axis=0, tiled=True
    )
    own_rows = (
        asked_back.reshape(ctx_count * capacity)[None, :]
        == jnp.arange(key_count, dtype=jnp.int32)[:, None]
    ).astype(jnp.float32)
    key_grad = jnp.dot(
        own_rows, returned.reshape(ctx_count * capacity, BS * DH), precision=lax.Precision.HIGHEST
    ).reshape(KD, DH)
    gain_part = jnp.sum(key_grad * key_hat, 0)
    bias_part = jnp.sum(key_grad, 0)
    scaled_grad = key_grad * key_gain
    grad_key_rows = (
        scaled_grad
        - jnp.mean(scaled_grad, -1, keepdims=True)
        - key_hat * jnp.mean(scaled_grad * key_hat, -1, keepdims=True)
    ) * key_scale
    loss_slots = jnp.where(jnp.arange(dp_count) == dp_index, divergence_total, 0.0)
    packed = butterfly_sum(jnp.concatenate([gain_part, bias_part, loss_slots]), ("dp", "ctx"))
    grad_gain = packed[:DH]
    grad_bias = packed[DH:2 * DH]
    loss_total = lax.dynamic_index_in_dim(packed, 2 * DH + dp_index, 0, keepdims=False)
    seq_loss = jnp.reshape(loss_total / (QD * ctx_count), (1,))
    return (
        seq_loss,
        grad_query_rows.reshape(1, QD, H * DH),
        weight_grads.reshape(1, QD, H),
        grad_key_rows.reshape(1, KD, DH),
        grad_gain,
        grad_bias,
    )


def solution(mesh):
    in_specs = (
        P("dp", "ctx", None),
        P("dp", "ctx", None),
        P("dp", "ctx", None),
        P("dp", "ctx", None),
        P("dp", "ctx", None),
        P(),
        P(),
    )
    out_specs = (
        P("dp"),
        P("dp", "ctx", None),
        P("dp", "ctx", None),
        P("dp", "ctx", None),
        P(),
        P(),
    )
    return jax.shard_map(
        per_device, mesh=mesh, in_specs=in_specs, out_specs=out_specs, check_vma=False
    )
```

```python
import functools
import jax
import jax.numpy as jnp
from jax import lax
from jax.experimental import pallas as pl
from jax.experimental.pallas import tpu as pltpu
from jax.sharding import PartitionSpec as P

H = 32
DH = 128
BS = 64
NSEL = 32
QD = 128
KD = 1024

epsilon = 1e-06
soft_cap = 20.0

HEAD_GROUP = 32
CHUNK = 256


def key_norm(key_rows, key_gain, key_bias):
    key_float = key_rows.astype(jnp.float32)
    key_mean = jnp.mean(key_float, -1, keepdims=True)
    centered = key_float - key_mean
    key_var = jnp.mean(centered * centered, -1, keepdims=True)
    key_scale = lax.rsqrt(key_var + epsilon)
    key_hat = centered * key_scale
    normed_keys = (key_hat * key_gain + key_bias).astype(jnp.bfloat16)
    return (key_hat, key_scale, normed_keys)


def query_norm(query_rows):
    query_float = query_rows.astype(jnp.float32).reshape(query_rows.shape[0], H, DH)
    query_scale = lax.rsqrt(jnp.mean(query_float * query_float, -1, keepdims=True) + epsilon)
    query_hat = query_float * query_scale
    return (query_hat, query_scale, query_hat.astype(jnp.bfloat16))


def score_kernel(q_ref, k_ref, kt_ref, w_ref, mass_ref, spos_ref, qpos_ref,
                 gq_ref, wg_ref, sgt_ref, div_ref, qr_ref, qt_ref, mix_ref, mg_ref, sp_ref):
    f32 = jnp.float32
    inv_root = DH ** (-0.5)
    rows = HEAD_GROUP * BS
    groups = H // HEAD_GROUP
    slots = kt_ref.shape[1]
    chunks = slots // CHUNK

    for h in range(H):
        x = q_ref[:, h * DH:(h + 1) * DH].astype(f32)
        scale = lax.rsqrt(jnp.mean(x * x, -1, keepdims=True) + epsilon)
        nq = (x * scale).astype(jnp.bfloat16)
        qr_ref[h * BS:(h + 1) * BS, :] = nq
        qt_ref[:, h * BS:(h + 1) * BS] = nq.astype(f32).T.astype(jnp.bfloat16)

    head_ids = lax.broadcasted_iota(jnp.int32, (H, HEAD_GROUP), 0)
    pick_ids = lax.broadcasted_iota(jnp.int32, (H, HEAD_GROUP), 1)
    lane_heads = lax.broadcasted_iota(jnp.int32, (1, H), 1)

    def group_weights(g):
        onehot = (head_ids == g * HEAD_GROUP + pick_ids).astype(jnp.bfloat16)
        w4 = jnp.dot(w_ref[...], onehot, preferred_element_type=f32)
        return jnp.concatenate([w4[:, hh:hh + 1] for hh in range(HEAD_GROUP)], 0)

    mix_ref[...] = jnp.zeros_like(mix_ref)
    neg_log2_root = -inv_root * 1.4426950408889634

    def first_pass(g, carry):
        r0 = pl.multiple_of(g * rows, rows)
        q = qr_ref[pl.ds(r0, rows), :]
        wcol = group_weights(g)
        for c in range(chunks):
            cs = slice(c * CHUNK, (c + 1) * CHUNK)
            raw = jnp.dot(q, kt_ref[:, cs], preferred_element_type=f32)
            tail = jnp.exp2(jnp.abs(raw) * neg_log2_root)
            sp = jnp.maximum(raw * inv_root, 0.0) + jnp.log(1.0 + tail)
            sp_ref[pl.ds(r0, rows), cs] = sp
            ws = (wcol * sp).reshape(HEAD_GROUP, BS, CHUNK)
            mix_ref[:, cs] += jnp.sum(ws, 0)
        return carry

    lax.fori_loop(0, groups, first_pass, 0)

    mixture = mix_ref[...]
    squashed = jnp.tanh(mixture / soft_cap)
    logits = soft_cap * squashed
    is_valid = spos_ref[...] <= qpos_ref[...]
    exp_terms = jnp.where(is_valid, jnp.exp(logits - soft_cap), 0.0)
    denominator = jnp.sum(exp_terms, 1, keepdims=True)
    log_prob = logits - soft_cap - jnp.log(denominator)
    kept_mass = jnp.where(is_valid, mass_ref[...].astype(f32), 0.0)
    target = kept_mass / jnp.sum(kept_mass, 1, keepdims=True)
    div_ref[...] = jnp.sum(
        jnp.where(is_valid, target * (jnp.log(jnp.where(is_valid, target, 1.0)) - log_prob), 0.0),
        1, keepdims=True)
    mg_ref[...] = (exp_terms / denominator - target) * (1.0 - squashed * squashed)

    sgt_ref[...] = jnp.zeros_like(sgt_ref)
    wg_ref[...] = jnp.zeros_like(wg_ref)

    def second_pass(g, carry):
        r0 = pl.multiple_of(g * rows, rows)
        q = qr_ref[pl.ds(r0, rows), :]
        qt = qt_ref[:, pl.ds(r0, rows)]
        wcol = group_weights(g)
        qg_acc = jnp.zeros((rows, DH), f32)
        wg_acc = jnp.zeros((rows, 1), f32)
        for c in range(chunks):
            cs = slice(c * CHUNK, (c + 1) * CHUNK)
            s = jnp.dot(q, kt_ref[:, cs], preferred_element_type=f32) * inv_root
            sp = sp_ref[pl.ds(r0, rows), cs]
            sig = jnp.exp(s - sp)
            mgc = mg_ref[:, cs]
            mg4 = jnp.broadcast_to(mgc[None], (HEAD_GROUP, BS, CHUNK)).reshape(rows, CHUNK)
            sg = (mg4 * wcol * sig).astype(jnp.bfloat16)
            wg_acc = wg_acc + jnp.sum(mg4 * sp, 1, keepdims=True)
            qg_acc = qg_acc + jnp.dot(sg, k_ref[cs, :], preferred_element_type=f32)
            sgt_ref[:, cs] += jnp.dot(qt, sg, preferred_element_type=f32)
        qg_acc = qg_acc * inv_root
        wg_sum = wg_ref[...]
        for hh in range(HEAD_GROUP):
            h = g * HEAD_GROUP + hh
            wg_sum = wg_sum + jnp.where(lane_heads == h, wg_acc[hh * BS:(hh + 1) * BS], 0.0)
            lanes = pl.ds(pl.multiple_of(h * DH, DH), DH)
            x = q_ref[:, lanes].astype(f32)
            scale = lax.rsqrt(jnp.mean(x * x, -1, keepdims=True) + epsilon)
            query_hat = x * scale
            qg = qg_acc[hh * BS:(hh + 1) * BS]
            gq_ref[:, lanes] = (qg - query_hat * jnp.mean(qg * query_hat, -1, keepdims=True)) * scale
        wg_ref[...] = wg_sum
        return carry

    lax.fori_loop(0, groups, second_pass, 0)
    sgt_ref[...] = sgt_ref[...] * inv_root


def score_blocks(q, k, kt, w, mass, spos, qpos):
    nblk = q.shape[0]
    slots = k.shape[1]
    nrows = H * BS
    f32 = jnp.float32

    def blk(*shape):
        return pl.BlockSpec((None,) + shape, lambda b: (b,) + (0,) * len(shape))

    flops = nblk * (4 * 2 * nrows * slots * DH)
    return pl.pallas_call(
        score_kernel,
        grid=(nblk,),
        in_specs=[
            blk(BS, H * DH), blk(slots, DH), blk(DH, slots),
            blk(BS, H), blk(BS, slots), blk(1, slots), blk(BS, 1),
        ],
        out_specs=[blk(BS, H * DH), blk(BS, H), blk(DH, slots), blk(BS, 1)],
        out_shape=[
            jax.ShapeDtypeStruct((nblk, BS, H * DH), f32),
            jax.ShapeDtypeStruct((nblk, BS, H), f32),
            jax.ShapeDtypeStruct((nblk, DH, slots), f32),
            jax.ShapeDtypeStruct((nblk, BS, 1), f32),
        ],
        scratch_shapes=[
            pltpu.VMEM((nrows, DH), jnp.bfloat16), pltpu.VMEM((DH, nrows), jnp.bfloat16),
            pltpu.VMEM((BS, slots), f32), pltpu.VMEM((BS, slots), f32), pltpu.VMEM((nrows, slots), f32)
        ],
        compiler_params=pltpu.CompilerParams(
            dimension_semantics=("arbitrary",), vmem_limit_bytes=60 * 1024 * 1024
        ),
        cost_estimate=pl.CostEstimate(
            flops=flops, transcendentals=nblk * nrows * slots * 3,
            bytes_accessed=nblk * (BS * H * DH * 6 + slots * DH * 4 + DH * slots * 4)),
    )(q, k, kt, w, mass, spos, qpos)


def butterfly_sum(value, axes):
    count = 1
    for axis in axes:
        count *= lax.axis_size(axis)
    if count & (count - 1):
        return lax.psum(value, axes)
    stride = 1
    while stride < count:
        pairs = [(i, i ^ stride) for i in range(count)]
        value = value + lax.ppermute(value, axes, pairs)
        stride *= 2
    return value


def per_device(queries, keys, head_weights, block_ids, target_mass, key_gain, key_bias):
    ctx_count = lax.axis_size("ctx")
    ctx_index = lax.axis_index("ctx")
    dp_count = lax.axis_size("dp")
    dp_index = lax.axis_index("dp")
    key_count = KD // BS
    query_count = QD // BS
    capacity = 2 * query_count
    request_count = query_count * NSEL
    slot_count = NSEL * BS
    key_hat, key_scale, normed_keys = key_norm(keys[0], key_gain, key_bias)
    listed_ids = block_ids[0].reshape(request_count)
    is_listed = listed_ids >= 0
    block_safe = jnp.maximum(listed_ids, 0)
    owner_index = block_safe // key_count
    local_block = block_safe % key_count
    owner_hits = (
        (owner_index[:, None] == jnp.arange(ctx_count, dtype=jnp.int32)[None, :])
        & is_listed[:, None]
    ).astype(jnp.int32)
    earlier = jnp.cumsum(owner_hits, 0) - owner_hits
    rank_slot = jnp.sum(earlier * owner_hits, 1)
    target_slot = jnp.where(is_listed, owner_index * capacity + rank_slot, 0)
    placement = (
        target_slot[:, None] == jnp.arange(ctx_count * capacity, dtype=jnp.int32)[None, :]
    ) & is_listed[:, None]
    request_table = jnp.sum(jnp.where(placement, local_block[:, None] + 1, 0), 0) - 1
    request_table = request_table.reshape(ctx_count, capacity)
    asked_back = lax.all_to_all(request_table, "ctx", split_axis=0, concat_axis=0, tiled=True)
    sent_keys = normed_keys.reshape(key_count, BS, DH)[jnp.clip(asked_back, 0, key_count - 1)]
    arrived_keys = lax.all_to_all(sent_keys, "ctx", split_axis=0, concat_axis=0, tiled=True)
    picked = arrived_keys.reshape(ctx_count * capacity, BS, DH)[target_slot]
    slot_keys = picked.reshape(query_count, slot_count, DH)
    slot_positions = (block_safe[:, None] * BS + jnp.arange(BS, dtype=jnp.int32)[None, :]).reshape(
        query_count, slot_count
    )
    slot_lives = jnp.repeat(is_listed, BS).reshape(query_count, slot_count)
    never = jnp.iinfo(jnp.int32).max
    slot_limit = jnp.where(slot_lives, slot_positions, never).reshape(query_count, 1, slot_count)
    first_pos = ctx_index * KD + KD - QD
    query_pos = (first_pos + jnp.arange(QD, dtype=jnp.int32)).reshape(query_count, BS, 1)

    key_cols = slot_keys.transpose(0, 2, 1)
    mass_rows = target_mass[0].reshape(query_count, BS, slot_count)
    grad_query_rows, weight_grads, slot_grad_t, div_rows = score_blocks(
        queries[0].reshape(query_count, BS, H * DH), slot_keys, key_cols,
        head_weights[0].reshape(query_count, BS, H), mass_rows, slot_limit, query_pos
    )
    divergence_total = jnp.sum(div_rows)
    grad_slots = slot_grad_t.transpose(0, 2, 1)
    slot_flat = grad_slots.reshape(request_count, BS * DH)
    outbound = jnp.dot(placement.T.astype(jnp.float32), slot_flat, precision=lax.Precision.HIGHEST)
    returned = lax.all_to_all(
        outbound.reshape(ctx_count, capacity, BS * DH), "ctx", split_axis=0, concat_axis=0, tiled=True
    )
    own_rows = (
        asked_back.reshape(ctx_count * capacity)[None, :]
        == jnp.arange(key_count, dtype=jnp.int32)[:, None]
    ).astype(jnp.float32)
    key_grad = jnp.dot(
        own_rows, returned.reshape(ctx_count * capacity, BS * DH), precision=lax.Precision.HIGHEST
    ).reshape(KD, DH)
    gain_part = jnp.sum(key_grad * key_hat, 0)
    bias_part = jnp.sum(key_grad, 0)
    scaled_grad = key_grad * key_gain
    grad_key_rows = (
        scaled_grad
        - jnp.mean(scaled_grad, -1, keepdims=True)
        - key_hat * jnp.mean(scaled_grad * key_hat, -1, keepdims=True)
    ) * key_scale
    loss_slots = jnp.where(jnp.arange(dp_count) == dp_index, divergence_total, 0.0)
    packed = butterfly_sum(jnp.concatenate([gain_part, bias_part, loss_slots]), ("dp", "ctx"))
    grad_gain = packed[:DH]
    grad_bias = packed[DH:2 * DH]
    loss_total = lax.dynamic_index_in_dim(packed, 2 * DH + dp_index, 0, keepdims=False)
    seq_loss = jnp.reshape(loss_total / (QD * ctx_count), (1,))
    return (
        seq_loss,
        grad_query_rows.reshape(1, QD, H * DH),
        weight_grads.reshape(1, QD, H),
        grad_key_rows.reshape(1, KD, DH),
        grad_gain,
        grad_bias,
    )


def solution(mesh):
    in_specs = (
        P("dp", "ctx", None),
        P("dp", "ctx", None),
        P("dp", "ctx", None),
        P("dp", "ctx", None),
        P("dp", "ctx", None),
        P(),
        P(),
    )
    out_specs = (
        P("dp"),
        P("dp", "ctx", None),
        P("dp", "ctx", None),
        P("dp", "ctx", None),
        P(),
        P(),
    )
    return jax.shard_map(
        per_device, mesh=mesh, in_specs=in_specs, out_specs=out_specs, check_vma=False
    )
```

```python
import functools
import jax
import jax.numpy as jnp
from jax import lax
from jax.experimental import pallas as pl
from jax.experimental.pallas import tpu as pltpu
from jax.sharding import PartitionSpec as P

H = 32
DH = 128
BS = 64
NSEL = 32
QD = 128
KD = 1024

epsilon = 1e-06
soft_cap = 20.0

HEAD_GROUP = 32
CHUNK = 256


def key_norm(key_rows, key_gain, key_bias):
    key_float = key_rows.astype(jnp.float32)
    key_mean = jnp.mean(key_float, -1, keepdims=True)
    centered = key_float - key_mean
    key_var = jnp.mean(centered * centered, -1, keepdims=True)
    key_scale = lax.rsqrt(key_var + epsilon)
    key_hat = centered * key_scale
    normed_keys = (key_hat * key_gain + key_bias).astype(jnp.bfloat16)
    return (key_hat, key_scale, normed_keys)


def query_norm(query_rows):
    query_float = query_rows.astype(jnp.float32).reshape(query_rows.shape[0], H, DH)
    query_scale = lax.rsqrt(jnp.mean(query_float * query_float, -1, keepdims=True) + epsilon)
    query_hat = query_float * query_scale
    return (query_hat, query_scale, query_hat.astype(jnp.bfloat16))


def query_kernel(q_ref, qr_ref, qt_ref):
    f32 = jnp.float32
    for h in range(H):
        x = q_ref[:, h * DH:(h + 1) * DH].astype(f32)
        scale = lax.rsqrt(jnp.mean(x * x, -1, keepdims=True) + epsilon)
        nq = (x * scale).astype(jnp.bfloat16)
        qr_ref[h * BS:(h + 1) * BS, :] = nq
        qt_ref[:, h * BS:(h + 1) * BS] = nq.astype(f32).T.astype(jnp.bfloat16)


def normed_query_rows(q):
    nblk = q.shape[0]
    nrows = H * BS

    def blk(*shape):
        return pl.BlockSpec((None,) + shape, lambda b: (b,) + (0,) * len(shape))

    return pl.pallas_call(
        query_kernel,
        grid=(nblk,),
        in_specs=[blk(BS, H * DH)],
        out_specs=[blk(nrows, DH), blk(DH, nrows)],
        out_shape=[
            jax.ShapeDtypeStruct((nblk, nrows, DH), jnp.bfloat16),
            jax.ShapeDtypeStruct((nblk, DH, nrows), jnp.bfloat16),
        ],
        compiler_params=pltpu.CompilerParams(dimension_semantics=("arbitrary",)),
        cost_estimate=pl.CostEstimate(
            flops=nblk * nrows * DH * 4, transcendentals=nblk * nrows,
            bytes_accessed=nblk * nrows * DH * 6),
    )(q)


def score_kernel(q_ref, qr_ref, qt_ref, k_ref, kt_ref, w_ref, mass_ref, spos_ref, qpos_ref,
                 gq_ref, wg_ref, sgt_ref, div_ref, mix_ref, mg_ref, sp_ref):
    f32 = jnp.float32
    inv_root = DH ** (-0.5)
    rows = HEAD_GROUP * BS
    groups = H // HEAD_GROUP
    slots = kt_ref.shape[1]
    chunks = slots // CHUNK

    head_ids = lax.broadcasted_iota(jnp.int32, (H, HEAD_GROUP), 0)
    pick_ids = lax.broadcasted_iota(jnp.int32, (H, HEAD_GROUP), 1)
    lane_heads = lax.broadcasted_iota(jnp.int32, (1, H), 1)

    def group_weights(g):
        onehot = (head_ids == g * HEAD_GROUP + pick_ids).astype(jnp.bfloat16)
        w4 = jnp.dot(w_ref[...], onehot, preferred_element_type=f32)
        return jnp.concatenate([w4[:, hh:hh + 1] for hh in range(HEAD_GROUP)], 0)

    mix_ref[...] = jnp.zeros_like(mix_ref)
    neg_log2_root = -inv_root * 1.4426950408889634

    def first_pass(g, carry):
        r0 = pl.multiple_of(g * rows, rows)
        q = qr_ref[pl.ds(r0, rows), :]
        wcol = group_weights(g)
        for c in range(chunks):
            cs = slice(c * CHUNK, (c + 1) * CHUNK)
            raw = jnp.dot(q, kt_ref[:, cs], preferred_element_type=f32)
            tail = jnp.exp2(jnp.abs(raw) * neg_log2_root)
            sp = jnp.maximum(raw * inv_root, 0.0) + jnp.log(1.0 + tail)
            sp_ref[pl.ds(r0, rows), cs] = sp
            ws = (wcol * sp).reshape(HEAD_GROUP, BS, CHUNK)
            mix_ref[:, cs] += jnp.sum(ws, 0)
        return carry

    lax.fori_loop(0, groups, first_pass, 0)

    mixture = mix_ref[...]
    squashed = jnp.tanh(mixture / soft_cap)
    logits = soft_cap * squashed
    is_valid = spos_ref[...] <= qpos_ref[...]
    exp_terms = jnp.where(is_valid, jnp.exp(logits - soft_cap), 0.0)
    denominator = jnp.sum(exp_terms, 1, keepdims=True)
    log_prob = logits - soft_cap - jnp.log(denominator)
    kept_mass = jnp.where(is_valid, mass_ref[...].astype(f32), 0.0)
    target = kept_mass / jnp.sum(kept_mass, 1, keepdims=True)
    div_ref[...] = jnp.sum(
        jnp.where(is_valid, target * (jnp.log(jnp.where(is_valid, target, 1.0)) - log_prob), 0.0),
        1, keepdims=True)
    mg_ref[...] = (exp_terms / denominator - target) * (1.0 - squashed * squashed)

    sgt_ref[...] = jnp.zeros_like(sgt_ref)
    wg_ref[...] = jnp.zeros_like(wg_ref)

    def second_pass(g, carry):
        r0 = pl.multiple_of(g * rows, rows)
        q = qr_ref[pl.ds(r0, rows), :]
        qt = qt_ref[:, pl.ds(r0, rows)]
        wcol = group_weights(g)
        qg_acc = jnp.zeros((rows, DH), f32)
        wg_acc = jnp.zeros((rows, 1), f32)
        for c in range(chunks):
            cs = slice(c * CHUNK, (c + 1) * CHUNK)
            s = jnp.dot(q, kt_ref[:, cs], preferred_element_type=f32) * inv_root
            sp = sp_ref[pl.ds(r0, rows), cs]
            sig = jnp.exp(s - sp)
            mgc = mg_ref[:, cs]
            mg4 = jnp.broadcast_to(mgc[None], (HEAD_GROUP, BS, CHUNK)).reshape(rows, CHUNK)
            sg = (mg4 * wcol * sig).astype(jnp.bfloat16)
            wg_acc = wg_acc + jnp.sum(mg4 * sp, 1, keepdims=True)
            qg_acc = qg_acc + jnp.dot(sg, k_ref[cs, :], preferred_element_type=f32)
            sgt_ref[:, cs] += jnp.dot(qt, sg, preferred_element_type=f32)
        qg_acc = qg_acc * inv_root
        wg_sum = wg_ref[...]
        for hh in range(HEAD_GROUP):
            h = g * HEAD_GROUP + hh
            wg_sum = wg_sum + jnp.where(lane_heads == h, wg_acc[hh * BS:(hh + 1) * BS], 0.0)
            lanes = pl.ds(pl.multiple_of(h * DH, DH), DH)
            x = q_ref[:, lanes].astype(f32)
            scale = lax.rsqrt(jnp.mean(x * x, -1, keepdims=True) + epsilon)
            query_hat = x * scale
            qg = qg_acc[hh * BS:(hh + 1) * BS]
            gq_ref[:, lanes] = (qg - query_hat * jnp.mean(qg * query_hat, -1, keepdims=True)) * scale
        wg_ref[...] = wg_sum
        return carry

    lax.fori_loop(0, groups, second_pass, 0)
    sgt_ref[...] = sgt_ref[...] * inv_root


def score_blocks(q, qr, qt, k, kt, w, mass, spos, qpos):
    nblk = q.shape[0]
    slots = k.shape[1]
    nrows = H * BS
    f32 = jnp.float32

    def blk(*shape):
        return pl.BlockSpec((None,) + shape, lambda b: (b,) + (0,) * len(shape))

    flops = nblk * (4 * 2 * nrows * slots * DH)
    return pl.pallas_call(
        score_kernel,
        grid=(nblk,),
        in_specs=[
            blk(BS, H * DH), blk(nrows, DH), blk(DH, nrows), blk(slots, DH), blk(DH, slots),
            blk(BS, H), blk(BS, slots), blk(1, slots), blk(BS, 1),
        ],
        out_specs=[blk(BS, H * DH), blk(BS, H), blk(DH, slots), blk(BS, 1)],
        out_shape=[
            jax.ShapeDtypeStruct((nblk, BS, H * DH), f32),
            jax.ShapeDtypeStruct((nblk, BS, H), f32),
            jax.ShapeDtypeStruct((nblk, DH, slots), f32),
            jax.ShapeDtypeStruct((nblk, BS, 1), f32),
        ],
        scratch_shapes=[
            pltpu.VMEM((BS, slots), f32), pltpu.VMEM((BS, slots), f32), pltpu.VMEM((nrows, slots), f32)
        ],
        compiler_params=pltpu.CompilerParams(
            dimension_semantics=("arbitrary",), vmem_limit_bytes=60 * 1024 * 1024
        ),
        cost_estimate=pl.CostEstimate(
            flops=flops, transcendentals=nblk * nrows * slots * 3,
            bytes_accessed=nblk * (BS * H * DH * 6 + slots * DH * 4 + DH * slots * 4)),
    )(q, qr, qt, k, kt, w, mass, spos, qpos)


def butterfly_sum(value, axes):
    count = 1
    for axis in axes:
        count *= lax.axis_size(axis)
    if count & (count - 1):
        return lax.psum(value, axes)
    stride = 1
    while stride < count:
        pairs = [(i, i ^ stride) for i in range(count)]
        value = value + lax.ppermute(value, axes, pairs)
        stride *= 2
    return value


def per_device(queries, keys, head_weights, block_ids, target_mass, key_gain, key_bias):
    ctx_count = lax.axis_size("ctx")
    ctx_index = lax.axis_index("ctx")
    dp_count = lax.axis_size("dp")
    dp_index = lax.axis_index("dp")
    key_count = KD // BS
    query_count = QD // BS
    capacity = 2 * query_count
    request_count = query_count * NSEL
    slot_count = NSEL * BS
    key_hat, key_scale, normed_keys = key_norm(keys[0], key_gain, key_bias)
    listed_ids = block_ids[0].reshape(request_count)
    is_listed = listed_ids >= 0
    block_safe = jnp.maximum(listed_ids, 0)
    owner_index = block_safe // key_count
    local_block = block_safe % key_count
    owner_hits = (
        (owner_index[:, None] == jnp.arange(ctx_count, dtype=jnp.int32)[None, :])
        & is_listed[:, None]
    ).astype(jnp.int32)
    earlier = jnp.cumsum(owner_hits, 0) - owner_hits
    rank_slot = jnp.sum(earlier * owner_hits, 1)
    target_slot = jnp.where(is_listed, owner_index * capacity + rank_slot, 0)
    placement = (
        target_slot[:, None] == jnp.arange(ctx_count * capacity, dtype=jnp.int32)[None, :]
    ) & is_listed[:, None]
    request_table = jnp.sum(jnp.where(placement, local_block[:, None] + 1, 0), 0) - 1
    request_table = request_table.reshape(ctx_count, capacity)
    asked_back = lax.all_to_all(request_table, "ctx", split_axis=0, concat_axis=0, tiled=True)
    sent_keys = normed_keys.reshape(key_count, BS, DH)[jnp.clip(asked_back, 0, key_count - 1)]
    arrived_keys = lax.all_to_all(sent_keys, "ctx", split_axis=0, concat_axis=0, tiled=True)
    picked = arrived_keys.reshape(ctx_count * capacity, BS, DH)[target_slot]
    slot_keys = picked.reshape(query_count, slot_count, DH)
    slot_positions = (block_safe[:, None] * BS + jnp.arange(BS, dtype=jnp.int32)[None, :]).reshape(
        query_count, slot_count
    )
    slot_lives = jnp.repeat(is_listed, BS).reshape(query_count, slot_count)
    never = jnp.iinfo(jnp.int32).max
    slot_limit = jnp.where(slot_lives, slot_positions, never).reshape(query_count, 1, slot_count)
    first_pos = ctx_index * KD + KD - QD
    query_pos = (first_pos + jnp.arange(QD, dtype=jnp.int32)).reshape(query_count, BS, 1)

    key_cols = slot_keys.transpose(0, 2, 1)
    mass_rows = target_mass[0].reshape(query_count, BS, slot_count)
    query_blocks = queries[0].reshape(query_count, BS, H * DH)
    head_rows, head_cols = normed_query_rows(query_blocks)
    grad_query_rows, weight_grads, slot_grad_t, div_rows = score_blocks(
        query_blocks, head_rows, head_cols, slot_keys, key_cols,
        head_weights[0].reshape(query_count, BS, H), mass_rows, slot_limit, query_pos
    )
    divergence_total = jnp.sum(div_rows)
    grad_slots = slot_grad_t.transpose(0, 2, 1)
    slot_flat = grad_slots.reshape(request_count, BS * DH)
    outbound = jnp.dot(placement.T.astype(jnp.float32), slot_flat, precision=lax.Precision.HIGHEST)
    returned = lax.all_to_all(
        outbound.reshape(ctx_count, capacity, BS * DH), "ctx", split_axis=0, concat_axis=0, tiled=True
    )
    own_rows = (
        asked_back.reshape(ctx_count * capacity)[None, :]
        == jnp.arange(key_count, dtype=jnp.int32)[:, None]
    ).astype(jnp.float32)
    key_grad = jnp.dot(
        own_rows, returned.reshape(ctx_count * capacity, BS * DH), precision=lax.Precision.HIGHEST
    ).reshape(KD, DH)
    gain_part = jnp.sum(key_grad * key_hat, 0)
    bias_part = jnp.sum(key_grad, 0)
    scaled_grad = key_grad * key_gain
    grad_key_rows = (
        scaled_grad
        - jnp.mean(scaled_grad, -1, keepdims=True)
        - key_hat * jnp.mean(scaled_grad * key_hat, -1, keepdims=True)
    ) * key_scale
    loss_slots = jnp.where(jnp.arange(dp_count) == dp_index, divergence_total, 0.0)
    packed = butterfly_sum(jnp.concatenate([gain_part, bias_part, loss_slots]), ("dp", "ctx"))
    grad_gain = packed[:DH]
    grad_bias = packed[DH:2 * DH]
    loss_total = lax.dynamic_index_in_dim(packed, 2 * DH + dp_index, 0, keepdims=False)
    seq_loss = jnp.reshape(loss_total / (QD * ctx_count), (1,))
    return (
        seq_loss,
        grad_query_rows.reshape(1, QD, H * DH),
        weight_grads.reshape(1, QD, H),
        grad_key_rows.reshape(1, KD, DH),
        grad_gain,
        grad_bias,
    )


def solution(mesh):
    in_specs = (
        P("dp", "ctx", None),
        P("dp", "ctx", None),
        P("dp", "ctx", None),
        P("dp", "ctx", None),
        P("dp", "ctx", None),
        P(),
        P(),
    )
    out_specs = (
        P("dp"),
        P("dp", "ctx", None),
        P("dp", "ctx", None),
        P("dp", "ctx", None),
        P(),
        P(),
    )
    return jax.shard_map(
        per_device, mesh=mesh, in_specs=in_specs, out_specs=out_specs, check_vma=False
    )
```

```python
import functools
import jax
import jax.numpy as jnp
from jax import lax
from jax.experimental import pallas as pl
from jax.experimental.pallas import tpu as pltpu
from jax.sharding import PartitionSpec as P

H = 32
DH = 128
BS = 64
NSEL = 32
QD = 128
KD = 1024

epsilon = 1e-06
soft_cap = 20.0

HEAD_GROUP = 32
CHUNK = 256


def key_norm(key_rows, key_gain, key_bias):
    key_float = key_rows.astype(jnp.float32)
    key_mean = jnp.mean(key_float, -1, keepdims=True)
    centered = key_float - key_mean
    key_var = jnp.mean(centered * centered, -1, keepdims=True)
    key_scale = lax.rsqrt(key_var + epsilon)
    key_hat = centered * key_scale
    normed_keys = (key_hat * key_gain + key_bias).astype(jnp.bfloat16)
    return (key_hat, key_scale, normed_keys)


def query_norm(query_rows):
    query_float = query_rows.astype(jnp.float32).reshape(query_rows.shape[0], H, DH)
    query_scale = lax.rsqrt(jnp.mean(query_float * query_float, -1, keepdims=True) + epsilon)
    query_hat = query_float * query_scale
    return (query_hat, query_scale, query_hat.astype(jnp.bfloat16))


def query_kernel(q_ref, qr_ref, qt_ref):
    f32 = jnp.float32
    for h in range(H):
        x = q_ref[:, h * DH:(h + 1) * DH].astype(f32)
        scale = lax.rsqrt(jnp.mean(x * x, -1, keepdims=True) + epsilon)
        nq = (x * scale).astype(jnp.bfloat16)
        qr_ref[h * BS:(h + 1) * BS, :] = nq
        qt_ref[:, h * BS:(h + 1) * BS] = nq.astype(f32).T.astype(jnp.bfloat16)


def normed_query_rows(q):
    nblk = q.shape[0]
    nrows = H * BS

    def blk(*shape):
        return pl.BlockSpec((None,) + shape, lambda b: (b,) + (0,) * len(shape))

    return pl.pallas_call(
        query_kernel,
        grid=(nblk,),
        in_specs=[blk(BS, H * DH)],
        out_specs=[blk(nrows, DH), blk(DH, nrows)],
        out_shape=[
            jax.ShapeDtypeStruct((nblk, nrows, DH), jnp.bfloat16),
            jax.ShapeDtypeStruct((nblk, DH, nrows), jnp.bfloat16),
        ],
        compiler_params=pltpu.CompilerParams(dimension_semantics=("arbitrary",)),
        cost_estimate=pl.CostEstimate(
            flops=nblk * nrows * DH * 4, transcendentals=nblk * nrows,
            bytes_accessed=nblk * nrows * DH * 6),
    )(q)


def score_kernel(q_ref, qr_ref, qt_ref, k_ref, kt_ref, w_ref, mass_ref, spos_ref, qpos_ref,
                 gq_ref, wg_ref, sgt_ref, div_ref, mix_ref, mg_ref, sp_ref):
    f32 = jnp.float32
    inv_root = DH ** (-0.5)
    rows = HEAD_GROUP * BS
    groups = H // HEAD_GROUP
    slots = kt_ref.shape[1]
    chunks = slots // CHUNK

    head_ids = lax.broadcasted_iota(jnp.int32, (H, HEAD_GROUP), 0)
    pick_ids = lax.broadcasted_iota(jnp.int32, (H, HEAD_GROUP), 1)
    lane_heads = lax.broadcasted_iota(jnp.int32, (1, H), 1)

    def group_weights(g):
        onehot = (head_ids == g * HEAD_GROUP + pick_ids).astype(jnp.bfloat16)
        w4 = jnp.dot(w_ref[...], onehot, preferred_element_type=f32)
        return jnp.concatenate([w4[:, hh:hh + 1] for hh in range(HEAD_GROUP)], 0)

    mix_ref[...] = jnp.zeros_like(mix_ref)
    neg_log2_root = -inv_root * 1.4426950408889634

    def first_pass(g, carry):
        r0 = pl.multiple_of(g * rows, rows)
        q = qr_ref[pl.ds(r0, rows), :]
        wcol = group_weights(g)
        for c in range(chunks):
            cs = slice(c * CHUNK, (c + 1) * CHUNK)
            raw = jnp.dot(q, kt_ref[:, cs], preferred_element_type=f32)
            tail = jnp.exp2(jnp.abs(raw) * neg_log2_root)
            sp = jnp.maximum(raw * inv_root, 0.0) + jnp.log(1.0 + tail)
            sp_ref[pl.ds(r0, rows), cs] = sp
            ws = (wcol * sp).reshape(HEAD_GROUP, BS, CHUNK)
            mix_ref[:, cs] += jnp.sum(ws, 0)
        return carry

    lax.fori_loop(0, groups, first_pass, 0)

    mixture = mix_ref[...]
    squashed = jnp.tanh(mixture / soft_cap)
    logits = soft_cap * squashed
    is_valid = spos_ref[...] <= qpos_ref[...]
    exp_terms = jnp.where(is_valid, jnp.exp(logits - soft_cap), 0.0)
    denominator = jnp.sum(exp_terms, 1, keepdims=True)
    log_prob = logits - soft_cap - jnp.log(denominator)
    kept_mass = jnp.where(is_valid, mass_ref[...].astype(f32), 0.0)
    target = kept_mass / jnp.sum(kept_mass, 1, keepdims=True)
    div_ref[...] = jnp.sum(
        jnp.where(is_valid, target * (jnp.log(jnp.where(is_valid, target, 1.0)) - log_prob), 0.0),
        1, keepdims=True)
    mg_ref[...] = (exp_terms / denominator - target) * (1.0 - squashed * squashed)

    sgt_ref[...] = jnp.zeros_like(sgt_ref)
    wg_ref[...] = jnp.zeros_like(wg_ref)

    def second_pass(g, carry):
        r0 = pl.multiple_of(g * rows, rows)
        q = qr_ref[pl.ds(r0, rows), :]
        qt = qt_ref[:, pl.ds(r0, rows)]
        wcol = group_weights(g)
        qg_acc = jnp.zeros((rows, DH), f32)
        wg_acc = jnp.zeros((rows, 1), f32)
        for c in range(chunks):
            cs = slice(c * CHUNK, (c + 1) * CHUNK)
            s = jnp.dot(q, kt_ref[:, cs], preferred_element_type=f32) * inv_root
            sp = sp_ref[pl.ds(r0, rows), cs]
            sig = jnp.exp(s - sp)
            mgc = mg_ref[:, cs]
            mg4 = jnp.broadcast_to(mgc[None], (HEAD_GROUP, BS, CHUNK)).reshape(rows, CHUNK)
            sg = (mg4 * wcol * sig).astype(jnp.bfloat16)
            wg_acc = wg_acc + jnp.sum(mg4 * sp, 1, keepdims=True)
            qg_acc = qg_acc + jnp.dot(sg, k_ref[cs, :], preferred_element_type=f32)
            sgt_ref[:, cs] += jnp.dot(qt, sg, preferred_element_type=f32)
        qg_acc = qg_acc * inv_root
        wg_sum = wg_ref[...]
        for hh in range(HEAD_GROUP):
            h = g * HEAD_GROUP + hh
            wg_sum = wg_sum + jnp.where(lane_heads == h, wg_acc[hh * BS:(hh + 1) * BS], 0.0)
            lanes = pl.ds(pl.multiple_of(h * DH, DH), DH)
            x = q_ref[:, lanes].astype(f32)
            scale = lax.rsqrt(jnp.mean(x * x, -1, keepdims=True) + epsilon)
            query_hat = x * scale
            qg = qg_acc[hh * BS:(hh + 1) * BS]
            gq_ref[:, lanes] = (qg - query_hat * jnp.mean(qg * query_hat, -1, keepdims=True)) * scale
        wg_ref[...] = wg_sum
        return carry

    lax.fori_loop(0, groups, second_pass, 0)
    sgt_ref[...] = sgt_ref[...] * inv_root


def score_blocks(q, qr, qt, k, kt, w, mass, spos, qpos):
    nblk = q.shape[0]
    slots = k.shape[1]
    nrows = H * BS
    f32 = jnp.float32

    def blk(*shape):
        return pl.BlockSpec((None,) + shape, lambda b: (b,) + (0,) * len(shape))

    flops = nblk * (4 * 2 * nrows * slots * DH)
    return pl.pallas_call(
        score_kernel,
        grid=(nblk,),
        in_specs=[
            blk(BS, H * DH), blk(nrows, DH), blk(DH, nrows), blk(slots, DH), blk(DH, slots),
            blk(BS, H), blk(BS, slots), blk(1, slots), blk(BS, 1),
        ],
        out_specs=[blk(BS, H * DH), blk(BS, H), blk(DH, slots), blk(BS, 1)],
        out_shape=[
            jax.ShapeDtypeStruct((nblk, BS, H * DH), f32),
            jax.ShapeDtypeStruct((nblk, BS, H), f32),
            jax.ShapeDtypeStruct((nblk, DH, slots), f32),
            jax.ShapeDtypeStruct((nblk, BS, 1), f32),
        ],
        scratch_shapes=[
            pltpu.VMEM((BS, slots), f32), pltpu.VMEM((BS, slots), f32), pltpu.VMEM((nrows, slots), f32)
        ],
        compiler_params=pltpu.CompilerParams(
            dimension_semantics=("arbitrary",), vmem_limit_bytes=60 * 1024 * 1024
        ),
        cost_estimate=pl.CostEstimate(
            flops=flops, transcendentals=nblk * nrows * slots * 3,
            bytes_accessed=nblk * (BS * H * DH * 6 + slots * DH * 4 + DH * slots * 4)),
    )(q, qr, qt, k, kt, w, mass, spos, qpos)


def butterfly_sum(value, axes):
    count = 1
    for axis in axes:
        count *= lax.axis_size(axis)
    if count & (count - 1):
        return lax.psum(value, axes)
    stride = 1
    while stride < count:
        pairs = [(i, i ^ stride) for i in range(count)]
        value = value + lax.ppermute(value, axes, pairs)
        stride *= 2
    return value


def per_device(queries, keys, head_weights, block_ids, target_mass, key_gain, key_bias):
    ctx_count = lax.axis_size("ctx")
    ctx_index = lax.axis_index("ctx")
    dp_count = lax.axis_size("dp")
    dp_index = lax.axis_index("dp")
    key_count = KD // BS
    query_count = QD // BS
    capacity = 2 * query_count
    request_count = query_count * NSEL
    slot_count = NSEL * BS
    key_hat, key_scale, normed_keys = key_norm(keys[0], key_gain, key_bias)
    listed_ids = block_ids[0].reshape(request_count)
    is_listed = listed_ids >= 0
    block_safe = jnp.maximum(listed_ids, 0)
    owner_index = block_safe // key_count
    local_block = block_safe % key_count
    owner_hits = (
        (owner_index[:, None] == jnp.arange(ctx_count, dtype=jnp.int32)[None, :])
        & is_listed[:, None]
    ).astype(jnp.int32)
    earlier = jnp.cumsum(owner_hits, 0) - owner_hits
    rank_slot = jnp.sum(earlier * owner_hits, 1)
    target_slot = jnp.where(is_listed, owner_index * capacity + rank_slot, 0)
    placement = (
        target_slot[:, None] == jnp.arange(ctx_count * capacity, dtype=jnp.int32)[None, :]
    ) & is_listed[:, None]
    request_table = jnp.sum(jnp.where(placement, local_block[:, None] + 1, 0), 0) - 1
    request_table = request_table.reshape(ctx_count, capacity)
    asked_back = lax.all_to_all(request_table, "ctx", split_axis=0, concat_axis=0, tiled=True)
    sent_hats = key_hat.reshape(key_count, BS, DH)[jnp.clip(asked_back, 0, key_count - 1)]
    arrived_hats = lax.all_to_all(sent_hats, "ctx", split_axis=0, concat_axis=0, tiled=True)
    slot_hats = arrived_hats.reshape(ctx_count * capacity, BS, DH)[target_slot]
    slot_keys = (slot_hats * key_gain + key_bias).astype(jnp.bfloat16)
    slot_keys = slot_keys.reshape(query_count, slot_count, DH)
    slot_positions = (block_safe[:, None] * BS + jnp.arange(BS, dtype=jnp.int32)[None, :]).reshape(
        query_count, slot_count
    )
    slot_lives = jnp.repeat(is_listed, BS).reshape(query_count, slot_count)
    never = jnp.iinfo(jnp.int32).max
    slot_limit = jnp.where(slot_lives, slot_positions, never).reshape(query_count, 1, slot_count)
    first_pos = ctx_index * KD + KD - QD
    query_pos = (first_pos + jnp.arange(QD, dtype=jnp.int32)).reshape(query_count, BS, 1)

    key_cols = slot_keys.transpose(0, 2, 1)
    mass_rows = target_mass[0].reshape(query_count, BS, slot_count)
    query_blocks = queries[0].reshape(query_count, BS, H * DH)
    head_rows, head_cols = normed_query_rows(query_blocks)
    grad_query_rows, weight_grads, slot_grad_t, div_rows = score_blocks(
        query_blocks, head_rows, head_cols, slot_keys, key_cols,
        head_weights[0].reshape(query_count, BS, H), mass_rows, slot_limit, query_pos
    )
    divergence_total = jnp.sum(div_rows)
    grad_slots = slot_grad_t.transpose(0, 2, 1)
    live_slots = jnp.where(is_listed[:, None, None], grad_slots.reshape(request_count, BS, DH), 0.0)
    gain_part = jnp.sum(live_slots * slot_hats, (0, 1))
    bias_part = jnp.sum(live_slots, (0, 1))
    slot_flat = grad_slots.reshape(request_count, BS * DH)
    outbound = jnp.dot(placement.T.astype(jnp.float32), slot_flat, precision=lax.Precision.HIGHEST)
    returned = lax.all_to_all(
        outbound.reshape(ctx_count, capacity, BS * DH), "ctx", split_axis=0, concat_axis=0, tiled=True
    )
    own_rows = (
        asked_back.reshape(ctx_count * capacity)[None, :]
        == jnp.arange(key_count, dtype=jnp.int32)[:, None]
    ).astype(jnp.float32)
    key_grad = jnp.dot(
        own_rows, returned.reshape(ctx_count * capacity, BS * DH), precision=lax.Precision.HIGHEST
    ).reshape(KD, DH)
    scaled_grad = key_grad * key_gain
    grad_key_rows = (
        scaled_grad
        - jnp.mean(scaled_grad, -1, keepdims=True)
        - key_hat * jnp.mean(scaled_grad * key_hat, -1, keepdims=True)
    ) * key_scale
    loss_slots = jnp.where(jnp.arange(dp_count) == dp_index, divergence_total, 0.0)
    packed = butterfly_sum(jnp.concatenate([gain_part, bias_part, loss_slots]), ("dp", "ctx"))
    grad_gain = packed[:DH]
    grad_bias = packed[DH:2 * DH]
    loss_total = lax.dynamic_index_in_dim(packed, 2 * DH + dp_index, 0, keepdims=False)
    seq_loss = jnp.reshape(loss_total / (QD * ctx_count), (1,))
    return (
        seq_loss,
        grad_query_rows.reshape(1, QD, H * DH),
        weight_grads.reshape(1, QD, H),
        grad_key_rows.reshape(1, KD, DH),
        grad_gain,
        grad_bias,
    )


def solution(mesh):
    in_specs = (
        P("dp", "ctx", None),
        P("dp", "ctx", None),
        P("dp", "ctx", None),
        P("dp", "ctx", None),
        P("dp", "ctx", None),
        P(),
        P(),
    )
    out_specs = (
        P("dp"),
        P("dp", "ctx", None),
        P("dp", "ctx", None),
        P("dp", "ctx", None),
        P(),
        P(),
    )
    return jax.shard_map(
        per_device, mesh=mesh, in_specs=in_specs, out_specs=out_specs, check_vma=False
    )
```

```python
import functools
import jax
import jax.numpy as jnp
from jax import lax
from jax.experimental import pallas as pl
from jax.experimental.pallas import tpu as pltpu
from jax.sharding import PartitionSpec as P

H = 32
DH = 128
BS = 64
NSEL = 32
QD = 128
KD = 1024

epsilon = 1e-06
soft_cap = 20.0

HEAD_GROUP = 32
CHUNK = 256


def key_norm(key_rows, key_gain, key_bias):
    key_float = key_rows.astype(jnp.float32)
    key_mean = jnp.mean(key_float, -1, keepdims=True)
    centered = key_float - key_mean
    key_var = jnp.mean(centered * centered, -1, keepdims=True)
    key_scale = lax.rsqrt(key_var + epsilon)
    key_hat = centered * key_scale
    normed_keys = (key_hat * key_gain + key_bias).astype(jnp.bfloat16)
    return (key_hat, key_scale, normed_keys)


def query_norm(query_rows):
    query_float = query_rows.astype(jnp.float32).reshape(query_rows.shape[0], H, DH)
    query_scale = lax.rsqrt(jnp.mean(query_float * query_float, -1, keepdims=True) + epsilon)
    query_hat = query_float * query_scale
    return (query_hat, query_scale, query_hat.astype(jnp.bfloat16))


def query_kernel(q_ref, qr_ref, qt_ref):
    f32 = jnp.float32
    for h in range(H):
        x = q_ref[:, h * DH:(h + 1) * DH].astype(f32)
        scale = lax.rsqrt(jnp.mean(x * x, -1, keepdims=True) + epsilon)
        nq = (x * scale).astype(jnp.bfloat16)
        qr_ref[h * BS:(h + 1) * BS, :] = nq
        qt_ref[:, h * BS:(h + 1) * BS] = nq.astype(f32).T.astype(jnp.bfloat16)


def normed_query_rows(q):
    nblk = q.shape[0]
    nrows = H * BS

    def blk(*shape):
        return pl.BlockSpec((None,) + shape, lambda b: (b,) + (0,) * len(shape))

    return pl.pallas_call(
        query_kernel,
        grid=(nblk,),
        in_specs=[blk(BS, H * DH)],
        out_specs=[blk(nrows, DH), blk(DH, nrows)],
        out_shape=[
            jax.ShapeDtypeStruct((nblk, nrows, DH), jnp.bfloat16),
            jax.ShapeDtypeStruct((nblk, DH, nrows), jnp.bfloat16),
        ],
        compiler_params=pltpu.CompilerParams(dimension_semantics=("arbitrary",)),
        cost_estimate=pl.CostEstimate(
            flops=nblk * nrows * DH * 4, transcendentals=nblk * nrows,
            bytes_accessed=nblk * nrows * DH * 6),
    )(q)


def score_kernel(q_ref, qr_ref, qt_ref, k_ref, w_ref, mass_ref, spos_ref, qpos_ref,
                 gq_ref, wg_ref, sgt_ref, div_ref, mix_ref, mg_ref, sp_ref):
    f32 = jnp.float32
    inv_root = DH ** (-0.5)
    rows = HEAD_GROUP * BS
    groups = H // HEAD_GROUP
    slots = k_ref.shape[0]
    chunks = slots // CHUNK

    head_ids = lax.broadcasted_iota(jnp.int32, (H, HEAD_GROUP), 0)
    pick_ids = lax.broadcasted_iota(jnp.int32, (H, HEAD_GROUP), 1)
    lane_heads = lax.broadcasted_iota(jnp.int32, (1, H), 1)

    def group_weights(g):
        onehot = (head_ids == g * HEAD_GROUP + pick_ids).astype(jnp.bfloat16)
        w4 = jnp.dot(w_ref[...], onehot, preferred_element_type=f32)
        return jnp.concatenate([w4[:, hh:hh + 1] for hh in range(HEAD_GROUP)], 0)

    mix_ref[...] = jnp.zeros_like(mix_ref)
    neg_log2_root = -inv_root * 1.4426950408889634

    def first_pass(g, carry):
        r0 = pl.multiple_of(g * rows, rows)
        q = qr_ref[pl.ds(r0, rows), :]
        wcol = group_weights(g)
        for c in range(chunks):
            cs = slice(c * CHUNK, (c + 1) * CHUNK)
            raw = lax.dot_general(q, k_ref[cs, :], (((1,), (1,)), ((), ())), preferred_element_type=f32)
            tail = jnp.exp2(jnp.abs(raw) * neg_log2_root)
            sp = jnp.maximum(raw * inv_root, 0.0) + jnp.log(1.0 + tail)
            sp_ref[pl.ds(r0, rows), cs] = sp
            ws = (wcol * sp).reshape(HEAD_GROUP, BS, CHUNK)
            mix_ref[:, cs] += jnp.sum(ws, 0)
        return carry

    lax.fori_loop(0, groups, first_pass, 0)

    mixture = mix_ref[...]
    squashed = jnp.tanh(mixture / soft_cap)
    logits = soft_cap * squashed
    is_valid = spos_ref[...] <= qpos_ref[...]
    exp_terms = jnp.where(is_valid, jnp.exp(logits - soft_cap), 0.0)
    denominator = jnp.sum(exp_terms, 1, keepdims=True)
    log_prob = logits - soft_cap - jnp.log(denominator)
    kept_mass = jnp.where(is_valid, mass_ref[...].astype(f32), 0.0)
    target = kept_mass / jnp.sum(kept_mass, 1, keepdims=True)
    div_ref[...] = jnp.sum(
        jnp.where(is_valid, target * (jnp.log(jnp.where(is_valid, target, 1.0)) - log_prob), 0.0),
        1, keepdims=True)
    mg_ref[...] = (exp_terms / denominator - target) * (1.0 - squashed * squashed)

    sgt_ref[...] = jnp.zeros_like(sgt_ref)
    wg_ref[...] = jnp.zeros_like(wg_ref)

    def second_pass(g, carry):
        r0 = pl.multiple_of(g * rows, rows)
        q = qr_ref[pl.ds(r0, rows), :]
        qt = qt_ref[:, pl.ds(r0, rows)]
        wcol = group_weights(g)
        qg_acc = jnp.zeros((rows, DH), f32)
        wg_acc = jnp.zeros((rows, 1), f32)
        for c in range(chunks):
            cs = slice(c * CHUNK, (c + 1) * CHUNK)
            s = lax.dot_general(q, k_ref[cs, :], (((1,), (1,)), ((), ())), preferred_element_type=f32) * inv_root
            sp = sp_ref[pl.ds(r0, rows), cs]
            sig = jnp.exp(s - sp)
            mgc = mg_ref[:, cs]
            mg4 = jnp.broadcast_to(mgc[None], (HEAD_GROUP, BS, CHUNK)).reshape(rows, CHUNK)
            sg = (mg4 * wcol * sig).astype(jnp.bfloat16)
            wg_acc = wg_acc + jnp.sum(mg4 * sp, 1, keepdims=True)
            qg_acc = qg_acc + jnp.dot(sg, k_ref[cs, :], preferred_element_type=f32)
            sgt_ref[:, cs] += jnp.dot(qt, sg, preferred_element_type=f32)
        qg_acc = qg_acc * inv_root
        wg_sum = wg_ref[...]
        for hh in range(HEAD_GROUP):
            h = g * HEAD_GROUP + hh
            wg_sum = wg_sum + jnp.where(lane_heads == h, wg_acc[hh * BS:(hh + 1) * BS], 0.0)
            lanes = pl.ds(pl.multiple_of(h * DH, DH), DH)
            x = q_ref[:, lanes].astype(f32)
            scale = lax.rsqrt(jnp.mean(x * x, -1, keepdims=True) + epsilon)
            query_hat = x * scale
            qg = qg_acc[hh * BS:(hh + 1) * BS]
            gq_ref[:, lanes] = (qg - query_hat * jnp.mean(qg * query_hat, -1, keepdims=True)) * scale
        wg_ref[...] = wg_sum
        return carry

    lax.fori_loop(0, groups, second_pass, 0)
    sgt_ref[...] = sgt_ref[...] * inv_root


def score_blocks(q, qr, qt, k, w, mass, spos, qpos):
    nblk = q.shape[0]
    slots = k.shape[1]
    nrows = H * BS
    f32 = jnp.float32

    def blk(*shape):
        return pl.BlockSpec((None,) + shape, lambda b: (b,) + (0,) * len(shape))

    flops = nblk * (4 * 2 * nrows * slots * DH)
    return pl.pallas_call(
        score_kernel,
        grid=(nblk,),
        in_specs=[
            blk(BS, H * DH), blk(nrows, DH), blk(DH, nrows), blk(slots, DH),
            blk(BS, H), blk(BS, slots), blk(1, slots), blk(BS, 1),
        ],
        out_specs=[blk(BS, H * DH), blk(BS, H), blk(DH, slots), blk(BS, 1)],
        out_shape=[
            jax.ShapeDtypeStruct((nblk, BS, H * DH), f32),
            jax.ShapeDtypeStruct((nblk, BS, H), f32),
            jax.ShapeDtypeStruct((nblk, DH, slots), f32),
            jax.ShapeDtypeStruct((nblk, BS, 1), f32),
        ],
        scratch_shapes=[
            pltpu.VMEM((BS, slots), f32), pltpu.VMEM((BS, slots), f32), pltpu.VMEM((nrows, slots), f32)
        ],
        compiler_params=pltpu.CompilerParams(
            dimension_semantics=("arbitrary",), vmem_limit_bytes=60 * 1024 * 1024
        ),
        cost_estimate=pl.CostEstimate(
            flops=flops, transcendentals=nblk * nrows * slots * 3,
            bytes_accessed=nblk * (BS * H * DH * 10 + slots * DH * 6)),
    )(q, qr, qt, k, w, mass, spos, qpos)


def butterfly_sum(value, axes):
    count = 1
    for axis in axes:
        count *= lax.axis_size(axis)
    if count & (count - 1):
        return lax.psum(value, axes)
    stride = 1
    while stride < count:
        pairs = [(i, i ^ stride) for i in range(count)]
        value = value + lax.ppermute(value, axes, pairs)
        stride *= 2
    return value


def per_device(queries, keys, head_weights, block_ids, target_mass, key_gain, key_bias):
    ctx_count = lax.axis_size("ctx")
    ctx_index = lax.axis_index("ctx")
    dp_count = lax.axis_size("dp")
    dp_index = lax.axis_index("dp")
    key_count = KD // BS
    query_count = QD // BS
    capacity = 2 * query_count
    request_count = query_count * NSEL
    slot_count = NSEL * BS
    key_hat, key_scale, normed_keys = key_norm(keys[0], key_gain, key_bias)
    listed_ids = block_ids[0].reshape(request_count)
    is_listed = listed_ids >= 0
    block_safe = jnp.maximum(listed_ids, 0)
    owner_index = block_safe // key_count
    local_block = block_safe % key_count
    owner_hits = (
        (owner_index[:, None] == jnp.arange(ctx_count, dtype=jnp.int32)[None, :])
        & is_listed[:, None]
    ).astype(jnp.int32)
    earlier = jnp.cumsum(owner_hits, 0) - owner_hits
    rank_slot = jnp.sum(earlier * owner_hits, 1)
    target_slot = jnp.where(is_listed, owner_index * capacity + rank_slot, 0)
    placement = (
        target_slot[:, None] == jnp.arange(ctx_count * capacity, dtype=jnp.int32)[None, :]
    ) & is_listed[:, None]
    request_table = jnp.sum(jnp.where(placement, local_block[:, None] + 1, 0), 0) - 1
    request_table = request_table.reshape(ctx_count, capacity)
    asked_back = lax.all_to_all(request_table, "ctx", split_axis=0, concat_axis=0, tiled=True)
    sent_keys = normed_keys.reshape(key_count, BS, DH)[jnp.clip(asked_back, 0, key_count - 1)]
    arrived_keys = lax.all_to_all(sent_keys, "ctx", split_axis=0, concat_axis=0, tiled=True)
    picked = arrived_keys.reshape(ctx_count * capacity, BS, DH)[target_slot]
    slot_keys = picked.reshape(query_count, slot_count, DH)
    slot_positions = (block_safe[:, None] * BS + jnp.arange(BS, dtype=jnp.int32)[None, :]).reshape(
        query_count, slot_count
    )
    slot_lives = jnp.repeat(is_listed, BS).reshape(query_count, slot_count)
    never = jnp.iinfo(jnp.int32).max
    slot_limit = jnp.where(slot_lives, slot_positions, never).reshape(query_count, 1, slot_count)
    first_pos = ctx_index * KD + KD - QD
    query_pos = (first_pos + jnp.arange(QD, dtype=jnp.int32)).reshape(query_count, BS, 1)

    mass_rows = target_mass[0].reshape(query_count, BS, slot_count)
    query_blocks = queries[0].reshape(query_count, BS, H * DH)
    head_rows, head_cols = normed_query_rows(query_blocks)
    grad_query_rows, weight_grads, slot_grad_t, div_rows = score_blocks(
        query_blocks, head_rows, head_cols, slot_keys,
        head_weights[0].reshape(query_count, BS, H), mass_rows, slot_limit, query_pos
    )
    divergence_total = jnp.sum(div_rows)
    grad_slots = slot_grad_t.transpose(0, 2, 1)
    slot_flat = grad_slots.reshape(request_count, BS * DH)
    request_iota = jnp.arange(request_count, dtype=jnp.int32)[:, None]
    source_request = jnp.sum(jnp.where(placement, request_iota, 0), 0)
    slot_used = jnp.any(placement, 0)
    outbound = jnp.where(slot_used[:, None], slot_flat[source_request], 0.0)
    returned = lax.all_to_all(
        outbound.reshape(ctx_count, capacity, BS * DH), "ctx", split_axis=0, concat_axis=0, tiled=True
    )
    own_rows = (
        asked_back.reshape(ctx_count * capacity)[None, :]
        == jnp.arange(key_count, dtype=jnp.int32)[:, None]
    ).astype(jnp.float32)
    key_grad = jnp.dot(
        own_rows, returned.reshape(ctx_count * capacity, BS * DH), precision=lax.Precision.HIGHEST
    ).reshape(KD, DH)
    gain_part = jnp.sum(key_grad * key_hat, 0)
    bias_part = jnp.sum(key_grad, 0)
    scaled_grad = key_grad * key_gain
    grad_key_rows = (
        scaled_grad
        - jnp.mean(scaled_grad, -1, keepdims=True)
        - key_hat * jnp.mean(scaled_grad * key_hat, -1, keepdims=True)
    ) * key_scale
    loss_slots = jnp.where(jnp.arange(dp_count) == dp_index, divergence_total, 0.0)
    packed = butterfly_sum(jnp.concatenate([gain_part, bias_part, loss_slots]), ("dp", "ctx"))
    grad_gain = packed[:DH]
    grad_bias = packed[DH:2 * DH]
    loss_total = lax.dynamic_index_in_dim(packed, 2 * DH + dp_index, 0, keepdims=False)
    seq_loss = jnp.reshape(loss_total / (QD * ctx_count), (1,))
    return (
        seq_loss,
        grad_query_rows.reshape(1, QD, H * DH),
        weight_grads.reshape(1, QD, H),
        grad_key_rows.reshape(1, KD, DH),
        grad_gain,
        grad_bias,
    )


def solution(mesh):
    in_specs = (
        P("dp", "ctx", None),
        P("dp", "ctx", None),
        P("dp", "ctx", None),
        P("dp", "ctx", None),
        P("dp", "ctx", None),
        P(),
        P(),
    )
    out_specs = (
        P("dp"),
        P("dp", "ctx", None),
        P("dp", "ctx", None),
        P("dp", "ctx", None),
        P(),
        P(),
    )
    return jax.shard_map(
        per_device, mesh=mesh, in_specs=in_specs, out_specs=out_specs, check_vma=False
    )
```

```python
import functools
import jax
import jax.numpy as jnp
from jax import lax
from jax.experimental import pallas as pl
from jax.experimental.pallas import tpu as pltpu
from jax.sharding import PartitionSpec as P

H = 32
DH = 128
BS = 64
NSEL = 32
QD = 128
KD = 1024

epsilon = 1e-06
soft_cap = 20.0

HEAD_GROUP = 32
CHUNK = 256


def key_norm(key_rows, key_gain, key_bias):
    key_float = key_rows.astype(jnp.float32)
    key_mean = jnp.mean(key_float, -1, keepdims=True)
    centered = key_float - key_mean
    key_var = jnp.mean(centered * centered, -1, keepdims=True)
    key_scale = lax.rsqrt(key_var + epsilon)
    key_hat = centered * key_scale
    normed_keys = (key_hat * key_gain + key_bias).astype(jnp.bfloat16)
    return (key_hat, key_scale, normed_keys)


def query_norm(query_rows):
    query_float = query_rows.astype(jnp.float32).reshape(query_rows.shape[0], H, DH)
    query_scale = lax.rsqrt(jnp.mean(query_float * query_float, -1, keepdims=True) + epsilon)
    query_hat = query_float * query_scale
    return (query_hat, query_scale, query_hat.astype(jnp.bfloat16))


def query_kernel(q_ref, qr_ref, qt_ref):
    f32 = jnp.float32
    for h in range(H):
        x = q_ref[:, h * DH:(h + 1) * DH].astype(f32)
        scale = lax.rsqrt(jnp.mean(x * x, -1, keepdims=True) + epsilon)
        nq = (x * scale).astype(jnp.bfloat16)
        qr_ref[h * BS:(h + 1) * BS, :] = nq
        qt_ref[:, h * BS:(h + 1) * BS] = nq.astype(f32).T.astype(jnp.bfloat16)


def normed_query_rows(q):
    nblk = q.shape[0]
    nrows = H * BS

    def blk(*shape):
        return pl.BlockSpec((None,) + shape, lambda b: (b,) + (0,) * len(shape))

    return pl.pallas_call(
        query_kernel,
        grid=(nblk,),
        in_specs=[blk(BS, H * DH)],
        out_specs=[blk(nrows, DH), blk(DH, nrows)],
        out_shape=[
            jax.ShapeDtypeStruct((nblk, nrows, DH), jnp.bfloat16),
            jax.ShapeDtypeStruct((nblk, DH, nrows), jnp.bfloat16),
        ],
        compiler_params=pltpu.CompilerParams(dimension_semantics=("arbitrary",)),
        cost_estimate=pl.CostEstimate(
            flops=nblk * nrows * DH * 4, transcendentals=nblk * nrows,
            bytes_accessed=nblk * nrows * DH * 6),
    )(q)


def score_kernel(q_ref, qr_ref, qt_ref, k_ref, w_ref, mass_ref, spos_ref, qpos_ref,
                 gq_ref, wg_ref, sgt_ref, div_ref, mix_ref, mg_ref, sp_ref):
    f32 = jnp.float32
    inv_root = DH ** (-0.5)
    rows = HEAD_GROUP * BS
    groups = H // HEAD_GROUP
    slots = k_ref.shape[0]
    chunks = slots // CHUNK

    head_ids = lax.broadcasted_iota(jnp.int32, (H, HEAD_GROUP), 0)
    pick_ids = lax.broadcasted_iota(jnp.int32, (H, HEAD_GROUP), 1)
    lane_heads = lax.broadcasted_iota(jnp.int32, (1, H), 1)

    def group_weights(g):
        onehot = (head_ids == g * HEAD_GROUP + pick_ids).astype(jnp.bfloat16)
        w4 = jnp.dot(w_ref[...], onehot, preferred_element_type=f32)
        return jnp.concatenate([w4[:, hh:hh + 1] for hh in range(HEAD_GROUP)], 0)

    mix_ref[...] = jnp.zeros_like(mix_ref)
    neg_log2_root = -inv_root * 1.4426950408889634

    def first_pass(g, carry):
        r0 = pl.multiple_of(g * rows, rows)
        q = qr_ref[pl.ds(r0, rows), :]
        wcol = group_weights(g)
        for c in range(chunks):
            cs = slice(c * CHUNK, (c + 1) * CHUNK)
            raw = lax.dot_general(q, k_ref[cs, :], (((1,), (1,)), ((), ())), preferred_element_type=f32)
            tail = jnp.exp2(jnp.abs(raw) * neg_log2_root)
            sp = jnp.maximum(raw * inv_root, 0.0) + jnp.log(1.0 + tail)
            sp_ref[pl.ds(r0, rows), cs] = sp
            ws = (wcol * sp).reshape(HEAD_GROUP, BS, CHUNK)
            mix_ref[:, cs] += jnp.sum(ws, 0)
        return carry

    lax.fori_loop(0, groups, first_pass, 0)

    mixture = mix_ref[...]
    squashed = jnp.tanh(mixture / soft_cap)
    logits = soft_cap * squashed
    is_valid = spos_ref[...] <= qpos_ref[...]
    exp_terms = jnp.where(is_valid, jnp.exp(logits - soft_cap), 0.0)
    denominator = jnp.sum(exp_terms, 1, keepdims=True)
    log_prob = logits - soft_cap - jnp.log(denominator)
    kept_mass = jnp.where(is_valid, mass_ref[...].astype(f32), 0.0)
    target = kept_mass / jnp.sum(kept_mass, 1, keepdims=True)
    div_ref[...] = jnp.sum(
        jnp.where(is_valid, target * (jnp.log(jnp.where(is_valid, target, 1.0)) - log_prob), 0.0),
        1, keepdims=True)
    mg_ref[...] = (exp_terms / denominator - target) * (1.0 - squashed * squashed)

    sgt_ref[...] = jnp.zeros_like(sgt_ref)
    wg_ref[...] = jnp.zeros_like(wg_ref)

    def second_pass(g, carry):
        r0 = pl.multiple_of(g * rows, rows)
        q = qr_ref[pl.ds(r0, rows), :]
        qt = qt_ref[:, pl.ds(r0, rows)]
        wcol = group_weights(g)
        qg_acc = jnp.zeros((rows, DH), f32)
        wg_acc = jnp.zeros((rows, 1), f32)
        for c in range(chunks):
            cs = slice(c * CHUNK, (c + 1) * CHUNK)
            s = lax.dot_general(q, k_ref[cs, :], (((1,), (1,)), ((), ())), preferred_element_type=f32) * inv_root
            sp = sp_ref[pl.ds(r0, rows), cs]
            sig = jnp.exp(s - sp)
            mgc = mg_ref[:, cs]
            mg4 = jnp.broadcast_to(mgc[None], (HEAD_GROUP, BS, CHUNK)).reshape(rows, CHUNK)
            sg = (mg4 * wcol * sig).astype(jnp.bfloat16)
            wg_acc = wg_acc + jnp.sum(mg4 * sp, 1, keepdims=True)
            qg_acc = qg_acc + jnp.dot(sg, k_ref[cs, :], preferred_element_type=f32)
            sgt_ref[:, cs] += jnp.dot(qt, sg, preferred_element_type=f32)
        qg_acc = qg_acc * inv_root
        wg_sum = wg_ref[...]
        for hh in range(HEAD_GROUP):
            h = g * HEAD_GROUP + hh
            wg_sum = wg_sum + jnp.where(lane_heads == h, wg_acc[hh * BS:(hh + 1) * BS], 0.0)
            lanes = pl.ds(pl.multiple_of(h * DH, DH), DH)
            x = q_ref[:, lanes].astype(f32)
            scale = lax.rsqrt(jnp.mean(x * x, -1, keepdims=True) + epsilon)
            query_hat = x * scale
            qg = qg_acc[hh * BS:(hh + 1) * BS]
            gq_ref[:, lanes] = (qg - query_hat * jnp.mean(qg * query_hat, -1, keepdims=True)) * scale
        wg_ref[...] = wg_sum
        return carry

    lax.fori_loop(0, groups, second_pass, 0)
    sgt_ref[...] = sgt_ref[...] * inv_root


def score_blocks(q, qr, qt, k, w, mass, spos, qpos):
    nblk = q.shape[0]
    slots = k.shape[1]
    nrows = H * BS
    f32 = jnp.float32

    def blk(*shape):
        return pl.BlockSpec((None,) + shape, lambda b: (b,) + (0,) * len(shape))

    flops = nblk * (4 * 2 * nrows * slots * DH)
    return pl.pallas_call(
        score_kernel,
        grid=(nblk,),
        in_specs=[
            blk(BS, H * DH), blk(nrows, DH), blk(DH, nrows), blk(slots, DH),
            blk(BS, H), blk(BS, slots), blk(1, slots), blk(BS, 1),
        ],
        out_specs=[blk(BS, H * DH), blk(BS, H), blk(DH, slots), blk(BS, 1)],
        out_shape=[
            jax.ShapeDtypeStruct((nblk, BS, H * DH), f32),
            jax.ShapeDtypeStruct((nblk, BS, H), f32),
            jax.ShapeDtypeStruct((nblk, DH, slots), f32),
            jax.ShapeDtypeStruct((nblk, BS, 1), f32),
        ],
        scratch_shapes=[
            pltpu.VMEM((BS, slots), f32), pltpu.VMEM((BS, slots), f32), pltpu.VMEM((nrows, slots), f32)
        ],
        compiler_params=pltpu.CompilerParams(
            dimension_semantics=("arbitrary",), vmem_limit_bytes=60 * 1024 * 1024
        ),
        cost_estimate=pl.CostEstimate(
            flops=flops, transcendentals=nblk * nrows * slots * 3,
            bytes_accessed=nblk * (BS * H * DH * 10 + slots * DH * 6)),
    )(q, qr, qt, k, w, mass, spos, qpos)


def butterfly_sum(value, axes):
    count = 1
    for axis in axes:
        count *= lax.axis_size(axis)
    if count & (count - 1):
        return lax.psum(value, axes)
    stride = 1
    while stride < count:
        pairs = [(i, i ^ stride) for i in range(count)]
        value = value + lax.ppermute(value, axes, pairs)
        stride *= 2
    return value


def per_device(queries, keys, head_weights, block_ids, target_mass, key_gain, key_bias):
    ctx_count = lax.axis_size("ctx")
    ctx_index = lax.axis_index("ctx")
    dp_count = lax.axis_size("dp")
    dp_index = lax.axis_index("dp")
    key_count = KD // BS
    query_count = QD // BS
    capacity = 2 * query_count
    request_count = query_count * NSEL
    slot_count = NSEL * BS
    key_hat, key_scale, normed_keys = key_norm(keys[0], key_gain, key_bias)
    listed_ids = block_ids[0].reshape(request_count)
    is_listed = listed_ids >= 0
    block_safe = jnp.maximum(listed_ids, 0)
    owner_index = block_safe // key_count
    local_block = block_safe % key_count
    owner_hits = (
        (owner_index[:, None] == jnp.arange(ctx_count, dtype=jnp.int32)[None, :])
        & is_listed[:, None]
    ).astype(jnp.int32)
    earlier = jnp.cumsum(owner_hits, 0) - owner_hits
    rank_slot = jnp.sum(earlier * owner_hits, 1)
    target_slot = jnp.where(is_listed, owner_index * capacity + rank_slot, 0)
    placement = (
        target_slot[:, None] == jnp.arange(ctx_count * capacity, dtype=jnp.int32)[None, :]
    ) & is_listed[:, None]
    request_table = jnp.sum(jnp.where(placement, local_block[:, None] + 1, 0), 0) - 1
    request_table = request_table.reshape(ctx_count, capacity)
    asked_back = lax.all_to_all(request_table, "ctx", split_axis=0, concat_axis=0, tiled=True)
    sent_keys = normed_keys.reshape(key_count, BS, DH)[jnp.clip(asked_back, 0, key_count - 1)]
    arrived_keys = lax.all_to_all(sent_keys, "ctx", split_axis=0, concat_axis=0, tiled=True)
    picked = arrived_keys.reshape(ctx_count * capacity, BS, DH)[target_slot]
    slot_keys = picked.reshape(query_count, slot_count, DH)
    slot_positions = (block_safe[:, None] * BS + jnp.arange(BS, dtype=jnp.int32)[None, :]).reshape(
        query_count, slot_count
    )
    slot_lives = jnp.repeat(is_listed, BS).reshape(query_count, slot_count)
    never = jnp.iinfo(jnp.int32).max
    slot_limit = jnp.where(slot_lives, slot_positions, never).reshape(query_count, 1, slot_count)
    first_pos = ctx_index * KD + KD - QD
    query_pos = (first_pos + jnp.arange(QD, dtype=jnp.int32)).reshape(query_count, BS, 1)

    mass_rows = target_mass[0].reshape(query_count, BS, slot_count)
    query_blocks = queries[0].reshape(query_count, BS, H * DH)
    head_rows, head_cols = normed_query_rows(query_blocks)
    grad_query_rows, weight_grads, slot_grad_t, div_rows = score_blocks(
        query_blocks, head_rows, head_cols, slot_keys,
        head_weights[0].reshape(query_count, BS, H), mass_rows, slot_limit, query_pos
    )
    divergence_total = jnp.sum(div_rows)
    grad_slots = slot_grad_t.transpose(0, 2, 1)
    slot_flat = grad_slots.reshape(request_count, BS * DH)
    request_iota = jnp.arange(request_count, dtype=jnp.int32)[:, None]
    source_request = jnp.sum(jnp.where(placement, request_iota, 0), 0)
    outbound = slot_flat[source_request]
    returned = lax.all_to_all(
        outbound.reshape(ctx_count, capacity, BS * DH), "ctx", split_axis=0, concat_axis=0, tiled=True
    )
    own_rows = (
        asked_back.reshape(ctx_count * capacity)[None, :]
        == jnp.arange(key_count, dtype=jnp.int32)[:, None]
    ).astype(jnp.float32)
    key_grad = jnp.dot(
        own_rows, returned.reshape(ctx_count * capacity, BS * DH), precision=lax.Precision.HIGHEST
    ).reshape(KD, DH)
    gain_part = jnp.sum(key_grad * key_hat, 0)
    bias_part = jnp.sum(key_grad, 0)
    scaled_grad = key_grad * key_gain
    grad_key_rows = (
        scaled_grad
        - jnp.mean(scaled_grad, -1, keepdims=True)
        - key_hat * jnp.mean(scaled_grad * key_hat, -1, keepdims=True)
    ) * key_scale
    loss_slots = jnp.where(jnp.arange(dp_count) == dp_index, divergence_total, 0.0)
    packed = butterfly_sum(jnp.concatenate([gain_part, bias_part, loss_slots]), ("dp", "ctx"))
    grad_gain = packed[:DH]
    grad_bias = packed[DH:2 * DH]
    loss_total = lax.dynamic_index_in_dim(packed, 2 * DH + dp_index, 0, keepdims=False)
    seq_loss = jnp.reshape(loss_total / (QD * ctx_count), (1,))
    return (
        seq_loss,
        grad_query_rows.reshape(1, QD, H * DH),
        weight_grads.reshape(1, QD, H),
        grad_key_rows.reshape(1, KD, DH),
        grad_gain,
        grad_bias,
    )


def solution(mesh):
    in_specs = (
        P("dp", "ctx", None),
        P("dp", "ctx", None),
        P("dp", "ctx", None),
        P("dp", "ctx", None),
        P("dp", "ctx", None),
        P(),
        P(),
    )
    out_specs = (
        P("dp"),
        P("dp", "ctx", None),
        P("dp", "ctx", None),
        P("dp", "ctx", None),
        P(),
        P(),
    )
    return jax.shard_map(
        per_device, mesh=mesh, in_specs=in_specs, out_specs=out_specs, check_vma=False
    )
```

```python
import functools
import jax
import jax.numpy as jnp
from jax import lax
from jax.experimental import pallas as pl
from jax.experimental.pallas import tpu as pltpu
from jax.sharding import PartitionSpec as P

H = 32
DH = 128
BS = 64
NSEL = 32
QD = 128
KD = 1024

epsilon = 1e-06
soft_cap = 20.0

HEAD_GROUP = 32
CHUNK = 256


def key_norm(key_rows, key_gain, key_bias):
    key_float = key_rows.astype(jnp.float32)
    key_mean = jnp.mean(key_float, -1, keepdims=True)
    centered = key_float - key_mean
    key_var = jnp.mean(centered * centered, -1, keepdims=True)
    key_scale = lax.rsqrt(key_var + epsilon)
    key_hat = centered * key_scale
    normed_keys = (key_hat * key_gain + key_bias).astype(jnp.bfloat16)
    return (key_hat, key_scale, normed_keys)


def query_norm(query_rows):
    query_float = query_rows.astype(jnp.float32).reshape(query_rows.shape[0], H, DH)
    query_scale = lax.rsqrt(jnp.mean(query_float * query_float, -1, keepdims=True) + epsilon)
    query_hat = query_float * query_scale
    return (query_hat, query_scale, query_hat.astype(jnp.bfloat16))


def query_kernel(q_ref, qr_ref, qt_ref):
    f32 = jnp.float32
    for h in range(H):
        x = q_ref[:, h * DH:(h + 1) * DH].astype(f32)
        scale = lax.rsqrt(jnp.mean(x * x, -1, keepdims=True) + epsilon)
        nq = (x * scale).astype(jnp.bfloat16)
        qr_ref[h * BS:(h + 1) * BS, :] = nq
        qt_ref[:, h * BS:(h + 1) * BS] = nq.astype(f32).T.astype(jnp.bfloat16)


def normed_query_rows(q):
    nblk = q.shape[0]
    nrows = H * BS

    def blk(*shape):
        return pl.BlockSpec((None,) + shape, lambda b: (b,) + (0,) * len(shape))

    return pl.pallas_call(
        query_kernel,
        grid=(nblk,),
        in_specs=[blk(BS, H * DH)],
        out_specs=[blk(nrows, DH), blk(DH, nrows)],
        out_shape=[
            jax.ShapeDtypeStruct((nblk, nrows, DH), jnp.bfloat16),
            jax.ShapeDtypeStruct((nblk, DH, nrows), jnp.bfloat16),
        ],
        compiler_params=pltpu.CompilerParams(dimension_semantics=("arbitrary",)),
        cost_estimate=pl.CostEstimate(
            flops=nblk * nrows * DH * 4, transcendentals=nblk * nrows,
            bytes_accessed=nblk * nrows * DH * 6),
    )(q)


def score_kernel(q_ref, qr_ref, qt_ref, k_ref, w_ref, mass_ref, spos_ref, qpos_ref,
                 gq_ref, wg_ref, sgo_ref, div_ref, mix_ref, mg_ref, sp_ref, sgt_ref):
    f32 = jnp.float32
    inv_root = DH ** (-0.5)
    rows = HEAD_GROUP * BS
    groups = H // HEAD_GROUP
    slots = k_ref.shape[0]
    chunks = slots // CHUNK

    head_ids = lax.broadcasted_iota(jnp.int32, (H, HEAD_GROUP), 0)
    pick_ids = lax.broadcasted_iota(jnp.int32, (H, HEAD_GROUP), 1)
    lane_heads = lax.broadcasted_iota(jnp.int32, (1, H), 1)

    def group_weights(g):
        onehot = (head_ids == g * HEAD_GROUP + pick_ids).astype(jnp.bfloat16)
        w4 = jnp.dot(w_ref[...], onehot, preferred_element_type=f32)
        return jnp.concatenate([w4[:, hh:hh + 1] for hh in range(HEAD_GROUP)], 0)

    mix_ref[...] = jnp.zeros_like(mix_ref)
    neg_log2_root = -inv_root * 1.4426950408889634

    def first_pass(g, carry):
        r0 = pl.multiple_of(g * rows, rows)
        q = qr_ref[pl.ds(r0, rows), :]
        wcol = group_weights(g)
        for c in range(chunks):
            cs = slice(c * CHUNK, (c + 1) * CHUNK)
            raw = lax.dot_general(q, k_ref[cs, :], (((1,), (1,)), ((), ())), preferred_element_type=f32)
            tail = jnp.exp2(jnp.abs(raw) * neg_log2_root)
            sp = jnp.maximum(raw * inv_root, 0.0) + jnp.log(1.0 + tail)
            sp_ref[pl.ds(r0, rows), cs] = sp
            ws = (wcol * sp).reshape(HEAD_GROUP, BS, CHUNK)
            mix_ref[:, cs] += jnp.sum(ws, 0)
        return carry

    lax.fori_loop(0, groups, first_pass, 0)

    mixture = mix_ref[...]
    squashed = jnp.tanh(mixture / soft_cap)
    logits = soft_cap * squashed
    is_valid = spos_ref[...] <= qpos_ref[...]
    exp_terms = jnp.where(is_valid, jnp.exp(logits - soft_cap), 0.0)
    denominator = jnp.sum(exp_terms, 1, keepdims=True)
    log_prob = logits - soft_cap - jnp.log(denominator)
    kept_mass = jnp.where(is_valid, mass_ref[...].astype(f32), 0.0)
    target = kept_mass / jnp.sum(kept_mass, 1, keepdims=True)
    div_ref[...] = jnp.sum(
        jnp.where(is_valid, target * (jnp.log(jnp.where(is_valid, target, 1.0)) - log_prob), 0.0),
        1, keepdims=True)
    mg_ref[...] = (exp_terms / denominator - target) * (1.0 - squashed * squashed)

    sgt_ref[...] = jnp.zeros_like(sgt_ref)
    wg_ref[...] = jnp.zeros_like(wg_ref)

    def second_pass(g, carry):
        r0 = pl.multiple_of(g * rows, rows)
        q = qr_ref[pl.ds(r0, rows), :]
        qt = qt_ref[:, pl.ds(r0, rows)]
        wcol = group_weights(g)
        qg_acc = jnp.zeros((rows, DH), f32)
        wg_acc = jnp.zeros((rows, 1), f32)
        for c in range(chunks):
            cs = slice(c * CHUNK, (c + 1) * CHUNK)
            s = lax.dot_general(q, k_ref[cs, :], (((1,), (1,)), ((), ())), preferred_element_type=f32) * inv_root
            sp = sp_ref[pl.ds(r0, rows), cs]
            sig = jnp.exp(s - sp)
            mgc = mg_ref[:, cs]
            mg4 = jnp.broadcast_to(mgc[None], (HEAD_GROUP, BS, CHUNK)).reshape(rows, CHUNK)
            sg = (mg4 * wcol * sig).astype(jnp.bfloat16)
            wg_acc = wg_acc + jnp.sum(mg4 * sp, 1, keepdims=True)
            qg_acc = qg_acc + jnp.dot(sg, k_ref[cs, :], preferred_element_type=f32)
            sgt_ref[:, cs] += jnp.dot(qt, sg, preferred_element_type=f32)
        qg_acc = qg_acc * inv_root
        wg_sum = wg_ref[...]
        for hh in range(HEAD_GROUP):
            h = g * HEAD_GROUP + hh
            wg_sum = wg_sum + jnp.where(lane_heads == h, wg_acc[hh * BS:(hh + 1) * BS], 0.0)
            lanes = pl.ds(pl.multiple_of(h * DH, DH), DH)
            x = q_ref[:, lanes].astype(f32)
            scale = lax.rsqrt(jnp.mean(x * x, -1, keepdims=True) + epsilon)
            query_hat = x * scale
            qg = qg_acc[hh * BS:(hh + 1) * BS]
            gq_ref[:, lanes] = (qg - query_hat * jnp.mean(qg * query_hat, -1, keepdims=True)) * scale
        wg_ref[...] = wg_sum
        return carry

    lax.fori_loop(0, groups, second_pass, 0)
    sgo_ref[...] = (sgt_ref[...] * inv_root).T


def score_blocks(q, qr, qt, k, w, mass, spos, qpos):
    nblk = q.shape[0]
    slots = k.shape[1]
    nrows = H * BS
    f32 = jnp.float32

    def blk(*shape):
        return pl.BlockSpec((None,) + shape, lambda b: (b,) + (0,) * len(shape))

    flops = nblk * (4 * 2 * nrows * slots * DH)
    return pl.pallas_call(
        score_kernel,
        grid=(nblk,),
        in_specs=[
            blk(BS, H * DH), blk(nrows, DH), blk(DH, nrows), blk(slots, DH),
            blk(BS, H), blk(BS, slots), blk(1, slots), blk(BS, 1),
        ],
        out_specs=[blk(BS, H * DH), blk(BS, H), blk(slots, DH), blk(BS, 1)],
        out_shape=[
            jax.ShapeDtypeStruct((nblk, BS, H * DH), f32),
            jax.ShapeDtypeStruct((nblk, BS, H), f32),
            jax.ShapeDtypeStruct((nblk, slots, DH), f32),
            jax.ShapeDtypeStruct((nblk, BS, 1), f32),
        ],
        scratch_shapes=[
            pltpu.VMEM((BS, slots), f32), pltpu.VMEM((BS, slots), f32), pltpu.VMEM((nrows, slots), f32),
            pltpu.VMEM((DH, slots), f32),
        ],
        compiler_params=pltpu.CompilerParams(
            dimension_semantics=("arbitrary",), vmem_limit_bytes=60 * 1024 * 1024
        ),
        cost_estimate=pl.CostEstimate(
            flops=flops, transcendentals=nblk * nrows * slots * 3,
            bytes_accessed=nblk * (BS * H * DH * 10 + slots * DH * 6)),
    )(q, qr, qt, k, w, mass, spos, qpos)


def butterfly_sum(value, axes):
    count = 1
    for axis in axes:
        count *= lax.axis_size(axis)
    if count & (count - 1):
        return lax.psum(value, axes)
    stride = 1
    while stride < count:
        pairs = [(i, i ^ stride) for i in range(count)]
        value = value + lax.ppermute(value, axes, pairs)
        stride *= 2
    return value


def per_device(queries, keys, head_weights, block_ids, target_mass, key_gain, key_bias):
    ctx_count = lax.axis_size("ctx")
    ctx_index = lax.axis_index("ctx")
    dp_count = lax.axis_size("dp")
    dp_index = lax.axis_index("dp")
    key_count = KD // BS
    query_count = QD // BS
    capacity = 2 * query_count
    request_count = query_count * NSEL
    slot_count = NSEL * BS
    key_hat, key_scale, normed_keys = key_norm(keys[0], key_gain, key_bias)
    listed_ids = block_ids[0].reshape(request_count)
    is_listed = listed_ids >= 0
    block_safe = jnp.maximum(listed_ids, 0)
    owner_index = block_safe // key_count
    local_block = block_safe % key_count
    owner_hits = (
        (owner_index[:, None] == jnp.arange(ctx_count, dtype=jnp.int32)[None, :])
        & is_listed[:, None]
    ).astype(jnp.int32)
    earlier = jnp.cumsum(owner_hits, 0) - owner_hits
    rank_slot = jnp.sum(earlier * owner_hits, 1)
    target_slot = jnp.where(is_listed, owner_index * capacity + rank_slot, 0)
    placement = (
        target_slot[:, None] == jnp.arange(ctx_count * capacity, dtype=jnp.int32)[None, :]
    ) & is_listed[:, None]
    request_table = jnp.sum(jnp.where(placement, local_block[:, None] + 1, 0), 0) - 1
    request_table = request_table.reshape(ctx_count, capacity)
    asked_back = lax.all_to_all(request_table, "ctx", split_axis=0, concat_axis=0, tiled=True)
    sent_keys = normed_keys.reshape(key_count, BS, DH)[jnp.clip(asked_back, 0, key_count - 1)]
    arrived_keys = lax.all_to_all(sent_keys, "ctx", split_axis=0, concat_axis=0, tiled=True)
    picked = arrived_keys.reshape(ctx_count * capacity, BS, DH)[target_slot]
    slot_keys = picked.reshape(query_count, slot_count, DH)
    slot_positions = (block_safe[:, None] * BS + jnp.arange(BS, dtype=jnp.int32)[None, :]).reshape(
        query_count, slot_count
    )
    slot_lives = jnp.repeat(is_listed, BS).reshape(query_count, slot_count)
    never = jnp.iinfo(jnp.int32).max
    slot_limit = jnp.where(slot_lives, slot_positions, never).reshape(query_count, 1, slot_count)
    first_pos = ctx_index * KD + KD - QD
    query_pos = (first_pos + jnp.arange(QD, dtype=jnp.int32)).reshape(query_count, BS, 1)

    mass_rows = target_mass[0].reshape(query_count, BS, slot_count)
    query_blocks = queries[0].reshape(query_count, BS, H * DH)
    head_rows, head_cols = normed_query_rows(query_blocks)
    grad_query_rows, weight_grads, slot_grad_t, div_rows = score_blocks(
        query_blocks, head_rows, head_cols, slot_keys,
        head_weights[0].reshape(query_count, BS, H), mass_rows, slot_limit, query_pos
    )
    divergence_total = jnp.sum(div_rows)
    grad_slots = slot_grad_t
    slot_flat = grad_slots.reshape(request_count, BS * DH)
    request_iota = jnp.arange(request_count, dtype=jnp.int32)[:, None]
    source_request = jnp.sum(jnp.where(placement, request_iota, 0), 0)
    outbound = slot_flat[source_request]
    returned = lax.all_to_all(
        outbound.reshape(ctx_count, capacity, BS * DH), "ctx", split_axis=0, concat_axis=0, tiled=True
    )
    own_rows = (
        asked_back.reshape(ctx_count * capacity)[None, :]
        == jnp.arange(key_count, dtype=jnp.int32)[:, None]
    ).astype(jnp.float32)
    key_grad = jnp.dot(
        own_rows, returned.reshape(ctx_count * capacity, BS * DH), precision=lax.Precision.HIGHEST
    ).reshape(KD, DH)
    gain_part = jnp.sum(key_grad * key_hat, 0)
    bias_part = jnp.sum(key_grad, 0)
    scaled_grad = key_grad * key_gain
    grad_key_rows = (
        scaled_grad
        - jnp.mean(scaled_grad, -1, keepdims=True)
        - key_hat * jnp.mean(scaled_grad * key_hat, -1, keepdims=True)
    ) * key_scale
    loss_slots = jnp.where(jnp.arange(dp_count) == dp_index, divergence_total, 0.0)
    packed = butterfly_sum(jnp.concatenate([gain_part, bias_part, loss_slots]), ("dp", "ctx"))
    grad_gain = packed[:DH]
    grad_bias = packed[DH:2 * DH]
    loss_total = lax.dynamic_index_in_dim(packed, 2 * DH + dp_index, 0, keepdims=False)
    seq_loss = jnp.reshape(loss_total / (QD * ctx_count), (1,))
    return (
        seq_loss,
        grad_query_rows.reshape(1, QD, H * DH),
        weight_grads.reshape(1, QD, H),
        grad_key_rows.reshape(1, KD, DH),
        grad_gain,
        grad_bias,
    )


def solution(mesh):
    in_specs = (
        P("dp", "ctx", None),
        P("dp", "ctx", None),
        P("dp", "ctx", None),
        P("dp", "ctx", None),
        P("dp", "ctx", None),
        P(),
        P(),
    )
    out_specs = (
        P("dp"),
        P("dp", "ctx", None),
        P("dp", "ctx", None),
        P("dp", "ctx", None),
        P(),
        P(),
    )
    return jax.shard_map(
        per_device, mesh=mesh, in_specs=in_specs, out_specs=out_specs, check_vma=False
    )
```
